32 devices in a mesh: band: 8 (over z, core), col: 4 (over y, x).
Axes of the slice: x: 2, y: 2, z: 4, core: 2. Of those that a mesh axis runs over, the one named last changes fastest.
Arguments:
- cells: bfloat16 [32, 256, 768], P('band', 'col'), may hold values from -25 to 25
- summary: bfloat16 [8, 256, 768], P('band', 'col'), may hold values from -6 to 6
- owner: int32 [4], P('col'), may hold values from 0 to 7
- schema: int32 [32, 256], P('band', 'col'), may hold values from 0 to 15
- w_qkv: bfloat16 [768, 2304], replicated, may hold values from -0.21875 to 0.21875
- w_out: bfloat16 [768, 768], replicated, may hold values from -0.625 to 0.625
- gain_attn: float32 [768], replicated, may hold values from 0.5 to 1.5
- w_up: bfloat16 [768, 3072], replicated, may hold values from -0.21875 to 0.21875
- w_down: bfloat16 [3072, 768], replicated, may hold values from -0.109375 to 0.109375
- gain_ffn: float32 [768], replicated, may hold values from 0.5 to 1.5
Outputs:
- cells_out: bfloat16 [32, 256, 768], P('band', 'col')
- summary_out: bfloat16 [256, 768], P('col')
The draws below stay inside these ranges and needn't reach their ends.
Inputs may be any that keep to these rules, and one draw needn't show every extreme that they name: `owner`: each entry names the band whose summary tokens its column group reads. `schema`: bit g of an entry allows the cell to attend to the row's cells of column group g; the cell's own group is allowed whatever the bits.
All inputs are finite; a program needn't handle non-finite values.
Results may differ from the reference program's by a relative error of at most 0.019.
Values may be sent and summed in bfloat16 or wider, within the bound.
No kernel may reach another device: no remote copies, remote signals or barrier semaphores. Data moves between devices by JAX's collectives and lax.ppermute only.
A program may use at most 128 MiB of HBM per device.

```python
import jax
import jax.numpy as jnp
from jax import lax

D = 768
HEADS = 12
HEAD_DIM = 64
FF = 3072
COLS_DEV = 64
ROWS = 32
COLS = 256
N_BAND = 8
N_COL = 4


def draw_cells(key, part):
    first_key = jax.random.fold_in(key, 0)
    rising = 0.6 * (1.0 + 2.0 * jnp.arange(ROWS, dtype=jnp.float32) / max(ROWS - 1, 1))
    sample = jnp.clip(jax.random.normal(first_key, (ROWS, COLS, D), jnp.float32), -4.0, 4.0)
    return (sample * rising[:, None, None]).astype(jnp.bfloat16)


def with_ends(result, key, low, largest):
    dims = result.shape
    spot = [jax.random.randint(jax.random.fold_in(key, axis), (), 0, dims[axis]) for axis in range(len(dims))]
    result = result.at[tuple(spot)].set(low)
    longest = dims.index(max(dims))
    spot[longest] = (spot[longest] + 1) % dims[longest]
    return result.at[tuple(spot)].set(largest)


def block_levels(own_key, dims, cuts, smallest, largest):
    def one(dim, parts):
        draws = jax.random.uniform(jax.random.fold_in(jax.random.fold_in(own_key, 6), dim), (parts,), jnp.float32, smallest / len(cuts), largest / len(cuts))
        return jnp.repeat(jnp.exp(draws), dims[dim] // parts).reshape((-1,) + (1,) * (len(dims) - dim - 1))

    loudness = one(*cuts[0])
    for cut in cuts[1:]:
        loudness = loudness * one(*cut)
    return loudness


def scatter_about(rng, dims, deviation, most, cuts=(), kind=jnp.bfloat16):
    values = jax.random.normal(rng, dims, jnp.float32) * deviation
    if len(cuts) > 0:
        values = block_levels(rng, dims, cuts, -0.22, 0.18) * values
    return jnp.clip(values, min=-most, max=most).astype(kind)


def setup_inputs(seed: int = 0) -> dict:
    arg_keys = jax.random.split(jax.random.key(seed), 11)
    return {
        "cells": draw_cells(jax.random.fold_in(arg_keys[10], 71), 0),
        "summary": scatter_about(arg_keys[1], (N_BAND, COLS, D), 1.0, 6.0, ((0, 8), (1, 4))),
        "owner": with_ends(jax.random.randint(arg_keys[2], (N_COL,), 0, N_BAND), jax.random.fold_in(arg_keys[2], 1), 0, N_BAND - 1).astype(jnp.int32),
        "schema": with_ends(jax.random.randint(arg_keys[3], (ROWS, COLS), 0, 2 ** N_COL), jax.random.fold_in(arg_keys[3], 1), 0, (2 ** N_COL) - 1).astype(jnp.int32),
        "w_qkv": scatter_about(arg_keys[4], (D, 3 * D), D ** -0.5, 0.21875),
        "w_out": scatter_about(arg_keys[5], (D, D), (D // 8) ** -0.5, 0.625),
        "gain_attn": jnp.clip(1.0 + 0.1 * jax.random.normal(arg_keys[6], (D,), jnp.float32), 0.5, 1.5),
        "w_up": scatter_about(arg_keys[7], (D, FF), D ** -0.5, 0.21875),
        "w_down": scatter_about(arg_keys[8], (FF, D), FF ** -0.5, 0.109375),
        "gain_ffn": jnp.clip(1.0 + 0.1 * jax.random.normal(arg_keys[9], (D,), jnp.float32), 0.5, 1.5),
    }


def layer_norm(values, gain_vec):
    center = values - lax.optimization_barrier(jnp.mean(values, -1, keepdims=True))
    spread = lax.optimization_barrier(jnp.mean(center * center, -1, keepdims=True))
    return center * lax.rsqrt(spread + 1e-05) * gain_vec

def finish(tokens_in, attended, w_out, gain_attn, w_up, w_down, gain_ffn):
    mixed_out = jnp.dot(attended, w_out, preferred_element_type=jnp.float32)
    hidden = layer_norm(tokens_in.astype(jnp.float32) + mixed_out, gain_attn).astype(jnp.bfloat16)
    inner_act = jax.nn.gelu(jnp.dot(hidden, w_up, preferred_element_type=jnp.float32)).astype(jnp.bfloat16)
    outer_out = jnp.dot(inner_act, w_down, preferred_element_type=jnp.float32)
    return layer_norm(hidden.astype(jnp.float32) + outer_out, gain_ffn).astype(jnp.bfloat16)

def rounded(values):
    return lax.optimization_barrier(values.astype(jnp.bfloat16)).astype(jnp.float32)

def reference(cells, summary, owner, schema, w_qkv, w_out, gain_attn, w_up, w_down, gain_ffn):
    score_scale = HEAD_DIM ** (-0.5)
    owner_cols = jnp.repeat(owner, COLS_DEV)
    chosen = summary[owner_cols, jnp.arange(COLS)]
    summary_qkv = jnp.dot(chosen, w_qkv, preferred_element_type=jnp.float32).astype(jnp.bfloat16)
    cell_qkv = jnp.dot(cells.reshape(ROWS * COLS, D), w_qkv, preferred_element_type=jnp.float32)
    cell_qkv = cell_qkv.astype(jnp.bfloat16).reshape(ROWS, COLS, 3, HEADS, HEAD_DIM)
    summ_float = summary_qkv.reshape(COLS, 3, HEADS, HEAD_DIM).astype(jnp.float32)
    sum_keys = summ_float[:, 1].reshape(N_COL, COLS_DEV, HEADS, HEAD_DIM)
    sum_vals = summ_float[:, 2].reshape(N_COL, COLS_DEV, HEADS, HEAD_DIM)
    groups = (jnp.arange(COLS) // COLS_DEV).astype(jnp.int32)

    def one_row(packed):
        row_qkv, row_bits = packed
        row_float = row_qkv.astype(jnp.float32)
        queries = row_float[:, 0]
        keys_cell = row_float[:, 1]
        vals_cell = row_float[:, 2]
        cell_scores = jnp.einsum('jhd,khd->hjk', queries, keys_cell) * score_scale
        allowed = (jnp.right_shift(row_bits[:, None], groups[None, :]) & 1 == 1) | (groups[:, None] == groups[None, :])
        cell_scores = jnp.where(allowed[None], cell_scores, -1e+30)
        sum_scores = jnp.einsum('gqhd,gkhd->hgqk', queries.reshape(N_COL, COLS_DEV, HEADS, HEAD_DIM), sum_keys)
        sum_scores = sum_scores.reshape(HEADS, COLS, COLS_DEV) * score_scale
        row_top = jnp.maximum(cell_scores.max(-1), sum_scores.max(-1))
        cell_exp = jnp.exp(cell_scores - row_top[..., None])
        sum_exp = jnp.exp(sum_scores - row_top[..., None])
        row_total = cell_exp.sum(-1) + sum_exp.sum(-1)
        mixed_sum = jnp.einsum('hjk,khd->jhd', rounded(cell_exp), vals_cell)
        sum_part = jnp.einsum('hgqk,gkhd->gqhd', rounded(sum_exp).reshape(HEADS, N_COL, COLS_DEV, COLS_DEV), sum_vals)
        mixed_sum = mixed_sum + sum_part.reshape(COLS, HEADS, HEAD_DIM)
        return (mixed_sum / row_total.T[..., None]).reshape(COLS, D).astype(jnp.bfloat16)
    attended = lax.map(one_row, (cell_qkv, schema))
    cells_out = finish(cells.reshape(ROWS * COLS, D), attended.reshape(ROWS * COLS, D), w_out, gain_attn, w_up, w_down, gain_ffn)
    cells_out = cells_out.reshape(ROWS, COLS, D)
    sum_queries = summ_float[:, 0]
    self_keys = summ_float[:, 1]
    self_vals = summ_float[:, 2]
    self_scores = lax.optimization_barrier(jnp.sum(sum_queries * self_keys, -1)) * score_scale
    col_scores = jnp.einsum('jhd,rjhd->jhr', sum_queries, cell_qkv[:, :, 1].astype(jnp.float32)) * score_scale
    col_top = jnp.maximum(col_scores.max(-1), self_scores)
    col_exp = jnp.exp(col_scores - col_top[..., None])
    self_exp = jnp.exp(self_scores - col_top)
    col_total = col_exp.sum(-1) + self_exp
    col_mixed = jnp.einsum('jhr,rjhd->jhd', rounded(col_exp), cell_qkv[:, :, 2].astype(jnp.float32))
    col_mixed = col_mixed + rounded(self_exp)[..., None] * self_vals
    summary_att = (col_mixed / col_total[..., None]).reshape(COLS, D).astype(jnp.bfloat16)
    summary_out = finish(chosen, summary_att, w_out, gain_attn, w_up, w_down, gain_ffn)
    return (cells_out, summary_out)
```

```python
import jax
import jax.numpy as jnp
from jax import lax
from jax.sharding import PartitionSpec as P

HEADS = 12
HEAD_DIM = 64


def spread_2(value, axis, source):
    kept = jnp.where(lax.axis_index(axis) == source, value, 0).astype(value.dtype)
    return lax.psum(kept, axis)


def layer_norm(values, gain_vec):
    center = values - jnp.mean(values, -1, keepdims=True)
    spread = jnp.mean(center * center, -1, keepdims=True)
    return center * lax.rsqrt(spread + 1e-05) * gain_vec


def finish(tokens_in, attended, w_out, gain_attn, w_up, w_down, gain_ffn):
    mixed_out = jnp.dot(attended, w_out, preferred_element_type=jnp.float32)
    hidden = layer_norm(tokens_in.astype(jnp.float32) + mixed_out, gain_attn).astype(jnp.bfloat16)
    inner_act = jax.nn.gelu(jnp.dot(hidden, w_up, preferred_element_type=jnp.float32)).astype(
        jnp.bfloat16
    )
    outer_out = jnp.dot(inner_act, w_down, preferred_element_type=jnp.float32)
    return layer_norm(hidden.astype(jnp.float32) + outer_out, gain_ffn).astype(jnp.bfloat16)


def project(values, weight):
    return jnp.dot(values, weight, preferred_element_type=jnp.float32).astype(jnp.bfloat16)


def head_sum(values):
    dims = values.shape[:-1]
    return values.reshape(dims + (HEADS, HEAD_DIM)).sum(-1)


def head_spread(values):
    dims = values.shape[:-1]
    return jnp.broadcast_to(values[..., None], dims + (HEADS, HEAD_DIM)).reshape(
        dims + (HEADS * HEAD_DIM,)
    )


def local(cells, summary, owner, schema, w_qkv, w_out, gain_attn, w_up, w_down, gain_ffn):
    row_count, cols_dev, model_width = cells.shape
    own_group = lax.axis_index("col")
    score_scale = HEAD_DIM ** (-0.5)
    flat_cells = cells.reshape(row_count * cols_dev, model_width)
    w_kv = w_qkv[:, model_width:]

    tokens = spread_2(summary[0], "band", owner[0])
    row_cells = lax.all_gather(cells, "col", axis=1, tiled=True)
    width_now = row_cells.shape[1]

    qkv_cells = project(flat_cells, w_qkv).reshape(row_count, cols_dev, 3 * model_width)
    queries = qkv_cells[:, :, :model_width]
    own_keys = qkv_cells[:, :, model_width : 2 * model_width].astype(jnp.float32)
    own_vals = qkv_cells[:, :, 2 * model_width :].astype(jnp.float32)

    summary_qkv = project(tokens, w_qkv)
    sum_queries = summary_qkv[:, :model_width]
    sum_keys = summary_qkv[:, model_width : 2 * model_width]
    sum_vals = summary_qkv[:, 2 * model_width :]

    sq = sum_queries.astype(jnp.float32)
    col_scores = head_sum(sq[None] * own_keys) * score_scale
    self_scores = head_sum(sq * sum_keys.astype(jnp.float32)) * score_scale
    col_top = jnp.maximum(lax.pmax(col_scores.max(0), "band"), self_scores)
    col_exp = jnp.exp(col_scores - col_top[None])
    self_exp = jnp.exp(self_scores - col_top)
    col_weights = head_spread(col_exp.astype(jnp.bfloat16).astype(jnp.float32))
    col_mixed = (col_weights * own_vals).sum(0)
    col_total = col_exp.sum(0)
    packed = jnp.concatenate([col_mixed, col_total], axis=-1)
    packed = lax.psum(packed, "band")
    col_mixed = packed[:, :model_width]
    col_total = packed[:, model_width:] + self_exp
    self_weights = head_spread(self_exp.astype(jnp.bfloat16).astype(jnp.float32))
    col_mixed = col_mixed + self_weights * sum_vals.astype(jnp.float32)
    summary_att = (col_mixed / head_spread(col_total)).astype(jnp.bfloat16)

    row_kv = project(row_cells.reshape(row_count * width_now, model_width), w_kv)
    row_kv = row_kv.reshape(row_count, width_now, 2 * model_width)
    q4 = queries.reshape(row_count, cols_dev, HEADS, HEAD_DIM)
    k4 = row_kv[:, :, :model_width].reshape(row_count, width_now, HEADS, HEAD_DIM)
    v4 = row_kv[:, :, model_width:].reshape(row_count, width_now, HEADS, HEAD_DIM)
    sk = sum_keys.reshape(cols_dev, HEADS, HEAD_DIM)
    sv = sum_vals.reshape(cols_dev, HEADS, HEAD_DIM)
    key_groups = jnp.arange(width_now, dtype=jnp.int32) // cols_dev
    allowed = (jnp.right_shift(schema[:, :, None], key_groups[None, None, :]) & 1 == 1) | (
        key_groups == own_group
    )[None, None, :]
    cell_scores = (
        jnp.einsum("rqhd,rkhd->rhqk", q4, k4, preferred_element_type=jnp.float32) * score_scale
    )
    cell_scores = jnp.where(allowed[:, None], cell_scores, -1e30)
    tok_scores = (
        jnp.einsum("rqhd,khd->rhqk", q4, sk, preferred_element_type=jnp.float32) * score_scale
    )
    row_top = jnp.maximum(cell_scores.max(-1), tok_scores.max(-1))
    cell_exp = jnp.exp(cell_scores - row_top[..., None])
    tok_exp = jnp.exp(tok_scores - row_top[..., None])
    row_total = cell_exp.sum(-1) + tok_exp.sum(-1)
    mixed = jnp.einsum(
        "rhqk,rkhd->rqhd", cell_exp.astype(jnp.bfloat16), v4, preferred_element_type=jnp.float32
    )
    mixed = mixed + jnp.einsum(
        "rhqk,khd->rqhd", tok_exp.astype(jnp.bfloat16), sv, preferred_element_type=jnp.float32
    )
    attended = mixed / row_total.transpose(0, 2, 1)[..., None]
    attended = attended.reshape(row_count * cols_dev, model_width).astype(jnp.bfloat16)

    all_in = jnp.concatenate([flat_cells, tokens], axis=0)
    all_att = jnp.concatenate([attended, summary_att], axis=0)
    all_out = finish(all_in, all_att, w_out, gain_attn, w_up, w_down, gain_ffn)
    cells_out = all_out[: row_count * cols_dev].reshape(row_count, cols_dev, model_width)
    summary_out = all_out[row_count * cols_dev :]
    return (cells_out, summary_out)


def solution(mesh):
    in_specs = (
        P("band", "col", None),
        P("band", "col", None),
        P("col"),
        P("band", "col"),
        P(),
        P(),
        P(),
        P(),
        P(),
        P(),
    )
    out_specs = (P("band", "col", None), P("col", None))
    return jax.shard_map(local, mesh=mesh, in_specs=in_specs, out_specs=out_specs, check_vma=False)
```

```python
import functools

import jax
import jax.numpy as jnp
from jax import lax
from jax.sharding import PartitionSpec as P

HEADS = 12
HEAD_DIM = 64


def spread_2(value, axis, source):
    kept = jnp.where(lax.axis_index(axis) == source, value, 0).astype(value.dtype)
    return lax.psum(kept, axis)


def layer_norm(values, gain_vec):
    center = values - jnp.mean(values, -1, keepdims=True)
    spread = jnp.mean(center * center, -1, keepdims=True)
    return center * lax.rsqrt(spread + 1e-05) * gain_vec


def finish(tokens_in, attended, w_out, gain_attn, w_up, w_down, gain_ffn):
    mixed_out = jnp.dot(attended, w_out, preferred_element_type=jnp.float32)
    hidden = layer_norm(tokens_in.astype(jnp.float32) + mixed_out, gain_attn).astype(jnp.bfloat16)
    inner_act = jax.nn.gelu(jnp.dot(hidden, w_up, preferred_element_type=jnp.float32)).astype(
        jnp.bfloat16
    )
    outer_out = jnp.dot(inner_act, w_down, preferred_element_type=jnp.float32)
    return layer_norm(hidden.astype(jnp.float32) + outer_out, gain_ffn).astype(jnp.bfloat16)


def project(values, weight):
    return jnp.dot(values, weight, preferred_element_type=jnp.float32).astype(jnp.bfloat16)


def head_sum(values):
    dims = values.shape[:-1]
    return values.reshape(dims + (HEADS, HEAD_DIM)).sum(-1)


def head_spread(values):
    dims = values.shape[:-1]
    return jnp.broadcast_to(values[..., None], dims + (HEADS, HEAD_DIM)).reshape(
        dims + (HEADS * HEAD_DIM,)
    )


def fan_out(value, axis, count):
    here = lax.axis_index(axis)
    got = []
    for step in range(1, count):
        if count & (count - 1) == 0:
            pairs = [(i, i ^ step) for i in range(count)]
            source = here ^ step
        else:
            pairs = [(i, (i + step) % count) for i in range(count)]
            source = (here - step) % count
        got.append((source, lax.ppermute(value, axis, pairs)))
    return got


def local(cells, summary, owner, schema, w_qkv, w_out, gain_attn, w_up, w_down, gain_ffn, *, n_band, n_col):
    row_count, cols_dev, model_width = cells.shape
    own_group = lax.axis_index("col")
    own_band = lax.axis_index("band")
    score_scale = HEAD_DIM ** (-0.5)
    flat_cells = cells.reshape(row_count * cols_dev, model_width)
    w_kv = w_qkv[:, model_width:]

    tokens = summary[0]
    for source, got in fan_out(summary[0], "band", n_band):
        tokens = jnp.where(source == owner[0], got, tokens)
    tokens = jnp.where(own_band == owner[0], summary[0], tokens)
    row_parts = fan_out(cells, "col", n_col)

    qkv_cells = project(flat_cells, w_qkv).reshape(row_count, cols_dev, 3 * model_width)
    queries = qkv_cells[:, :, :model_width]
    own_keys = qkv_cells[:, :, model_width : 2 * model_width]
    own_vals = qkv_cells[:, :, 2 * model_width :]

    summary_qkv = project(tokens, w_qkv)
    sum_queries = summary_qkv[:, :model_width]
    sum_keys = summary_qkv[:, model_width : 2 * model_width]
    sum_vals = summary_qkv[:, 2 * model_width :]

    sq = sum_queries.astype(jnp.float32)
    col_scores = head_sum(sq[None] * own_keys.astype(jnp.float32)) * score_scale
    self_scores = head_sum(sq * sum_keys.astype(jnp.float32)) * score_scale
    part_top = col_scores.max(0)
    col_exp = jnp.exp(col_scores - part_top[None])
    col_weights = head_spread(col_exp.astype(jnp.bfloat16).astype(jnp.float32))
    part_mixed = (col_weights * own_vals.astype(jnp.float32)).sum(0)
    part_total = col_exp.sum(0)
    packed = jnp.concatenate([part_mixed, part_total, part_top], axis=-1)
    stacked = jnp.stack([packed] + [got for _, got in fan_out(packed, "band", n_band)])
    stacked = jnp.take(stacked, jnp.arange(n_band, dtype=jnp.int32) ^ own_band, axis=0)
    parts = [stacked[k] for k in range(n_band)]
    tops = [p[:, model_width + HEADS :] for p in parts]
    col_top = self_scores
    for t in tops:
        col_top = jnp.maximum(col_top, t)
    self_exp = jnp.exp(self_scores - col_top)
    col_total = self_exp
    self_weights = head_spread(self_exp.astype(jnp.bfloat16).astype(jnp.float32))
    col_mixed = self_weights * sum_vals.astype(jnp.float32)
    for p, t in zip(parts, tops):
        fade = jnp.exp(t - col_top)
        col_total = col_total + fade * p[:, model_width : model_width + HEADS]
        col_mixed = col_mixed + head_spread(fade) * p[:, :model_width]
    summary_att = (col_mixed / head_spread(col_total)).astype(jnp.bfloat16)

    sources = [own_group] + [s for s, _ in row_parts]
    other_cells = jnp.concatenate([got for _, got in row_parts], axis=1)
    width_other = other_cells.shape[1]
    other_kv = project(other_cells.reshape(row_count * width_other, model_width), w_kv)
    other_kv = other_kv.reshape(row_count, width_other, 2 * model_width)
    row_keys = jnp.concatenate([own_keys, other_kv[:, :, :model_width]], axis=1)
    row_vals = jnp.concatenate([own_vals, other_kv[:, :, model_width:]], axis=1)
    width_now = row_keys.shape[1]
    q4 = queries.reshape(row_count, cols_dev, HEADS, HEAD_DIM)
    k4 = row_keys.reshape(row_count, width_now, HEADS, HEAD_DIM)
    v4 = row_vals.reshape(row_count, width_now, HEADS, HEAD_DIM)
    sk = sum_keys.reshape(cols_dev, HEADS, HEAD_DIM)
    sv = sum_vals.reshape(cols_dev, HEADS, HEAD_DIM)
    key_groups = jnp.concatenate(
        [jnp.full((cols_dev,), s, jnp.int32) for s in sources]
    )
    own_block = jnp.arange(width_now, dtype=jnp.int32) < cols_dev
    allowed = (jnp.right_shift(schema[:, :, None], key_groups[None, None, :]) & 1 == 1) | own_block[
        None, None, :
    ]
    cell_scores = (
        jnp.einsum("rqhd,rkhd->rhqk", q4, k4, preferred_element_type=jnp.float32) * score_scale
    )
    cell_scores = jnp.where(allowed[:, None], cell_scores, -1e30)
    tok_scores = (
        jnp.einsum("rqhd,khd->rhqk", q4, sk, preferred_element_type=jnp.float32) * score_scale
    )
    row_top = jnp.maximum(cell_scores.max(-1), tok_scores.max(-1))
    cell_exp = jnp.exp(cell_scores - row_top[..., None])
    tok_exp = jnp.exp(tok_scores - row_top[..., None])
    row_total = cell_exp.sum(-1) + tok_exp.sum(-1)
    mixed = jnp.einsum(
        "rhqk,rkhd->rqhd", cell_exp.astype(jnp.bfloat16), v4, preferred_element_type=jnp.float32
    )
    mixed = mixed + jnp.einsum(
        "rhqk,khd->rqhd", tok_exp.astype(jnp.bfloat16), sv, preferred_element_type=jnp.float32
    )
    attended = mixed / row_total.transpose(0, 2, 1)[..., None]
    attended = attended.reshape(row_count * cols_dev, model_width).astype(jnp.bfloat16)

    all_in = jnp.concatenate([flat_cells, tokens], axis=0)
    all_att = jnp.concatenate([attended, summary_att], axis=0)
    all_out = finish(all_in, all_att, w_out, gain_attn, w_up, w_down, gain_ffn)
    cells_out = all_out[: row_count * cols_dev].reshape(row_count, cols_dev, model_width)
    summary_out = all_out[row_count * cols_dev :]
    return (cells_out, summary_out)


def solution(mesh):
    in_specs = (
        P("band", "col", None),
        P("band", "col", None),
        P("col"),
        P("band", "col"),
        P(),
        P(),
        P(),
        P(),
        P(),
        P(),
    )
    out_specs = (P("band", "col", None), P("col", None))
    body = functools.partial(local, n_band=mesh.shape["band"], n_col=mesh.shape["col"])
    return jax.shard_map(body, mesh=mesh, in_specs=in_specs, out_specs=out_specs, check_vma=False)
```

```python
import functools

import jax
import jax.numpy as jnp
from jax import lax
from jax.sharding import PartitionSpec as P

HEADS = 12
HEAD_DIM = 64


def spread_2(value, axis, source):
    kept = jnp.where(lax.axis_index(axis) == source, value, 0).astype(value.dtype)
    return lax.psum(kept, axis)


def layer_norm(values, gain_vec):
    center = values - jnp.mean(values, -1, keepdims=True)
    spread = jnp.mean(center * center, -1, keepdims=True)
    return center * lax.rsqrt(spread + 1e-05) * gain_vec


def finish(tokens_in, attended, w_out, gain_attn, w_up, w_down, gain_ffn):
    mixed_out = jnp.dot(attended, w_out, preferred_element_type=jnp.float32)
    hidden = layer_norm(tokens_in.astype(jnp.float32) + mixed_out, gain_attn).astype(jnp.bfloat16)
    inner_act = jax.nn.gelu(jnp.dot(hidden, w_up, preferred_element_type=jnp.float32)).astype(
        jnp.bfloat16
    )
    outer_out = jnp.dot(inner_act, w_down, preferred_element_type=jnp.float32)
    return layer_norm(hidden.astype(jnp.float32) + outer_out, gain_ffn).astype(jnp.bfloat16)


def project(values, weight):
    return jnp.dot(values, weight, preferred_element_type=jnp.float32).astype(jnp.bfloat16)


def head_matrix():
    lanes = jnp.arange(HEADS * HEAD_DIM, dtype=jnp.int32) // HEAD_DIM
    return (lanes[None, :] == jnp.arange(HEADS, dtype=jnp.int32)[:, None]).astype(jnp.float32)


def head_sum(values):
    dims = values.shape[:-1]
    flat = values.reshape(-1, values.shape[-1])
    out = jnp.dot(flat, head_matrix().T, precision=lax.Precision.HIGHEST,
                  preferred_element_type=jnp.float32)
    return out.reshape(dims + (HEADS,))


def head_spread(values):
    dims = values.shape[:-1]
    flat = values.reshape(-1, HEADS)
    out = jnp.dot(flat, head_matrix(), precision=lax.Precision.HIGHEST,
                  preferred_element_type=jnp.float32)
    return out.reshape(dims + (HEADS * HEAD_DIM,))


def partner(value, axis, step, count):
    return lax.ppermute(value, axis, [(i, i ^ step) for i in range(count)])


def broadcast_from(value, axis, count, source):
    here = lax.axis_index(axis)
    step = 1
    while step < count:
        got = partner(value, axis, step, count)
        value = jnp.where(here // step == source // step, value, got)
        step *= 2
    return value


def merge(lo, hi, width):
    top = jnp.maximum(lo[:, width + HEADS :], hi[:, width + HEADS :])
    fade_lo = jnp.exp(lo[:, width + HEADS :] - top)
    fade_hi = jnp.exp(hi[:, width + HEADS :] - top)
    total = lo[:, width : width + HEADS] * fade_lo + hi[:, width : width + HEADS] * fade_hi
    fades = head_spread(jnp.concatenate([fade_lo, fade_hi], axis=0))
    rows = lo.shape[0]
    mixed = lo[:, :width] * fades[:rows] + hi[:, :width] * fades[rows:]
    return jnp.concatenate([mixed, total, top], axis=-1)


def all_merge(value, axis, count, width):
    here = lax.axis_index(axis)
    step = 1
    while step < count:
        got = partner(value, axis, step, count)
        low_side = (here & step) == 0
        lo = jnp.where(low_side, value, got)
        hi = jnp.where(low_side, got, value)
        value = merge(lo, hi, width)
        step *= 2
    return value


def fan_out(value, axis, count):
    here = lax.axis_index(axis)
    got = []
    for step in range(1, count):
        if count & (count - 1) == 0:
            pairs = [(i, i ^ step) for i in range(count)]
            source = here ^ step
        else:
            pairs = [(i, (i + step) % count) for i in range(count)]
            source = (here - step) % count
        got.append((source, lax.ppermute(value, axis, pairs)))
    return got


def local(cells, summary, owner, schema, w_qkv, w_out, gain_attn, w_up, w_down, gain_ffn, *, n_band, n_col):
    row_count, cols_dev, model_width = cells.shape
    own_group = lax.axis_index("col")
    own_band = lax.axis_index("band")
    score_scale = HEAD_DIM ** (-0.5)
    flat_cells = cells.reshape(row_count * cols_dev, model_width)
    w_kv = w_qkv[:, model_width:]

    tokens = broadcast_from(summary[0], "band", n_band, owner[0])
    row_parts = fan_out(cells, "col", n_col)

    qkv_cells = project(flat_cells, w_qkv).reshape(row_count, cols_dev, 3 * model_width)
    queries = qkv_cells[:, :, :model_width]
    own_keys = qkv_cells[:, :, model_width : 2 * model_width]
    own_vals = qkv_cells[:, :, 2 * model_width :]

    summary_qkv = project(tokens, w_qkv)
    sum_queries = summary_qkv[:, :model_width]
    sum_keys = summary_qkv[:, model_width : 2 * model_width]
    sum_vals = summary_qkv[:, 2 * model_width :]

    sq = sum_queries.astype(jnp.float32)
    col_scores = head_sum(sq[None] * own_keys.astype(jnp.float32)) * score_scale
    self_scores = head_sum(sq * sum_keys.astype(jnp.float32)) * score_scale
    part_top = col_scores.max(0)
    col_exp = jnp.exp(col_scores - part_top[None])
    col_weights = head_spread(col_exp.astype(jnp.bfloat16).astype(jnp.float32))
    part_mixed = (col_weights * own_vals.astype(jnp.float32)).sum(0)
    part_total = col_exp.sum(0)
    packed = jnp.concatenate([part_mixed, part_total, part_top], axis=-1)
    packed = all_merge(packed, "band", n_band, model_width)
    col_top = jnp.maximum(packed[:, model_width + HEADS :], self_scores)
    fade = jnp.exp(packed[:, model_width + HEADS :] - col_top)
    self_exp = jnp.exp(self_scores - col_top)
    col_total = packed[:, model_width : model_width + HEADS] * fade + self_exp
    spreads = head_spread(jnp.concatenate([fade, self_exp.astype(jnp.bfloat16).astype(jnp.float32)], axis=0))
    col_mixed = packed[:, :model_width] * spreads[:cols_dev] + spreads[cols_dev:] * sum_vals.astype(jnp.float32)
    summary_att = (col_mixed / head_spread(col_total)).astype(jnp.bfloat16)

    sources = [own_group] + [s for s, _ in row_parts]
    other_cells = jnp.concatenate([got for _, got in row_parts], axis=1)
    width_other = other_cells.shape[1]
    other_kv = project(other_cells.reshape(row_count * width_other, model_width), w_kv)
    other_kv = other_kv.reshape(row_count, width_other, 2 * model_width)
    row_keys = jnp.concatenate([own_keys, other_kv[:, :, :model_width]], axis=1)
    row_vals = jnp.concatenate([own_vals, other_kv[:, :, model_width:]], axis=1)
    width_now = row_keys.shape[1]
    q4 = queries.reshape(row_count, cols_dev, HEADS, HEAD_DIM)
    k4 = row_keys.reshape(row_count, width_now, HEADS, HEAD_DIM)
    v4 = row_vals.reshape(row_count, width_now, HEADS, HEAD_DIM)
    sk = sum_keys.reshape(cols_dev, HEADS, HEAD_DIM)
    sv = sum_vals.reshape(cols_dev, HEADS, HEAD_DIM)
    key_groups = jnp.concatenate(
        [jnp.full((cols_dev,), s, jnp.int32) for s in sources]
    )
    own_block = jnp.arange(width_now, dtype=jnp.int32) < cols_dev
    allowed = (jnp.right_shift(schema[:, :, None], key_groups[None, None, :]) & 1 == 1) | own_block[
        None, None, :
    ]
    cell_scores = (
        jnp.einsum("rqhd,rkhd->rhqk", q4, k4, preferred_element_type=jnp.float32) * score_scale
    )
    cell_scores = jnp.where(allowed[:, None], cell_scores, -1e30)
    tok_scores = (
        jnp.einsum("rqhd,khd->rhqk", q4, sk, preferred_element_type=jnp.float32) * score_scale
    )
    row_top = jnp.maximum(cell_scores.max(-1), tok_scores.max(-1))
    cell_exp = jnp.exp(cell_scores - row_top[..., None])
    tok_exp = jnp.exp(tok_scores - row_top[..., None])
    row_total = cell_exp.sum(-1) + tok_exp.sum(-1)
    mixed = jnp.einsum(
        "rhqk,rkhd->rqhd", cell_exp.astype(jnp.bfloat16), v4, preferred_element_type=jnp.float32
    )
    mixed = mixed + jnp.einsum(
        "rhqk,khd->rqhd", tok_exp.astype(jnp.bfloat16), sv, preferred_element_type=jnp.float32
    )
    attended = mixed / row_total.transpose(0, 2, 1)[..., None]
    attended = attended.reshape(row_count * cols_dev, model_width).astype(jnp.bfloat16)

    all_in = jnp.concatenate([flat_cells, tokens], axis=0)
    all_att = jnp.concatenate([attended, summary_att], axis=0)
    all_out = finish(all_in, all_att, w_out, gain_attn, w_up, w_down, gain_ffn)
    cells_out = all_out[: row_count * cols_dev].reshape(row_count, cols_dev, model_width)
    summary_out = all_out[row_count * cols_dev :]
    return (cells_out, summary_out)


def solution(mesh):
    in_specs = (
        P("band", "col", None),
        P("band", "col", None),
        P("col"),
        P("band", "col"),
        P(),
        P(),
        P(),
        P(),
        P(),
        P(),
    )
    out_specs = (P("band", "col", None), P("col", None))
    body = functools.partial(local, n_band=mesh.shape["band"], n_col=mesh.shape["col"])
    return jax.shard_map(body, mesh=mesh, in_specs=in_specs, out_specs=out_specs, check_vma=False)
```

```python
import functools

import jax
import jax.numpy as jnp
from jax import lax
from jax.sharding import PartitionSpec as P

HEADS = 12
HEAD_DIM = 64


def spread_2(value, axis, source):
    kept = jnp.where(lax.axis_index(axis) == source, value, 0).astype(value.dtype)
    return lax.psum(kept, axis)


def layer_norm(values, gain_vec):
    center = values - jnp.mean(values, -1, keepdims=True)
    spread = jnp.mean(center * center, -1, keepdims=True)
    return center * lax.rsqrt(spread + 1e-05) * gain_vec


def finish(tokens_in, attended, w_out, gain_attn, w_up, w_down, gain_ffn):
    mixed_out = jnp.dot(attended, w_out, preferred_element_type=jnp.float32)
    hidden = layer_norm(tokens_in.astype(jnp.float32) + mixed_out, gain_attn).astype(jnp.bfloat16)
    inner_act = jax.nn.gelu(jnp.dot(hidden, w_up, preferred_element_type=jnp.float32)).astype(
        jnp.bfloat16
    )
    outer_out = jnp.dot(inner_act, w_down, preferred_element_type=jnp.float32)
    return layer_norm(hidden.astype(jnp.float32) + outer_out, gain_ffn).astype(jnp.bfloat16)


def project(values, weight):
    return jnp.dot(values, weight, preferred_element_type=jnp.float32).astype(jnp.bfloat16)


def head_matrix():
    lanes = jnp.arange(HEADS * HEAD_DIM, dtype=jnp.int32) // HEAD_DIM
    return (lanes[None, :] == jnp.arange(HEADS, dtype=jnp.int32)[:, None]).astype(jnp.float32)


def head_sum(values):
    dims = values.shape[:-1]
    flat = values.reshape(-1, values.shape[-1])
    out = jnp.dot(flat, head_matrix().T, precision=lax.Precision.HIGHEST,
                  preferred_element_type=jnp.float32)
    return out.reshape(dims + (HEADS,))


def head_spread(values):
    dims = values.shape[:-1]
    flat = values.reshape(-1, HEADS)
    out = jnp.dot(flat, head_matrix(), precision=lax.Precision.HIGHEST,
                  preferred_element_type=jnp.float32)
    return out.reshape(dims + (HEADS * HEAD_DIM,))


def partner(value, axis, step, count):
    return lax.ppermute(value, axis, [(i, i ^ step) for i in range(count)])


def broadcast_from(value, axis, count, source):
    here = lax.axis_index(axis)
    step = 1
    while step < count:
        got = partner(value, axis, step, count)
        value = jnp.where(here // step == source // step, value, got)
        step *= 2
    return value


def merge(lo, hi, width):
    top = jnp.maximum(lo[:, width + HEADS :], hi[:, width + HEADS :])
    fade_lo = jnp.exp(lo[:, width + HEADS :] - top)
    fade_hi = jnp.exp(hi[:, width + HEADS :] - top)
    total = lo[:, width : width + HEADS] * fade_lo + hi[:, width : width + HEADS] * fade_hi
    fades = head_spread(jnp.concatenate([fade_lo, fade_hi], axis=0))
    rows = lo.shape[0]
    mixed = lo[:, :width] * fades[:rows] + hi[:, :width] * fades[rows:]
    return jnp.concatenate([mixed, total, top], axis=-1)


def swap(value, axis, step, count, width, narrow):
    if not narrow:
        return value, partner(value, axis, step, count)
    mixed = value[:, :width].astype(jnp.bfloat16)
    stats = value[:, width:]
    got_mixed = partner(mixed, axis, step, count)
    got_stats = partner(stats, axis, step, count)
    mine = jnp.concatenate([mixed.astype(jnp.float32), stats], axis=-1)
    got = jnp.concatenate([got_mixed.astype(jnp.float32), got_stats], axis=-1)
    return mine, got


def all_merge(value, axis, count, width):
    here = lax.axis_index(axis)
    half = value.shape[0] // 2
    first = (here & 1) == 0
    mine = jnp.where(first, value[:half], value[half:])
    sent = jnp.where(first, value[half:], value[:half])
    got = partner(sent, axis, 1, count)
    value = merge(jnp.where(first, mine, got), jnp.where(first, got, mine), width)
    step = 2
    while step < count:
        mine, got = swap(value, axis, step, count, width, True)
        low_side = (here & step) == 0
        lo = jnp.where(low_side, mine, got)
        hi = jnp.where(low_side, got, mine)
        value = merge(lo, hi, width)
        step *= 2
    got = partner(value, axis, 1, count)
    return jnp.where(first, jnp.concatenate([value, got]), jnp.concatenate([got, value]))


def fan_out(value, axis, count):
    here = lax.axis_index(axis)
    got = []
    for step in range(1, count):
        if count & (count - 1) == 0:
            pairs = [(i, i ^ step) for i in range(count)]
            source = here ^ step
        else:
            pairs = [(i, (i + step) % count) for i in range(count)]
            source = (here - step) % count
        got.append((source, lax.ppermute(value, axis, pairs)))
    return got


def local(cells, summary, owner, schema, w_qkv, w_out, gain_attn, w_up, w_down, gain_ffn, *, n_band, n_col):
    row_count, cols_dev, model_width = cells.shape
    own_group = lax.axis_index("col")
    own_band = lax.axis_index("band")
    score_scale = HEAD_DIM ** (-0.5)
    flat_cells = cells.reshape(row_count * cols_dev, model_width)
    w_kv = w_qkv[:, model_width:]

    tokens = broadcast_from(summary[0], "band", n_band, owner[0])
    row_parts = fan_out(cells, "col", n_col)

    qkv_cells = project(flat_cells, w_qkv).reshape(row_count, cols_dev, 3 * model_width)
    queries = qkv_cells[:, :, :model_width]
    own_keys = qkv_cells[:, :, model_width : 2 * model_width]
    own_vals = qkv_cells[:, :, 2 * model_width :]

    summary_qkv = project(tokens, w_qkv)
    sum_queries = summary_qkv[:, :model_width]
    sum_keys = summary_qkv[:, model_width : 2 * model_width]
    sum_vals = summary_qkv[:, 2 * model_width :]

    sq = sum_queries.astype(jnp.float32)
    col_scores = head_sum(sq[None] * own_keys.astype(jnp.float32)) * score_scale
    self_scores = head_sum(sq * sum_keys.astype(jnp.float32)) * score_scale
    part_top = col_scores.max(0)
    col_exp = jnp.exp(col_scores - part_top[None])
    col_weights = head_spread(col_exp.astype(jnp.bfloat16).astype(jnp.float32))
    part_mixed = (col_weights * own_vals.astype(jnp.float32)).sum(0)
    part_total = col_exp.sum(0)
    packed = jnp.concatenate([part_mixed, part_total, part_top], axis=-1)
    packed = all_merge(packed, "band", n_band, model_width)
    col_top = jnp.maximum(packed[:, model_width + HEADS :], self_scores)
    fade = jnp.exp(packed[:, model_width + HEADS :] - col_top)
    self_exp = jnp.exp(self_scores - col_top)
    col_total = packed[:, model_width : model_width + HEADS] * fade + self_exp
    spreads = head_spread(jnp.concatenate([fade, self_exp.astype(jnp.bfloat16).astype(jnp.float32)], axis=0))
    col_mixed = packed[:, :model_width] * spreads[:cols_dev] + spreads[cols_dev:] * sum_vals.astype(jnp.float32)
    summary_att = (col_mixed / head_spread(col_total)).astype(jnp.bfloat16)

    sources = [own_group] + [s for s, _ in row_parts]
    other_cells = jnp.concatenate([got for _, got in row_parts], axis=1)
    width_other = other_cells.shape[1]
    other_kv = project(other_cells.reshape(row_count * width_other, model_width), w_kv)
    other_kv = other_kv.reshape(row_count, width_other, 2 * model_width)
    row_keys = jnp.concatenate([own_keys, other_kv[:, :, :model_width]], axis=1)
    row_vals = jnp.concatenate([own_vals, other_kv[:, :, model_width:]], axis=1)
    width_now = row_keys.shape[1]
    q4 = queries.reshape(row_count, cols_dev, HEADS, HEAD_DIM)
    k4 = row_keys.reshape(row_count, width_now, HEADS, HEAD_DIM)
    v4 = row_vals.reshape(row_count, width_now, HEADS, HEAD_DIM)
    sk = sum_keys.reshape(cols_dev, HEADS, HEAD_DIM)
    sv = sum_vals.reshape(cols_dev, HEADS, HEAD_DIM)
    key_groups = jnp.concatenate(
        [jnp.full((cols_dev,), s, jnp.int32) for s in sources]
    )
    own_block = jnp.arange(width_now, dtype=jnp.int32) < cols_dev
    allowed = (jnp.right_shift(schema[:, :, None], key_groups[None, None, :]) & 1 == 1) | own_block[
        None, None, :
    ]
    cell_scores = (
        jnp.einsum("rqhd,rkhd->rhqk", q4, k4, preferred_element_type=jnp.float32) * score_scale
    )
    cell_scores = jnp.where(allowed[:, None], cell_scores, -1e30)
    tok_scores = (
        jnp.einsum("rqhd,khd->rhqk", q4, sk, preferred_element_type=jnp.float32) * score_scale
    )
    row_top = jnp.maximum(cell_scores.max(-1), tok_scores.max(-1))
    cell_exp = jnp.exp(cell_scores - row_top[..., None])
    tok_exp = jnp.exp(tok_scores - row_top[..., None])
    row_total = cell_exp.sum(-1) + tok_exp.sum(-1)
    mixed = jnp.einsum(
        "rhqk,rkhd->rqhd", cell_exp.astype(jnp.bfloat16), v4, preferred_element_type=jnp.float32
    )
    mixed = mixed + jnp.einsum(
        "rhqk,khd->rqhd", tok_exp.astype(jnp.bfloat16), sv, preferred_element_type=jnp.float32
    )
    attended = mixed / row_total.transpose(0, 2, 1)[..., None]
    attended = attended.reshape(row_count * cols_dev, model_width).astype(jnp.bfloat16)

    all_in = jnp.concatenate([flat_cells, tokens], axis=0)
    all_att = jnp.concatenate([attended, summary_att], axis=0)
    all_out = finish(all_in, all_att, w_out, gain_attn, w_up, w_down, gain_ffn)
    cells_out = all_out[: row_count * cols_dev].reshape(row_count, cols_dev, model_width)
    summary_out = all_out[row_count * cols_dev :]
    return (cells_out, summary_out)


def solution(mesh):
    in_specs = (
        P("band", "col", None),
        P("band", "col", None),
        P("col"),
        P("band", "col"),
        P(),
        P(),
        P(),
        P(),
        P(),
        P(),
    )
    out_specs = (P("band", "col", None), P("col", None))
    body = functools.partial(local, n_band=mesh.shape["band"], n_col=mesh.shape["col"])
    return jax.shard_map(body, mesh=mesh, in_specs=in_specs, out_specs=out_specs, check_vma=False)
```

```python
import functools

import jax
import jax.numpy as jnp
from jax import lax
from jax.sharding import PartitionSpec as P

HEADS = 12
HEAD_DIM = 64


def spread_2(value, axis, source):
    kept = jnp.where(lax.axis_index(axis) == source, value, 0).astype(value.dtype)
    return lax.psum(kept, axis)


def layer_norm(values, gain_vec):
    center = values - jnp.mean(values, -1, keepdims=True)
    spread = jnp.mean(center * center, -1, keepdims=True)
    return center * lax.rsqrt(spread + 1e-05) * gain_vec


def finish(tokens_in, attended, w_out, gain_attn, w_up, w_down, gain_ffn):
    mixed_out = jnp.dot(attended, w_out, preferred_element_type=jnp.float32)
    hidden = layer_norm(tokens_in.astype(jnp.float32) + mixed_out, gain_attn).astype(jnp.bfloat16)
    inner_act = jax.nn.gelu(jnp.dot(hidden, w_up, preferred_element_type=jnp.float32)).astype(
        jnp.bfloat16
    )
    outer_out = jnp.dot(inner_act, w_down, preferred_element_type=jnp.float32)
    return layer_norm(hidden.astype(jnp.float32) + outer_out, gain_ffn).astype(jnp.bfloat16)


def project(values, weight):
    return jnp.dot(values, weight, preferred_element_type=jnp.float32).astype(jnp.bfloat16)


def head_matrix():
    lanes = jnp.arange(HEADS * HEAD_DIM, dtype=jnp.int32) // HEAD_DIM
    return (lanes[None, :] == jnp.arange(HEADS, dtype=jnp.int32)[:, None]).astype(jnp.float32)


def head_sum(values):
    dims = values.shape[:-1]
    flat = values.reshape(-1, values.shape[-1])
    out = jnp.dot(flat, head_matrix().T, precision=lax.Precision.HIGHEST,
                  preferred_element_type=jnp.float32)
    return out.reshape(dims + (HEADS,))


def head_spread(values):
    dims = values.shape[:-1]
    flat = values.reshape(-1, HEADS)
    out = jnp.dot(flat, head_matrix(), precision=lax.Precision.HIGHEST,
                  preferred_element_type=jnp.float32)
    return out.reshape(dims + (HEADS * HEAD_DIM,))


def partner(value, axis, step, count):
    return lax.ppermute(value, axis, [(i, i ^ step) for i in range(count)])


def broadcast_from(value, axis, count, source):
    here = lax.axis_index(axis)
    step = 1
    while step < count:
        got = partner(value, axis, step, count)
        value = jnp.where(here // step == source // step, value, got)
        step *= 2
    return value


def merge(lo, hi, width):
    top = jnp.maximum(lo[:, width + HEADS :], hi[:, width + HEADS :])
    fade_lo = jnp.exp(lo[:, width + HEADS :] - top)
    fade_hi = jnp.exp(hi[:, width + HEADS :] - top)
    total = lo[:, width : width + HEADS] * fade_lo + hi[:, width : width + HEADS] * fade_hi
    fades = head_spread(jnp.concatenate([fade_lo, fade_hi], axis=0))
    rows = lo.shape[0]
    mixed = lo[:, :width] * fades[:rows] + hi[:, :width] * fades[rows:]
    return jnp.concatenate([mixed, total, top], axis=-1)


def all_merge(value, axis, count, width, fillers, state):
    here = lax.axis_index(axis)
    rounds = [0]

    def exchange(sent, state):
        k = rounds[0]
        rounds[0] += 1
        if k < len(fillers):
            sent, state = lax.optimization_barrier((sent, state))
        got = [partner(s, axis, step_of[k], count) for s in sent]
        if k < len(fillers):
            state = fillers[k](state)
            got, state = lax.optimization_barrier((got, state))
        return got, state

    steps = []
    step = 2
    while step < count:
        steps.append(step)
        step *= 2
    step_of = [1] + steps + [1]

    half = value.shape[0] // 2
    first = (here & 1) == 0
    mine = jnp.where(first, value[:half], value[half:])
    sent = jnp.where(first, value[half:], value[:half])
    (got,), state = exchange([sent], state)
    value = merge(jnp.where(first, mine, got), jnp.where(first, got, mine), width)
    for step in steps:
        mixed = value[:, :width].astype(jnp.bfloat16)
        stats = value[:, width:]
        (got_mixed, got_stats), state = exchange([mixed, stats], state)
        mine = jnp.concatenate([mixed.astype(jnp.float32), stats], axis=-1)
        got = jnp.concatenate([got_mixed.astype(jnp.float32), got_stats], axis=-1)
        low_side = (here & step) == 0
        value = merge(jnp.where(low_side, mine, got), jnp.where(low_side, got, mine), width)
    (got,), state = exchange([value], state)
    value = jnp.where(first, jnp.concatenate([value, got]), jnp.concatenate([got, value]))
    return value, state


def fan_out(value, axis, count):
    here = lax.axis_index(axis)
    got = []
    for step in range(1, count):
        if count & (count - 1) == 0:
            pairs = [(i, i ^ step) for i in range(count)]
            source = here ^ step
        else:
            pairs = [(i, (i + step) % count) for i in range(count)]
            source = (here - step) % count
        got.append((source, lax.ppermute(value, axis, pairs)))
    return got


def local(cells, summary, owner, schema, w_qkv, w_out, gain_attn, w_up, w_down, gain_ffn, *, n_band, n_col):
    row_count, cols_dev, model_width = cells.shape
    own_group = lax.axis_index("col")
    own_band = lax.axis_index("band")
    score_scale = HEAD_DIM ** (-0.5)
    flat_cells = cells.reshape(row_count * cols_dev, model_width)
    w_kv = w_qkv[:, model_width:]

    tokens = broadcast_from(summary[0], "band", n_band, owner[0])
    row_parts = fan_out(cells, "col", n_col)

    qkv_cells = project(flat_cells, w_qkv).reshape(row_count, cols_dev, 3 * model_width)
    queries = qkv_cells[:, :, :model_width]
    own_keys = qkv_cells[:, :, model_width : 2 * model_width]
    own_vals = qkv_cells[:, :, 2 * model_width :]

    summary_qkv = project(tokens, w_qkv)
    sum_queries = summary_qkv[:, :model_width]
    sum_keys = summary_qkv[:, model_width : 2 * model_width]
    sum_vals = summary_qkv[:, 2 * model_width :]

    sq = sum_queries.astype(jnp.float32)
    col_scores = head_sum(sq[None] * own_keys.astype(jnp.float32)) * score_scale
    self_scores = head_sum(sq * sum_keys.astype(jnp.float32)) * score_scale
    part_top = col_scores.max(0)
    col_exp = jnp.exp(col_scores - part_top[None])
    col_weights = head_spread(col_exp.astype(jnp.bfloat16).astype(jnp.float32))
    part_mixed = (col_weights * own_vals.astype(jnp.float32)).sum(0)
    part_total = col_exp.sum(0)
    packed = jnp.concatenate([part_mixed, part_total, part_top], axis=-1)

    sources = [own_group] + [s for s, _ in row_parts]
    q4 = queries.reshape(row_count, cols_dev, HEADS, HEAD_DIM)
    sk = sum_keys.reshape(cols_dev, HEADS, HEAD_DIM)
    sv = sum_vals.reshape(cols_dev, HEADS, HEAD_DIM)

    def scores_stage(state):
        other_cells = jnp.concatenate(state, axis=1)
        width_other = other_cells.shape[1]
        other_kv = project(other_cells.reshape(row_count * width_other, model_width), w_kv)
        other_kv = other_kv.reshape(row_count, width_other, 2 * model_width)
        row_keys = jnp.concatenate([own_keys, other_kv[:, :, :model_width]], axis=1)
        row_vals = jnp.concatenate([own_vals, other_kv[:, :, model_width:]], axis=1)
        width_now = row_keys.shape[1]
        k4 = row_keys.reshape(row_count, width_now, HEADS, HEAD_DIM)
        v4 = row_vals.reshape(row_count, width_now, HEADS, HEAD_DIM)
        key_groups = jnp.concatenate([jnp.full((cols_dev,), s, jnp.int32) for s in sources])
        own_block = jnp.arange(width_now, dtype=jnp.int32) < cols_dev
        allowed = (jnp.right_shift(schema[:, :, None], key_groups[None, None, :]) & 1 == 1) | (
            own_block[None, None, :]
        )
        cell_scores = (
            jnp.einsum("rqhd,rkhd->rhqk", q4, k4, preferred_element_type=jnp.float32) * score_scale
        )
        cell_scores = jnp.where(allowed[:, None], cell_scores, -1e30)
        tok_scores = (
            jnp.einsum("rqhd,khd->rhqk", q4, sk, preferred_element_type=jnp.float32) * score_scale
        )
        return cell_scores, tok_scores, v4

    def weights_stage(state):
        cell_scores, tok_scores, v4 = state
        row_top = jnp.maximum(cell_scores.max(-1), tok_scores.max(-1))
        cell_exp = jnp.exp(cell_scores - row_top[..., None])
        tok_exp = jnp.exp(tok_scores - row_top[..., None])
        row_total = cell_exp.sum(-1) + tok_exp.sum(-1)
        mixed = jnp.einsum(
            "rhqk,rkhd->rqhd", cell_exp.astype(jnp.bfloat16), v4, preferred_element_type=jnp.float32
        )
        return mixed, tok_exp.astype(jnp.bfloat16), row_total

    def output_stage(state):
        mixed, tok_weights, row_total = state
        mixed = mixed + jnp.einsum(
            "rhqk,khd->rqhd", tok_weights, sv, preferred_element_type=jnp.float32
        )
        attended = mixed / row_total.transpose(0, 2, 1)[..., None]
        return attended.reshape(row_count * cols_dev, model_width).astype(jnp.bfloat16)

    packed, attended = all_merge(
        packed, "band", n_band, model_width,
        [scores_stage, weights_stage, output_stage],
        [got for _, got in row_parts],
    )
    col_top = jnp.maximum(packed[:, model_width + HEADS :], self_scores)
    fade = jnp.exp(packed[:, model_width + HEADS :] - col_top)
    self_exp = jnp.exp(self_scores - col_top)
    col_total = packed[:, model_width : model_width + HEADS] * fade + self_exp
    spreads = head_spread(jnp.concatenate([fade, self_exp.astype(jnp.bfloat16).astype(jnp.float32)], axis=0))
    col_mixed = packed[:, :model_width] * spreads[:cols_dev] + spreads[cols_dev:] * sum_vals.astype(jnp.float32)
    summary_att = (col_mixed / head_spread(col_total)).astype(jnp.bfloat16)

    all_in = jnp.concatenate([flat_cells, tokens], axis=0)
    all_att = jnp.concatenate([attended, summary_att], axis=0)
    all_out = finish(all_in, all_att, w_out, gain_attn, w_up, w_down, gain_ffn)
    cells_out = all_out[: row_count * cols_dev].reshape(row_count, cols_dev, model_width)
    summary_out = all_out[row_count * cols_dev :]
    return (cells_out, summary_out)


def solution(mesh):
    in_specs = (
        P("band", "col", None),
        P("band", "col", None),
        P("col"),
        P("band", "col"),
        P(),
        P(),
        P(),
        P(),
        P(),
        P(),
    )
    out_specs = (P("band", "col", None), P("col", None))
    body = functools.partial(local, n_band=mesh.shape["band"], n_col=mesh.shape["col"])
    return jax.shard_map(body, mesh=mesh, in_specs=in_specs, out_specs=out_specs, check_vma=False)
```

```python
import functools

import jax
import jax.numpy as jnp
from jax import lax
from jax.sharding import PartitionSpec as P

HEADS = 12
HEAD_DIM = 64


def spread_2(value, axis, source):
    kept = jnp.where(lax.axis_index(axis) == source, value, 0).astype(value.dtype)
    return lax.psum(kept, axis)


def layer_norm(values, gain_vec):
    center = values - jnp.mean(values, -1, keepdims=True)
    spread = jnp.mean(center * center, -1, keepdims=True)
    return center * lax.rsqrt(spread + 1e-05) * gain_vec


def finish(tokens_in, attended, w_out, gain_attn, w_up, w_down, gain_ffn):
    mixed_out = jnp.dot(attended, w_out, preferred_element_type=jnp.float32)
    hidden = layer_norm(tokens_in.astype(jnp.float32) + mixed_out, gain_attn).astype(jnp.bfloat16)
    inner_act = jax.nn.gelu(jnp.dot(hidden, w_up, preferred_element_type=jnp.float32)).astype(
        jnp.bfloat16
    )
    outer_out = jnp.dot(inner_act, w_down, preferred_element_type=jnp.float32)
    return layer_norm(hidden.astype(jnp.float32) + outer_out, gain_ffn).astype(jnp.bfloat16)


def project(values, weight):
    return jnp.dot(values, weight, preferred_element_type=jnp.float32).astype(jnp.bfloat16)


def head_matrix():
    lanes = jnp.arange(HEADS * HEAD_DIM, dtype=jnp.int32) // HEAD_DIM
    return (lanes[None, :] == jnp.arange(HEADS, dtype=jnp.int32)[:, None]).astype(jnp.float32)


def head_sum(values):
    dims = values.shape[:-1]
    flat = values.reshape(-1, values.shape[-1])
    out = jnp.dot(flat, head_matrix().T, precision=lax.Precision.HIGHEST,
                  preferred_element_type=jnp.float32)
    return out.reshape(dims + (HEADS,))


def head_spread(values):
    dims = values.shape[:-1]
    flat = values.reshape(-1, HEADS)
    out = jnp.dot(flat, head_matrix(), precision=lax.Precision.HIGHEST,
                  preferred_element_type=jnp.float32)
    return out.reshape(dims + (HEADS * HEAD_DIM,))


def partner(value, axis, step, count):
    return lax.ppermute(value, axis, [(i, i ^ step) for i in range(count)])


def broadcast_from(value, axis, count, source):
    here = lax.axis_index(axis)
    step = 1
    while step < count:
        got = partner(value, axis, step, count)
        value = jnp.where(here // step == source // step, value, got)
        step *= 2
    return value


def merge(lo, hi):
    top = jnp.maximum(lo[2], hi[2])
    fade_lo = jnp.exp(lo[2] - top)
    fade_hi = jnp.exp(hi[2] - top)
    total = lo[1] * fade_lo + hi[1] * fade_hi
    mixed = lo[0] * head_spread(fade_lo) + hi[0] * head_spread(fade_hi)
    return mixed, total, top


def pick(flag, a, b):
    return tuple(jnp.where(flag, x, y) for x, y in zip(a, b))


def all_merge(value, axis, count):
    here = lax.axis_index(axis)
    half = value[0].shape[0] // 2
    first = (here & 1) == 0
    top_half = tuple(v[:half] for v in value)
    low_half = tuple(v[half:] for v in value)
    mine = pick(first, top_half, low_half)
    sent = pick(first, low_half, top_half)
    got = tuple(partner(v, axis, 1, count) for v in sent)
    value = merge(pick(first, mine, got), pick(first, got, mine))
    step = 2
    while step < count:
        mixed = value[0].astype(jnp.bfloat16)
        got = (
            partner(mixed, axis, step, count).astype(jnp.float32),
            partner(value[1], axis, step, count),
            partner(value[2], axis, step, count),
        )
        mine = (mixed.astype(jnp.float32), value[1], value[2])
        low_side = (here & step) == 0
        value = merge(pick(low_side, mine, got), pick(low_side, got, mine))
        step *= 2
    got = tuple(partner(v, axis, 1, count) for v in value)
    return tuple(
        jnp.where(first, jnp.concatenate([v, g]), jnp.concatenate([g, v]))
        for v, g in zip(value, got)
    )


def fan_out(value, axis, count):
    here = lax.axis_index(axis)
    got = []
    for step in range(1, count):
        if count & (count - 1) == 0:
            pairs = [(i, i ^ step) for i in range(count)]
            source = here ^ step
        else:
            pairs = [(i, (i + step) % count) for i in range(count)]
            source = (here - step) % count
        got.append((source, lax.ppermute(value, axis, pairs)))
    return got


def local(cells, summary, owner, schema, w_qkv, w_out, gain_attn, w_up, w_down, gain_ffn, *, n_band, n_col):
    row_count, cols_dev, model_width = cells.shape
    own_group = lax.axis_index("col")
    own_band = lax.axis_index("band")
    score_scale = HEAD_DIM ** (-0.5)
    flat_cells = cells.reshape(row_count * cols_dev, model_width)
    w_kv = w_qkv[:, model_width:]

    tokens = broadcast_from(summary[0], "band", n_band, owner[0])
    row_parts = fan_out(cells, "col", n_col)

    qkv_cells = project(flat_cells, w_qkv).reshape(row_count, cols_dev, 3 * model_width)
    queries = qkv_cells[:, :, :model_width]
    own_keys = qkv_cells[:, :, model_width : 2 * model_width]
    own_vals = qkv_cells[:, :, 2 * model_width :]

    summary_qkv = project(tokens, w_qkv)
    sum_queries = summary_qkv[:, :model_width]
    sum_keys = summary_qkv[:, model_width : 2 * model_width]
    sum_vals = summary_qkv[:, 2 * model_width :]

    sq = sum_queries.astype(jnp.float32)
    col_scores = head_sum(sq[None] * own_keys.astype(jnp.float32)) * score_scale
    self_scores = head_sum(sq * sum_keys.astype(jnp.float32)) * score_scale
    part_top = col_scores.max(0)
    col_exp = jnp.exp(col_scores - part_top[None])
    col_weights = head_spread(col_exp.astype(jnp.bfloat16).astype(jnp.float32))
    part_mixed = (col_weights * own_vals.astype(jnp.float32)).sum(0)
    part_total = col_exp.sum(0)
    merged = all_merge((part_mixed, part_total, part_top), "band", n_band)
    col_top = jnp.maximum(merged[2], self_scores)
    fade = jnp.exp(merged[2] - col_top)
    self_exp = jnp.exp(self_scores - col_top)
    col_total = merged[1] * fade + self_exp
    col_mixed = merged[0] * head_spread(fade) + head_spread(
        self_exp.astype(jnp.bfloat16).astype(jnp.float32)
    ) * sum_vals.astype(jnp.float32)
    summary_att = (col_mixed / head_spread(col_total)).astype(jnp.bfloat16)

    sources = [own_group] + [s for s, _ in row_parts]
    other_cells = jnp.concatenate([got for _, got in row_parts], axis=1)
    width_other = other_cells.shape[1]
    other_kv = project(other_cells.reshape(row_count * width_other, model_width), w_kv)
    other_kv = other_kv.reshape(row_count, width_other, 2 * model_width)
    row_keys = jnp.concatenate([own_keys, other_kv[:, :, :model_width]], axis=1)
    row_vals = jnp.concatenate([own_vals, other_kv[:, :, model_width:]], axis=1)
    width_now = row_keys.shape[1]
    q4 = queries.reshape(row_count, cols_dev, HEADS, HEAD_DIM)
    k4 = row_keys.reshape(row_count, width_now, HEADS, HEAD_DIM)
    v4 = row_vals.reshape(row_count, width_now, HEADS, HEAD_DIM)
    sk = sum_keys.reshape(cols_dev, HEADS, HEAD_DIM)
    sv = sum_vals.reshape(cols_dev, HEADS, HEAD_DIM)
    key_groups = jnp.concatenate(
        [jnp.full((cols_dev,), s, jnp.int32) for s in sources]
    )
    own_block = jnp.arange(width_now, dtype=jnp.int32) < cols_dev
    allowed = (jnp.right_shift(schema[:, :, None], key_groups[None, None, :]) & 1 == 1) | own_block[
        None, None, :
    ]
    cell_scores = (
        jnp.einsum("rqhd,rkhd->rhqk", q4, k4, preferred_element_type=jnp.float32) * score_scale
    )
    cell_scores = jnp.where(allowed[:, None], cell_scores, -1e30)
    tok_scores = (
        jnp.einsum("rqhd,khd->rhqk", q4, sk, preferred_element_type=jnp.float32) * score_scale
    )
    row_top = jnp.maximum(cell_scores.max(-1), tok_scores.max(-1))
    cell_exp = jnp.exp(cell_scores - row_top[..., None])
    tok_exp = jnp.exp(tok_scores - row_top[..., None])
    row_total = cell_exp.sum(-1) + tok_exp.sum(-1)
    mixed = jnp.einsum(
        "rhqk,rkhd->rqhd", cell_exp.astype(jnp.bfloat16), v4, preferred_element_type=jnp.float32
    )
    mixed = mixed + jnp.einsum(
        "rhqk,khd->rqhd", tok_exp.astype(jnp.bfloat16), sv, preferred_element_type=jnp.float32
    )
    attended = mixed / row_total.transpose(0, 2, 1)[..., None]
    attended = attended.reshape(row_count * cols_dev, model_width).astype(jnp.bfloat16)

    all_in = jnp.concatenate([flat_cells, tokens], axis=0)
    all_att = jnp.concatenate([attended, summary_att], axis=0)
    all_out = finish(all_in, all_att, w_out, gain_attn, w_up, w_down, gain_ffn)
    cells_out = all_out[: row_count * cols_dev].reshape(row_count, cols_dev, model_width)
    summary_out = all_out[row_count * cols_dev :]
    return (cells_out, summary_out)


def solution(mesh):
    in_specs = (
        P("band", "col", None),
        P("band", "col", None),
        P("col"),
        P("band", "col"),
        P(),
        P(),
        P(),
        P(),
        P(),
        P(),
    )
    out_specs = (P("band", "col", None), P("col", None))
    body = functools.partial(local, n_band=mesh.shape["band"], n_col=mesh.shape["col"])
    return jax.shard_map(body, mesh=mesh, in_specs=in_specs, out_specs=out_specs, check_vma=False)
```

```python
import functools

import jax
import jax.numpy as jnp
from jax import lax
from jax.sharding import PartitionSpec as P

HEADS = 12
HEAD_DIM = 64


def spread_2(value, axis, source):
    kept = jnp.where(lax.axis_index(axis) == source, value, 0).astype(value.dtype)
    return lax.psum(kept, axis)


def layer_norm(values, gain_vec):
    center = values - jnp.mean(values, -1, keepdims=True)
    spread = jnp.mean(center * center, -1, keepdims=True)
    return center * lax.rsqrt(spread + 1e-05) * gain_vec


def finish(tokens_in, attended, w_out, gain_attn, w_up, w_down, gain_ffn):
    mixed_out = jnp.dot(attended, w_out, preferred_element_type=jnp.float32)
    hidden = layer_norm(tokens_in.astype(jnp.float32) + mixed_out, gain_attn).astype(jnp.bfloat16)
    inner_act = jax.nn.gelu(jnp.dot(hidden, w_up, preferred_element_type=jnp.float32)).astype(
        jnp.bfloat16
    )
    outer_out = jnp.dot(inner_act, w_down, preferred_element_type=jnp.float32)
    return layer_norm(hidden.astype(jnp.float32) + outer_out, gain_ffn).astype(jnp.bfloat16)


def project(values, weight):
    return jnp.dot(values, weight, preferred_element_type=jnp.float32).astype(jnp.bfloat16)


def head_matrix():
    lanes = jnp.arange(HEADS * HEAD_DIM, dtype=jnp.int32) // HEAD_DIM
    return (lanes[None, :] == jnp.arange(HEADS, dtype=jnp.int32)[:, None]).astype(jnp.float32)


def head_sum(values):
    dims = values.shape[:-1]
    flat = values.reshape(-1, values.shape[-1])
    out = jnp.dot(flat, head_matrix().T, precision=lax.Precision.HIGHEST,
                  preferred_element_type=jnp.float32)
    return out.reshape(dims + (HEADS,))


def head_spread(values):
    dims = values.shape[:-1]
    flat = values.reshape(-1, HEADS)
    out = jnp.dot(flat, head_matrix(), precision=lax.Precision.HIGHEST,
                  preferred_element_type=jnp.float32)
    return out.reshape(dims + (HEADS * HEAD_DIM,))


def partner(value, axis, step, count):
    return lax.ppermute(value, axis, [(i, i ^ step) for i in range(count)])


def broadcast_from(value, axis, count, source):
    here = lax.axis_index(axis)
    step = 1
    while step < count:
        got = partner(value, axis, step, count)
        value = jnp.where(here // step == source // step, value, got)
        step *= 2
    return value


def merge(lo, hi):
    top = jnp.maximum(lo[2], hi[2])
    fade_lo = jnp.exp(lo[2] - top)
    fade_hi = jnp.exp(hi[2] - top)
    total = lo[1] * fade_lo + hi[1] * fade_hi
    mixed = lo[0] * head_spread(fade_lo) + hi[0] * head_spread(fade_hi)
    return mixed, total, top


def pick(flag, a, b):
    return tuple(jnp.where(flag, x, y) for x, y in zip(a, b))


def all_merge(value, axis, count, fillers, state):
    here = lax.axis_index(axis)
    rounds = []

    def exchange(sent, step, state):
        filler = fillers[len(rounds)] if len(rounds) < len(fillers) else None
        rounds.append(step)
        if filler is not None:
            sent, state = lax.optimization_barrier((sent, state))
        got = tuple(partner(v, axis, step, count) for v in sent)
        if filler is not None:
            state = filler(state)
            got, state = lax.optimization_barrier((got, state))
        return got, state

    half = value[0].shape[0] // 2
    first = (here & 1) == 0
    top_half = tuple(v[:half] for v in value)
    low_half = tuple(v[half:] for v in value)
    mine = pick(first, top_half, low_half)
    sent = pick(first, low_half, top_half)
    got, state = exchange(sent, 1, state)
    value = merge(pick(first, mine, got), pick(first, got, mine))
    step = 2
    while step < count:
        mixed = value[0].astype(jnp.bfloat16)
        got, state = exchange((mixed, value[1], value[2]), step, state)
        got = (got[0].astype(jnp.float32), got[1], got[2])
        mine = (mixed.astype(jnp.float32), value[1], value[2])
        low_side = (here & step) == 0
        value = merge(pick(low_side, mine, got), pick(low_side, got, mine))
        step *= 2
    got, state = exchange(value, 1, state)
    value = tuple(
        jnp.where(first, jnp.concatenate([v, g]), jnp.concatenate([g, v]))
        for v, g in zip(value, got)
    )
    return value, state


def fan_out(value, axis, count):
    here = lax.axis_index(axis)
    got = []
    for step in range(1, count):
        if count & (count - 1) == 0:
            pairs = [(i, i ^ step) for i in range(count)]
            source = here ^ step
        else:
            pairs = [(i, (i + step) % count) for i in range(count)]
            source = (here - step) % count
        got.append((source, lax.ppermute(value, axis, pairs)))
    return got


def local(cells, summary, owner, schema, w_qkv, w_out, gain_attn, w_up, w_down, gain_ffn, *, n_band, n_col):
    row_count, cols_dev, model_width = cells.shape
    own_group = lax.axis_index("col")
    own_band = lax.axis_index("band")
    score_scale = HEAD_DIM ** (-0.5)
    flat_cells = cells.reshape(row_count * cols_dev, model_width)
    w_kv = w_qkv[:, model_width:]

    tokens = broadcast_from(summary[0], "band", n_band, owner[0])
    row_parts = fan_out(cells, "col", n_col)

    qkv_cells = project(flat_cells, w_qkv).reshape(row_count, cols_dev, 3 * model_width)
    queries = qkv_cells[:, :, :model_width]
    own_keys = qkv_cells[:, :, model_width : 2 * model_width]
    own_vals = qkv_cells[:, :, 2 * model_width :]

    summary_qkv = project(tokens, w_qkv)
    sum_queries = summary_qkv[:, :model_width]
    sum_keys = summary_qkv[:, model_width : 2 * model_width]
    sum_vals = summary_qkv[:, 2 * model_width :]

    sq = sum_queries.astype(jnp.float32)
    col_scores = head_sum(sq[None] * own_keys.astype(jnp.float32)) * score_scale
    self_scores = head_sum(sq * sum_keys.astype(jnp.float32)) * score_scale
    part_top = col_scores.max(0)
    col_exp = jnp.exp(col_scores - part_top[None])
    col_weights = head_spread(col_exp.astype(jnp.bfloat16).astype(jnp.float32))
    part_mixed = (col_weights * own_vals.astype(jnp.float32)).sum(0)
    part_total = col_exp.sum(0)

    sources = [own_group] + [s for s, _ in row_parts]
    q4 = queries.reshape(row_count, cols_dev, HEADS, HEAD_DIM)
    sk = sum_keys.reshape(cols_dev, HEADS, HEAD_DIM)
    sv = sum_vals.reshape(cols_dev, HEADS, HEAD_DIM)

    def scores_stage(state):
        other_cells = jnp.concatenate(state, axis=1)
        width_other = other_cells.shape[1]
        other_kv = project(other_cells.reshape(row_count * width_other, model_width), w_kv)
        other_kv = other_kv.reshape(row_count, width_other, 2 * model_width)
        row_keys = jnp.concatenate([own_keys, other_kv[:, :, :model_width]], axis=1)
        row_vals = jnp.concatenate([own_vals, other_kv[:, :, model_width:]], axis=1)
        width_now = row_keys.shape[1]
        k4 = row_keys.reshape(row_count, width_now, HEADS, HEAD_DIM)
        v4 = row_vals.reshape(row_count, width_now, HEADS, HEAD_DIM)
        key_groups = jnp.concatenate([jnp.full((cols_dev,), s, jnp.int32) for s in sources])
        own_block = jnp.arange(width_now, dtype=jnp.int32) < cols_dev
        allowed = (jnp.right_shift(schema[:, :, None], key_groups[None, None, :]) & 1 == 1) | (
            own_block[None, None, :]
        )
        cell_scores = (
            jnp.einsum("rqhd,rkhd->rhqk", q4, k4, preferred_element_type=jnp.float32) * score_scale
        )
        cell_scores = jnp.where(allowed[:, None], cell_scores, -1e30)
        tok_scores = (
            jnp.einsum("rqhd,khd->rhqk", q4, sk, preferred_element_type=jnp.float32) * score_scale
        )
        return cell_scores, tok_scores, v4

    def weights_stage(state):
        cell_scores, tok_scores, v4 = state
        row_top = jnp.maximum(cell_scores.max(-1), tok_scores.max(-1))
        cell_exp = jnp.exp(cell_scores - row_top[..., None])
        tok_exp = jnp.exp(tok_scores - row_top[..., None])
        row_total = cell_exp.sum(-1) + tok_exp.sum(-1)
        mixed = jnp.einsum(
            "rhqk,rkhd->rqhd", cell_exp.astype(jnp.bfloat16), v4, preferred_element_type=jnp.float32
        )
        return mixed, tok_exp.astype(jnp.bfloat16), row_total

    def output_stage(state):
        mixed, tok_weights, row_total = state
        mixed = mixed + jnp.einsum(
            "rhqk,khd->rqhd", tok_weights, sv, preferred_element_type=jnp.float32
        )
        attended = mixed / row_total.transpose(0, 2, 1)[..., None]
        return attended.reshape(row_count * cols_dev, model_width).astype(jnp.bfloat16)

    merged, attended = all_merge(
        (part_mixed, part_total, part_top), "band", n_band,
        [None, scores_stage, weights_stage, output_stage],
        [got for _, got in row_parts],
    )
    col_top = jnp.maximum(merged[2], self_scores)
    fade = jnp.exp(merged[2] - col_top)
    self_exp = jnp.exp(self_scores - col_top)
    col_total = merged[1] * fade + self_exp
    col_mixed = merged[0] * head_spread(fade) + head_spread(
        self_exp.astype(jnp.bfloat16).astype(jnp.float32)
    ) * sum_vals.astype(jnp.float32)
    summary_att = (col_mixed / head_spread(col_total)).astype(jnp.bfloat16)

    all_in = jnp.concatenate([flat_cells, tokens], axis=0)
    all_att = jnp.concatenate([attended, summary_att], axis=0)
    all_out = finish(all_in, all_att, w_out, gain_attn, w_up, w_down, gain_ffn)
    cells_out = all_out[: row_count * cols_dev].reshape(row_count, cols_dev, model_width)
    summary_out = all_out[row_count * cols_dev :]
    return (cells_out, summary_out)


def solution(mesh):
    in_specs = (
        P("band", "col", None),
        P("band", "col", None),
        P("col"),
        P("band", "col"),
        P(),
        P(),
        P(),
        P(),
        P(),
        P(),
    )
    out_specs = (P("band", "col", None), P("col", None))
    body = functools.partial(local, n_band=mesh.shape["band"], n_col=mesh.shape["col"])
    return jax.shard_map(body, mesh=mesh, in_specs=in_specs, out_specs=out_specs, check_vma=False)
```

```python
import functools

import jax
import jax.numpy as jnp
from jax import lax
from jax.sharding import PartitionSpec as P

HEADS = 12
HEAD_DIM = 64


def spread_2(value, axis, source):
    kept = jnp.where(lax.axis_index(axis) == source, value, 0).astype(value.dtype)
    return lax.psum(kept, axis)


def layer_norm(values, gain_vec):
    center = values - jnp.mean(values, -1, keepdims=True)
    spread = jnp.mean(center * center, -1, keepdims=True)
    return center * lax.rsqrt(spread + 1e-05) * gain_vec


def finish(tokens_in, attended, w_out, gain_attn, w_up, w_down, gain_ffn):
    mixed_out = jnp.dot(attended, w_out, preferred_element_type=jnp.float32)
    hidden = layer_norm(tokens_in.astype(jnp.float32) + mixed_out, gain_attn).astype(jnp.bfloat16)
    inner_act = jax.nn.gelu(jnp.dot(hidden, w_up, preferred_element_type=jnp.float32)).astype(
        jnp.bfloat16
    )
    outer_out = jnp.dot(inner_act, w_down, preferred_element_type=jnp.float32)
    return layer_norm(hidden.astype(jnp.float32) + outer_out, gain_ffn).astype(jnp.bfloat16)


def project(values, weight):
    return jnp.dot(values, weight, preferred_element_type=jnp.float32).astype(jnp.bfloat16)


def head_matrix():
    lanes = jnp.arange(HEADS * HEAD_DIM, dtype=jnp.int32) // HEAD_DIM
    return (lanes[None, :] == jnp.arange(HEADS, dtype=jnp.int32)[:, None]).astype(jnp.float32)


def head_sum(values):
    dims = values.shape[:-1]
    flat = values.reshape(-1, values.shape[-1])
    out = jnp.dot(flat, head_matrix().T, precision=lax.Precision.HIGHEST,
                  preferred_element_type=jnp.float32)
    return out.reshape(dims + (HEADS,))


def head_spread(values):
    dims = values.shape[:-1]
    flat = values.reshape(-1, HEADS)
    out = jnp.dot(flat, head_matrix(), precision=lax.Precision.HIGHEST,
                  preferred_element_type=jnp.float32)
    return out.reshape(dims + (HEADS * HEAD_DIM,))


def partner(value, axis, step, count):
    return lax.ppermute(value, axis, [(i, i ^ step) for i in range(count)])


def broadcast_from(value, axis, count, source):
    here = lax.axis_index(axis)
    step = 1
    while step < count:
        got = partner(value, axis, step, count)
        value = jnp.where(here // step == source // step, value, got)
        step *= 2
    return value


def merge(lo, hi):
    top = jnp.maximum(lo[1][:, HEADS:], hi[1][:, HEADS:])
    fade_lo = jnp.exp(lo[1][:, HEADS:] - top)
    fade_hi = jnp.exp(hi[1][:, HEADS:] - top)
    total = lo[1][:, :HEADS] * fade_lo + hi[1][:, :HEADS] * fade_hi
    mixed = lo[0] * head_spread(fade_lo) + hi[0] * head_spread(fade_hi)
    return mixed, jnp.concatenate([total, top], axis=-1)


def pick(flag, a, b):
    return tuple(jnp.where(flag, x, y) for x, y in zip(a, b))


def half_merge(value, axis, count):
    here = lax.axis_index(axis)
    half = value[0].shape[0] // 2
    first = (here & 1) == 0
    top_half = tuple(v[:half] for v in value)
    low_half = tuple(v[half:] for v in value)
    mine = pick(first, top_half, low_half)
    sent = pick(first, low_half, top_half)
    got = tuple(partner(v, axis, 1, count) for v in sent)
    value = merge(pick(first, mine, got), pick(first, got, mine))
    step = 2
    while step < count:
        mixed = value[0].astype(jnp.bfloat16)
        got = (
            partner(mixed, axis, step, count).astype(jnp.float32),
            partner(value[1], axis, step, count),
        )
        mine = (mixed.astype(jnp.float32), value[1])
        low_side = (here & step) == 0
        value = merge(pick(low_side, mine, got), pick(low_side, got, mine))
        step *= 2
    return value


def join_halves(value, axis, count):
    first = (lax.axis_index(axis) & 1) == 0
    got = partner(value, axis, 1, count)
    return jnp.where(first, jnp.concatenate([value, got]), jnp.concatenate([got, value]))


def fan_out(value, axis, count):
    here = lax.axis_index(axis)
    got = []
    for step in range(1, count):
        if count & (count - 1) == 0:
            pairs = [(i, i ^ step) for i in range(count)]
            source = here ^ step
        else:
            pairs = [(i, (i + step) % count) for i in range(count)]
            source = (here - step) % count
        got.append((source, lax.ppermute(value, axis, pairs)))
    return got


def local(cells, summary, owner, schema, w_qkv, w_out, gain_attn, w_up, w_down, gain_ffn, *, n_band, n_col):
    row_count, cols_dev, model_width = cells.shape
    own_group = lax.axis_index("col")
    own_band = lax.axis_index("band")
    score_scale = HEAD_DIM ** (-0.5)
    flat_cells = cells.reshape(row_count * cols_dev, model_width)
    w_kv = w_qkv[:, model_width:]

    tokens = broadcast_from(summary[0], "band", n_band, owner[0])
    row_parts = fan_out(cells, "col", n_col)

    qkv_cells = project(flat_cells, w_qkv).reshape(row_count, cols_dev, 3 * model_width)
    queries = qkv_cells[:, :, :model_width]
    own_keys = qkv_cells[:, :, model_width : 2 * model_width]
    own_vals = qkv_cells[:, :, 2 * model_width :]

    summary_qkv = project(tokens, w_qkv)
    sum_queries = summary_qkv[:, :model_width]
    sum_keys = summary_qkv[:, model_width : 2 * model_width]
    sum_vals = summary_qkv[:, 2 * model_width :]

    sq = sum_queries.astype(jnp.float32)
    col_scores = head_sum(sq[None] * own_keys.astype(jnp.float32)) * score_scale
    self_scores = head_sum(sq * sum_keys.astype(jnp.float32)) * score_scale
    part_top = col_scores.max(0)
    col_exp = jnp.exp(col_scores - part_top[None])
    col_weights = head_spread(col_exp.astype(jnp.bfloat16).astype(jnp.float32))
    part_mixed = (col_weights * own_vals.astype(jnp.float32)).sum(0)
    part_total = col_exp.sum(0)
    merged = half_merge(
        (part_mixed, jnp.concatenate([part_total, part_top], axis=-1)), "band", n_band
    )
    half = cols_dev // 2
    first = (own_band & 1) == 0
    half_self = jnp.where(first, self_scores[:half], self_scores[half:])
    half_vals = jnp.where(first, sum_vals[:half], sum_vals[half:]).astype(jnp.float32)
    col_top = jnp.maximum(merged[1][:, HEADS:], half_self)
    fade = jnp.exp(merged[1][:, HEADS:] - col_top)
    self_exp = jnp.exp(half_self - col_top)
    col_total = merged[1][:, :HEADS] * fade + self_exp
    col_mixed = merged[0] * head_spread(fade) + head_spread(
        self_exp.astype(jnp.bfloat16).astype(jnp.float32)
    ) * half_vals
    summary_att = (col_mixed / head_spread(col_total)).astype(jnp.bfloat16)
    summary_att = join_halves(summary_att, "band", n_band)

    sources = [own_group] + [s for s, _ in row_parts]
    other_cells = jnp.concatenate([got for _, got in row_parts], axis=1)
    width_other = other_cells.shape[1]
    other_kv = project(other_cells.reshape(row_count * width_other, model_width), w_kv)
    other_kv = other_kv.reshape(row_count, width_other, 2 * model_width)
    row_keys = jnp.concatenate([own_keys, other_kv[:, :, :model_width]], axis=1)
    row_vals = jnp.concatenate([own_vals, other_kv[:, :, model_width:]], axis=1)
    width_now = row_keys.shape[1]
    q4 = queries.reshape(row_count, cols_dev, HEADS, HEAD_DIM)
    k4 = row_keys.reshape(row_count, width_now, HEADS, HEAD_DIM)
    v4 = row_vals.reshape(row_count, width_now, HEADS, HEAD_DIM)
    sk = sum_keys.reshape(cols_dev, HEADS, HEAD_DIM)
    sv = sum_vals.reshape(cols_dev, HEADS, HEAD_DIM)
    key_groups = jnp.concatenate(
        [jnp.full((cols_dev,), s, jnp.int32) for s in sources]
    )
    own_block = jnp.arange(width_now, dtype=jnp.int32) < cols_dev
    allowed = (jnp.right_shift(schema[:, :, None], key_groups[None, None, :]) & 1 == 1) | own_block[
        None, None, :
    ]
    cell_scores = (
        jnp.einsum("rqhd,rkhd->rhqk", q4, k4, preferred_element_type=jnp.float32) * score_scale
    )
    cell_scores = jnp.where(allowed[:, None], cell_scores, -1e30)
    tok_scores = (
        jnp.einsum("rqhd,khd->rhqk", q4, sk, preferred_element_type=jnp.float32) * score_scale
    )
    row_top = jnp.maximum(cell_scores.max(-1), tok_scores.max(-1))
    cell_exp = jnp.exp(cell_scores - row_top[..., None])
    tok_exp = jnp.exp(tok_scores - row_top[..., None])
    row_total = cell_exp.sum(-1) + tok_exp.sum(-1)
    mixed = jnp.einsum(
        "rhqk,rkhd->rqhd", cell_exp.astype(jnp.bfloat16), v4, preferred_element_type=jnp.float32
    )
    mixed = mixed + jnp.einsum(
        "rhqk,khd->rqhd", tok_exp.astype(jnp.bfloat16), sv, preferred_element_type=jnp.float32
    )
    attended = mixed / row_total.transpose(0, 2, 1)[..., None]
    attended = attended.reshape(row_count * cols_dev, model_width).astype(jnp.bfloat16)

    all_in = jnp.concatenate([flat_cells, tokens], axis=0)
    all_att = jnp.concatenate([attended, summary_att], axis=0)
    all_out = finish(all_in, all_att, w_out, gain_attn, w_up, w_down, gain_ffn)
    cells_out = all_out[: row_count * cols_dev].reshape(row_count, cols_dev, model_width)
    summary_out = all_out[row_count * cols_dev :]
    return (cells_out, summary_out)


def solution(mesh):
    in_specs = (
        P("band", "col", None),
        P("band", "col", None),
        P("col"),
        P("band", "col"),
        P(),
        P(),
        P(),
        P(),
        P(),
        P(),
    )
    out_specs = (P("band", "col", None), P("col", None))
    body = functools.partial(local, n_band=mesh.shape["band"], n_col=mesh.shape["col"])
    return jax.shard_map(body, mesh=mesh, in_specs=in_specs, out_specs=out_specs, check_vma=False)
```

```python
import functools

import jax
import jax.numpy as jnp
from jax import lax
from jax.sharding import PartitionSpec as P

HEADS = 12
HEAD_DIM = 64


def spread_2(value, axis, source):
    kept = jnp.where(lax.axis_index(axis) == source, value, 0).astype(value.dtype)
    return lax.psum(kept, axis)


def layer_norm(values, gain_vec):
    center = values - jnp.mean(values, -1, keepdims=True)
    spread = jnp.mean(center * center, -1, keepdims=True)
    return center * lax.rsqrt(spread + 1e-05) * gain_vec


def finish(tokens_in, attended, w_out, gain_attn, w_up, w_down, gain_ffn):
    mixed_out = jnp.dot(attended, w_out, preferred_element_type=jnp.float32)
    hidden = layer_norm(tokens_in.astype(jnp.float32) + mixed_out, gain_attn).astype(jnp.bfloat16)
    inner_act = jax.nn.gelu(jnp.dot(hidden, w_up, preferred_element_type=jnp.float32)).astype(
        jnp.bfloat16
    )
    outer_out = jnp.dot(inner_act, w_down, preferred_element_type=jnp.float32)
    return layer_norm(hidden.astype(jnp.float32) + outer_out, gain_ffn).astype(jnp.bfloat16)


def project(values, weight):
    return jnp.dot(values, weight, preferred_element_type=jnp.float32).astype(jnp.bfloat16)


def head_matrix():
    lanes = jnp.arange(HEADS * HEAD_DIM, dtype=jnp.int32) // HEAD_DIM
    return (lanes[None, :] == jnp.arange(HEADS, dtype=jnp.int32)[:, None]).astype(jnp.float32)


def head_sum(values):
    dims = values.shape[:-1]
    flat = values.reshape(-1, values.shape[-1])
    out = jnp.dot(flat, head_matrix().T, precision=lax.Precision.HIGHEST,
                  preferred_element_type=jnp.float32)
    return out.reshape(dims + (HEADS,))


def head_spread(values):
    dims = values.shape[:-1]
    flat = values.reshape(-1, HEADS)
    out = jnp.dot(flat, head_matrix(), precision=lax.Precision.HIGHEST,
                  preferred_element_type=jnp.float32)
    return out.reshape(dims + (HEADS * HEAD_DIM,))


def partner(value, axis, step, count):
    return lax.ppermute(value, axis, [(i, i ^ step) for i in range(count)])


def broadcast_from(value, axis, count, source, held):
    here = lax.axis_index(axis)
    step = 1
    while step < count:
        got = partner(value, axis, step, count)
        if step == 1:
            got, held = lax.optimization_barrier((got, held))
        value = jnp.where(here // step == source // step, value, got)
        step *= 2
    return value, held


def merge(lo, hi):
    top = jnp.maximum(lo[1][:, HEADS:], hi[1][:, HEADS:])
    fade_lo = jnp.exp(lo[1][:, HEADS:] - top)
    fade_hi = jnp.exp(hi[1][:, HEADS:] - top)
    total = lo[1][:, :HEADS] * fade_lo + hi[1][:, :HEADS] * fade_hi
    mixed = lo[0] * head_spread(fade_lo) + hi[0] * head_spread(fade_hi)
    return mixed, jnp.concatenate([total, top], axis=-1)


def pick(flag, a, b):
    return tuple(jnp.where(flag, x, y) for x, y in zip(a, b))


def half_merge(value, axis, count):
    here = lax.axis_index(axis)
    half = value[0].shape[0] // 2
    first = (here & 1) == 0
    top_half = tuple(v[:half] for v in value)
    low_half = tuple(v[half:] for v in value)
    mine = pick(first, top_half, low_half)
    sent = pick(first, low_half, top_half)
    got = tuple(partner(v, axis, 1, count) for v in sent)
    value = merge(pick(first, mine, got), pick(first, got, mine))
    step = 2
    while step < count:
        mixed = value[0].astype(jnp.bfloat16)
        got = (
            partner(mixed, axis, step, count).astype(jnp.float32),
            partner(value[1], axis, step, count),
        )
        mine = (mixed.astype(jnp.float32), value[1])
        low_side = (here & step) == 0
        value = merge(pick(low_side, mine, got), pick(low_side, got, mine))
        step *= 2
    return value


def join_halves(value, axis, count):
    first = (lax.axis_index(axis) & 1) == 0
    got = partner(value, axis, 1, count)
    return jnp.where(first, jnp.concatenate([value, got]), jnp.concatenate([got, value]))


def fan_out(value, axis, count):
    here = lax.axis_index(axis)
    got = []
    for step in range(1, count):
        if count & (count - 1) == 0:
            pairs = [(i, i ^ step) for i in range(count)]
            source = here ^ step
        else:
            pairs = [(i, (i + step) % count) for i in range(count)]
            source = (here - step) % count
        got.append((source, lax.ppermute(value, axis, pairs)))
    return got


def local(cells, summary, owner, schema, w_qkv, w_out, gain_attn, w_up, w_down, gain_ffn, *, n_band, n_col):
    row_count, cols_dev, model_width = cells.shape
    own_group = lax.axis_index("col")
    own_band = lax.axis_index("band")
    score_scale = HEAD_DIM ** (-0.5)
    flat_cells = cells.reshape(row_count * cols_dev, model_width)
    w_kv = w_qkv[:, model_width:]

    tokens = broadcast_from(summary[0], "band", n_band, owner[0], cells)
    row_parts = fan_out(tokens[1], "col", n_col)
    tokens = tokens[0]

    qkv_cells = project(flat_cells, w_qkv).reshape(row_count, cols_dev, 3 * model_width)
    queries = qkv_cells[:, :, :model_width]
    own_keys = qkv_cells[:, :, model_width : 2 * model_width]
    own_vals = qkv_cells[:, :, 2 * model_width :]

    sum_queries = project(tokens, w_qkv[:, :model_width])
    summary_kv = project(tokens, w_kv)
    sum_keys = summary_kv[:, :model_width]
    sum_vals = summary_kv[:, model_width:]

    sq = sum_queries.astype(jnp.float32)
    col_scores = head_sum(sq[None] * own_keys.astype(jnp.float32)) * score_scale
    self_scores = head_sum(sq * sum_keys.astype(jnp.float32)) * score_scale
    part_top = col_scores.max(0)
    col_exp = jnp.exp(col_scores - part_top[None])
    col_weights = head_spread(col_exp.astype(jnp.bfloat16).astype(jnp.float32))
    part_mixed = (col_weights * own_vals.astype(jnp.float32)).sum(0)
    part_total = col_exp.sum(0)
    merged = half_merge(
        (part_mixed, jnp.concatenate([part_total, part_top], axis=-1)), "band", n_band
    )
    half = cols_dev // 2
    first = (own_band & 1) == 0
    half_self = jnp.where(first, self_scores[:half], self_scores[half:])
    half_vals = jnp.where(first, sum_vals[:half], sum_vals[half:]).astype(jnp.float32)
    col_top = jnp.maximum(merged[1][:, HEADS:], half_self)
    fade = jnp.exp(merged[1][:, HEADS:] - col_top)
    self_exp = jnp.exp(half_self - col_top)
    col_total = merged[1][:, :HEADS] * fade + self_exp
    col_mixed = merged[0] * head_spread(fade) + head_spread(
        self_exp.astype(jnp.bfloat16).astype(jnp.float32)
    ) * half_vals
    summary_att = (col_mixed / head_spread(col_total)).astype(jnp.bfloat16)
    summary_att = join_halves(summary_att, "band", n_band)

    sources = [own_group] + [s for s, _ in row_parts]
    other_cells = jnp.concatenate([got for _, got in row_parts], axis=1)
    width_other = other_cells.shape[1]
    other_kv = project(other_cells.reshape(row_count * width_other, model_width), w_kv)
    other_kv = other_kv.reshape(row_count, width_other, 2 * model_width)
    row_keys = jnp.concatenate([own_keys, other_kv[:, :, :model_width]], axis=1)
    row_vals = jnp.concatenate([own_vals, other_kv[:, :, model_width:]], axis=1)
    width_now = row_keys.shape[1]
    q4 = queries.reshape(row_count, cols_dev, HEADS, HEAD_DIM)
    k4 = row_keys.reshape(row_count, width_now, HEADS, HEAD_DIM)
    v4 = row_vals.reshape(row_count, width_now, HEADS, HEAD_DIM)
    sk = sum_keys.reshape(cols_dev, HEADS, HEAD_DIM)
    sv = sum_vals.reshape(cols_dev, HEADS, HEAD_DIM)
    key_groups = jnp.concatenate(
        [jnp.full((cols_dev,), s, jnp.int32) for s in sources]
    )
    own_block = jnp.arange(width_now, dtype=jnp.int32) < cols_dev
    allowed = (jnp.right_shift(schema[:, :, None], key_groups[None, None, :]) & 1 == 1) | own_block[
        None, None, :
    ]
    cell_scores = (
        jnp.einsum("rqhd,rkhd->rhqk", q4, k4, preferred_element_type=jnp.float32) * score_scale
    )
    cell_scores = jnp.where(allowed[:, None], cell_scores, -1e30)
    tok_scores = (
        jnp.einsum("rqhd,khd->rhqk", q4, sk, preferred_element_type=jnp.float32) * score_scale
    )
    row_top = jnp.maximum(cell_scores.max(-1), tok_scores.max(-1))
    cell_exp = jnp.exp(cell_scores - row_top[..., None])
    tok_exp = jnp.exp(tok_scores - row_top[..., None])
    row_total = cell_exp.sum(-1) + tok_exp.sum(-1)
    mixed = jnp.einsum(
        "rhqk,rkhd->rqhd", cell_exp.astype(jnp.bfloat16), v4, preferred_element_type=jnp.float32
    )
    mixed = mixed + jnp.einsum(
        "rhqk,khd->rqhd", tok_exp.astype(jnp.bfloat16), sv, preferred_element_type=jnp.float32
    )
    attended = mixed / row_total.transpose(0, 2, 1)[..., None]
    attended = attended.reshape(row_count * cols_dev, model_width).astype(jnp.bfloat16)

    all_in = jnp.concatenate([flat_cells, tokens], axis=0)
    all_att = jnp.concatenate([attended, summary_att], axis=0)
    all_out = finish(all_in, all_att, w_out, gain_attn, w_up, w_down, gain_ffn)
    cells_out = all_out[: row_count * cols_dev].reshape(row_count, cols_dev, model_width)
    summary_out = all_out[row_count * cols_dev :]
    return (cells_out, summary_out)


def solution(mesh):
    in_specs = (
        P("band", "col", None),
        P("band", "col", None),
        P("col"),
        P("band", "col"),
        P(),
        P(),
        P(),
        P(),
        P(),
        P(),
    )
    out_specs = (P("band", "col", None), P("col", None))
    body = functools.partial(local, n_band=mesh.shape["band"], n_col=mesh.shape["col"])
    return jax.shard_map(body, mesh=mesh, in_specs=in_specs, out_specs=out_specs, check_vma=False)
```

```python
import functools

import jax
import jax.numpy as jnp
from jax import lax
from jax.sharding import PartitionSpec as P

HEADS = 12
HEAD_DIM = 64


def spread_2(value, axis, source):
    kept = jnp.where(lax.axis_index(axis) == source, value, 0).astype(value.dtype)
    return lax.psum(kept, axis)


def layer_norm(values, gain_vec):
    center = values - jnp.mean(values, -1, keepdims=True)
    spread = jnp.mean(center * center, -1, keepdims=True)
    return center * lax.rsqrt(spread + 1e-05) * gain_vec


def finish(tokens_in, attended, w_out, gain_attn, w_up, w_down, gain_ffn):
    mixed_out = jnp.dot(attended, w_out, preferred_element_type=jnp.float32)
    hidden = layer_norm(tokens_in.astype(jnp.float32) + mixed_out, gain_attn).astype(jnp.bfloat16)
    inner_act = jax.nn.gelu(jnp.dot(hidden, w_up, preferred_element_type=jnp.float32)).astype(
        jnp.bfloat16
    )
    outer_out = jnp.dot(inner_act, w_down, preferred_element_type=jnp.float32)
    return layer_norm(hidden.astype(jnp.float32) + outer_out, gain_ffn).astype(jnp.bfloat16)


def project(values, weight):
    return jnp.dot(values, weight, preferred_element_type=jnp.float32).astype(jnp.bfloat16)


def head_matrix():
    lanes = jnp.arange(HEADS * HEAD_DIM, dtype=jnp.int32) // HEAD_DIM
    return (lanes[None, :] == jnp.arange(HEADS, dtype=jnp.int32)[:, None]).astype(jnp.float32)


def head_sum(values):
    dims = values.shape[:-1]
    flat = values.reshape(-1, values.shape[-1])
    out = jnp.dot(flat, head_matrix().T, precision=lax.Precision.HIGHEST,
                  preferred_element_type=jnp.float32)
    return out.reshape(dims + (HEADS,))


def head_spread(values):
    dims = values.shape[:-1]
    flat = values.reshape(-1, HEADS)
    out = jnp.dot(flat, head_matrix(), precision=lax.Precision.HIGHEST,
                  preferred_element_type=jnp.float32)
    return out.reshape(dims + (HEADS * HEAD_DIM,))


def partner(value, axis, step, count):
    return lax.ppermute(value, axis, [(i, i ^ step) for i in range(count)])


def broadcast_from(value, axis, count, source, held):
    here = lax.axis_index(axis)
    step = 1
    while step < count:
        got = partner(value, axis, step, count)
        if step == 1:
            got, held = lax.optimization_barrier((got, held))
        value = jnp.where(here // step == source // step, value, got)
        step *= 2
    return value, held


def merge(lo, hi):
    top = jnp.maximum(lo[1][:, HEADS:], hi[1][:, HEADS:])
    fade_lo = jnp.exp(lo[1][:, HEADS:] - top)
    fade_hi = jnp.exp(hi[1][:, HEADS:] - top)
    total = lo[1][:, :HEADS] * fade_lo + hi[1][:, :HEADS] * fade_hi
    mixed = lo[0] * head_spread(fade_lo) + hi[0] * head_spread(fade_hi)
    return mixed, jnp.concatenate([total, top], axis=-1)


def pick(flag, a, b):
    return tuple(jnp.where(flag, x, y) for x, y in zip(a, b))


def half_merge(value, axis, count):
    here = lax.axis_index(axis)
    half = value[0].shape[0] // 2
    first = (here & 1) == 0
    top_half = tuple(v[:half] for v in value)
    low_half = tuple(v[half:] for v in value)
    mine = pick(first, top_half, low_half)
    sent = pick(first, low_half, top_half)
    got = tuple(partner(v, axis, 1, count) for v in sent)
    value = merge(pick(first, mine, got), pick(first, got, mine))
    step = 2
    while step < count:
        mixed = value[0].astype(jnp.bfloat16)
        got = (
            partner(mixed, axis, step, count).astype(jnp.float32),
            partner(value[1], axis, step, count),
        )
        mine = (mixed.astype(jnp.float32), value[1])
        low_side = (here & step) == 0
        value = merge(pick(low_side, mine, got), pick(low_side, got, mine))
        step *= 2
    return value


def join_halves(value, axis, count):
    first = (lax.axis_index(axis) & 1) == 0
    got = partner(value, axis, 1, count)
    return jnp.where(first, jnp.concatenate([value, got]), jnp.concatenate([got, value]))


def fan_out(value, axis, count):
    here = lax.axis_index(axis)
    got = []
    for step in range(1, count):
        if count & (count - 1) == 0:
            pairs = [(i, i ^ step) for i in range(count)]
            source = here ^ step
        else:
            pairs = [(i, (i + step) % count) for i in range(count)]
            source = (here - step) % count
        got.append((source, lax.ppermute(value, axis, pairs)))
    return got


def local(cells, summary, owner, schema, w_qkv, w_out, gain_attn, w_up, w_down, gain_ffn, *, n_band, n_col):
    row_count, cols_dev, model_width = cells.shape
    own_group = lax.axis_index("col")
    own_band = lax.axis_index("band")
    score_scale = HEAD_DIM ** (-0.5)
    flat_cells = cells.reshape(row_count * cols_dev, model_width)
    w_kv = w_qkv[:, model_width:]

    tokens = broadcast_from(summary[0], "band", n_band, owner[0], cells)
    row_parts = fan_out(tokens[1], "col", n_col)
    tokens = tokens[0]

    qkv_cells = project(flat_cells, w_qkv).reshape(row_count, cols_dev, 3 * model_width)
    queries = qkv_cells[:, :, :model_width]
    own_keys = qkv_cells[:, :, model_width : 2 * model_width]
    own_vals = qkv_cells[:, :, 2 * model_width :]

    sum_queries = project(tokens, w_qkv[:, :model_width])
    summary_kv = project(tokens, w_kv)
    sum_keys = summary_kv[:, :model_width]
    sum_vals = summary_kv[:, model_width:]

    sq = sum_queries.astype(jnp.float32)
    col_scores = head_sum(sq[None] * own_keys.astype(jnp.float32)) * score_scale
    self_scores = head_sum(sq * sum_keys.astype(jnp.float32)) * score_scale
    part_top = col_scores.max(0)
    col_exp = jnp.exp(col_scores - part_top[None])
    col_weights = head_spread(col_exp.astype(jnp.bfloat16).astype(jnp.float32))
    part_mixed = (col_weights * own_vals.astype(jnp.float32)).sum(0)
    part_total = col_exp.sum(0)
    merged = half_merge(
        (part_mixed, jnp.concatenate([part_total, part_top], axis=-1)), "band", n_band
    )
    half = cols_dev // 2
    first = (own_band & 1) == 0
    half_self = jnp.where(first, self_scores[:half], self_scores[half:])
    half_vals = jnp.where(first, sum_vals[:half], sum_vals[half:]).astype(jnp.float32)
    col_top = jnp.maximum(merged[1][:, HEADS:], half_self)
    fade = jnp.exp(merged[1][:, HEADS:] - col_top)
    self_exp = jnp.exp(half_self - col_top)
    col_total = merged[1][:, :HEADS] * fade + self_exp
    col_mixed = merged[0] * head_spread(fade) + head_spread(
        self_exp.astype(jnp.bfloat16).astype(jnp.float32)
    ) * half_vals
    summary_att = (col_mixed / head_spread(col_total)).astype(jnp.bfloat16)
    summary_att = join_halves(summary_att, "band", n_band)

    sources = [own_group] + [s for s, _ in row_parts]
    row_cells = jnp.concatenate([cells] + [got for _, got in row_parts], axis=1)
    width_now = row_cells.shape[1]
    keys_t = jnp.einsum(
        "ic,rki->rck", w_qkv[:, model_width : 2 * model_width], row_cells,
        preferred_element_type=jnp.float32,
    ).astype(jnp.bfloat16)
    vals_t = jnp.einsum(
        "ic,rki->rck", w_qkv[:, 2 * model_width :], row_cells,
        preferred_element_type=jnp.float32,
    ).astype(jnp.bfloat16)
    q4 = queries.reshape(row_count, cols_dev, HEADS, HEAD_DIM)
    k4 = keys_t.reshape(row_count, HEADS, HEAD_DIM, width_now)
    v4 = vals_t.reshape(row_count, HEADS, HEAD_DIM, width_now)
    sk = sum_keys.reshape(cols_dev, HEADS, HEAD_DIM)
    sv = sum_vals.reshape(cols_dev, HEADS, HEAD_DIM)
    key_groups = jnp.concatenate(
        [jnp.full((cols_dev,), s, jnp.int32) for s in sources]
    )
    own_block = jnp.arange(width_now, dtype=jnp.int32) < cols_dev
    allowed = (jnp.right_shift(schema[:, :, None], key_groups[None, None, :]) & 1 == 1) | own_block[
        None, None, :
    ]
    cell_scores = (
        jnp.einsum("rqhd,rhdk->rhqk", q4, k4, preferred_element_type=jnp.float32) * score_scale
    )
    cell_scores = jnp.where(allowed[:, None], cell_scores, -1e30)
    tok_scores = (
        jnp.einsum("rqhd,khd->rhqk", q4, sk, preferred_element_type=jnp.float32) * score_scale
    )
    row_top = jnp.maximum(cell_scores.max(-1), tok_scores.max(-1))
    cell_exp = jnp.exp(cell_scores - row_top[..., None])
    tok_exp = jnp.exp(tok_scores - row_top[..., None])
    row_total = cell_exp.sum(-1) + tok_exp.sum(-1)
    mixed = jnp.einsum(
        "rhqk,rhdk->rqhd", cell_exp.astype(jnp.bfloat16), v4, preferred_element_type=jnp.float32
    )
    mixed = mixed + jnp.einsum(
        "rhqk,khd->rqhd", tok_exp.astype(jnp.bfloat16), sv, preferred_element_type=jnp.float32
    )
    attended = mixed / row_total.transpose(0, 2, 1)[..., None]
    attended = attended.reshape(row_count * cols_dev, model_width).astype(jnp.bfloat16)

    all_in = jnp.concatenate([flat_cells, tokens], axis=0)
    all_att = jnp.concatenate([attended, summary_att], axis=0)
    all_out = finish(all_in, all_att, w_out, gain_attn, w_up, w_down, gain_ffn)
    cells_out = all_out[: row_count * cols_dev].reshape(row_count, cols_dev, model_width)
    summary_out = all_out[row_count * cols_dev :]
    return (cells_out, summary_out)


def solution(mesh):
    in_specs = (
        P("band", "col", None),
        P("band", "col", None),
        P("col"),
        P("band", "col"),
        P(),
        P(),
        P(),
        P(),
        P(),
        P(),
    )
    out_specs = (P("band", "col", None), P("col", None))
    body = functools.partial(local, n_band=mesh.shape["band"], n_col=mesh.shape["col"])
    return jax.shard_map(body, mesh=mesh, in_specs=in_specs, out_specs=out_specs, check_vma=False)
```

```python
import functools

import jax
import jax.numpy as jnp
from jax import lax
from jax.sharding import PartitionSpec as P

HEADS = 12
HEAD_DIM = 64


def spread_2(value, axis, source):
    kept = jnp.where(lax.axis_index(axis) == source, value, 0).astype(value.dtype)
    return lax.psum(kept, axis)


def layer_norm(values, gain_vec):
    center = values - jnp.mean(values, -1, keepdims=True)
    spread = jnp.mean(center * center, -1, keepdims=True)
    return center * lax.rsqrt(spread + 1e-05) * gain_vec


def finish(tokens_in, attended, w_out, gain_attn, w_up, w_down, gain_ffn):
    mixed_out = jnp.dot(attended, w_out, preferred_element_type=jnp.float32)
    hidden = layer_norm(tokens_in.astype(jnp.float32) + mixed_out, gain_attn).astype(jnp.bfloat16)
    inner_act = jax.nn.gelu(jnp.dot(hidden, w_up, preferred_element_type=jnp.float32)).astype(
        jnp.bfloat16
    )
    outer_out = jnp.dot(inner_act, w_down, preferred_element_type=jnp.float32)
    return layer_norm(hidden.astype(jnp.float32) + outer_out, gain_ffn).astype(jnp.bfloat16)


def project(values, weight):
    return jnp.dot(values, weight, preferred_element_type=jnp.float32).astype(jnp.bfloat16)


def head_matrix():
    lanes = jnp.arange(HEADS * HEAD_DIM, dtype=jnp.int32) // HEAD_DIM
    return (lanes[None, :] == jnp.arange(HEADS, dtype=jnp.int32)[:, None]).astype(jnp.float32)


def head_sum(values):
    dims = values.shape[:-1]
    flat = values.reshape(-1, values.shape[-1])
    out = jnp.dot(flat, head_matrix().T, precision=lax.Precision.HIGHEST,
                  preferred_element_type=jnp.float32)
    return out.reshape(dims + (HEADS,))


def head_spread(values):
    dims = values.shape[:-1]
    flat = values.reshape(-1, HEADS)
    out = jnp.dot(flat, head_matrix(), precision=lax.Precision.HIGHEST,
                  preferred_element_type=jnp.float32)
    return out.reshape(dims + (HEADS * HEAD_DIM,))


def partner(value, axis, step, count):
    return lax.ppermute(value, axis, [(i, i ^ step) for i in range(count)])


def broadcast_from(value, axis, count, source, held):
    here = lax.axis_index(axis)
    got = partner(value, axis, 1, count)
    got, held = lax.optimization_barrier((got, held))
    value = jnp.where(here == source, value, got)
    chip = here // 2
    result = value
    for step in range(1, count // 2):
        got = partner(value, axis, 2 * step, count)
        result = jnp.where((chip ^ step) == source // 2, got, result)
    return result, held


def merge(lo, hi):
    top = jnp.maximum(lo[1][:, HEADS:], hi[1][:, HEADS:])
    fade_lo = jnp.exp(lo[1][:, HEADS:] - top)
    fade_hi = jnp.exp(hi[1][:, HEADS:] - top)
    total = lo[1][:, :HEADS] * fade_lo + hi[1][:, :HEADS] * fade_hi
    mixed = lo[0] * head_spread(fade_lo) + hi[0] * head_spread(fade_hi)
    return mixed, jnp.concatenate([total, top], axis=-1)


def pick(flag, a, b):
    return tuple(jnp.where(flag, x, y) for x, y in zip(a, b))


def half_merge(value, axis, count):
    here = lax.axis_index(axis)
    half = value[0].shape[0] // 2
    first = (here & 1) == 0
    top_half = tuple(v[:half] for v in value)
    low_half = tuple(v[half:] for v in value)
    mine = pick(first, top_half, low_half)
    sent = pick(first, low_half, top_half)
    got = tuple(partner(v, axis, 1, count) for v in sent)
    value = merge(pick(first, mine, got), pick(first, got, mine))
    chip = here // 2
    mine = (value[0].astype(jnp.bfloat16).astype(jnp.float32), value[1])
    got = []
    for step in range(1, count // 2):
        got.append((
            partner(value[0].astype(jnp.bfloat16), axis, 2 * step, count).astype(jnp.float32),
            partner(value[1], axis, 2 * step, count),
        ))
    parts = []
    for c in range(count // 2):
        part = mine
        for step in range(1, count // 2):
            part = pick((chip ^ step) == c, got[step - 1], part)
        parts.append(part)
    while len(parts) > 1:
        parts = [merge(parts[i], parts[i + 1]) for i in range(0, len(parts), 2)]
    return parts[0]


def join_halves(value, axis, count):
    first = (lax.axis_index(axis) & 1) == 0
    got = partner(value, axis, 1, count)
    return jnp.where(first, jnp.concatenate([value, got]), jnp.concatenate([got, value]))


def fan_out(value, axis, count):
    here = lax.axis_index(axis)
    got = []
    for step in range(1, count):
        if count & (count - 1) == 0:
            pairs = [(i, i ^ step) for i in range(count)]
            source = here ^ step
        else:
            pairs = [(i, (i + step) % count) for i in range(count)]
            source = (here - step) % count
        got.append((source, lax.ppermute(value, axis, pairs)))
    return got


def local(cells, summary, owner, schema, w_qkv, w_out, gain_attn, w_up, w_down, gain_ffn, *, n_band, n_col):
    row_count, cols_dev, model_width = cells.shape
    own_group = lax.axis_index("col")
    own_band = lax.axis_index("band")
    score_scale = HEAD_DIM ** (-0.5)
    flat_cells = cells.reshape(row_count * cols_dev, model_width)
    w_kv = w_qkv[:, model_width:]

    tokens = broadcast_from(summary[0], "band", n_band, owner[0], cells)
    row_parts = fan_out(tokens[1], "col", n_col)
    tokens = tokens[0]

    qkv_cells = project(flat_cells, w_qkv).reshape(row_count, cols_dev, 3 * model_width)
    queries = qkv_cells[:, :, :model_width]
    own_keys = qkv_cells[:, :, model_width : 2 * model_width]
    own_vals = qkv_cells[:, :, 2 * model_width :]

    sum_queries = project(tokens, w_qkv[:, :model_width])
    summary_kv = project(tokens, w_kv)
    sum_keys = summary_kv[:, :model_width]
    sum_vals = summary_kv[:, model_width:]

    sq = sum_queries.astype(jnp.float32)
    col_scores = head_sum(sq[None] * own_keys.astype(jnp.float32)) * score_scale
    self_scores = head_sum(sq * sum_keys.astype(jnp.float32)) * score_scale
    part_top = col_scores.max(0)
    col_exp = jnp.exp(col_scores - part_top[None])
    col_weights = head_spread(col_exp.astype(jnp.bfloat16).astype(jnp.float32))
    part_mixed = (col_weights * own_vals.astype(jnp.float32)).sum(0)
    part_total = col_exp.sum(0)
    merged = half_merge(
        (part_mixed, jnp.concatenate([part_total, part_top], axis=-1)), "band", n_band
    )
    half = cols_dev // 2
    first = (own_band & 1) == 0
    half_self = jnp.where(first, self_scores[:half], self_scores[half:])
    half_vals = jnp.where(first, sum_vals[:half], sum_vals[half:]).astype(jnp.float32)
    col_top = jnp.maximum(merged[1][:, HEADS:], half_self)
    fade = jnp.exp(merged[1][:, HEADS:] - col_top)
    self_exp = jnp.exp(half_self - col_top)
    col_total = merged[1][:, :HEADS] * fade + self_exp
    col_mixed = merged[0] * head_spread(fade) + head_spread(
        self_exp.astype(jnp.bfloat16).astype(jnp.float32)
    ) * half_vals
    summary_att = (col_mixed / head_spread(col_total)).astype(jnp.bfloat16)
    summary_att = join_halves(summary_att, "band", n_band)

    sources = [own_group] + [s for s, _ in row_parts]
    other_cells = jnp.concatenate([got for _, got in row_parts], axis=1)
    width_other = other_cells.shape[1]
    other_kv = project(other_cells.reshape(row_count * width_other, model_width), w_kv)
    other_kv = other_kv.reshape(row_count, width_other, 2 * model_width)
    row_keys = jnp.concatenate([own_keys, other_kv[:, :, :model_width]], axis=1)
    row_vals = jnp.concatenate([own_vals, other_kv[:, :, model_width:]], axis=1)
    width_now = row_keys.shape[1]
    q4 = queries.reshape(row_count, cols_dev, HEADS, HEAD_DIM)
    k4 = row_keys.reshape(row_count, width_now, HEADS, HEAD_DIM)
    v4 = row_vals.reshape(row_count, width_now, HEADS, HEAD_DIM)
    sk = sum_keys.reshape(cols_dev, HEADS, HEAD_DIM)
    sv = sum_vals.reshape(cols_dev, HEADS, HEAD_DIM)
    key_groups = jnp.concatenate(
        [jnp.full((cols_dev,), s, jnp.int32) for s in sources]
    )
    own_block = jnp.arange(width_now, dtype=jnp.int32) < cols_dev
    allowed = (jnp.right_shift(schema[:, :, None], key_groups[None, None, :]) & 1 == 1) | own_block[
        None, None, :
    ]
    cell_scores = (
        jnp.einsum("rqhd,rkhd->rhqk", q4, k4, preferred_element_type=jnp.float32) * score_scale
    )
    cell_scores = jnp.where(allowed[:, None], cell_scores, -1e30)
    tok_scores = (
        jnp.einsum("rqhd,khd->rhqk", q4, sk, preferred_element_type=jnp.float32) * score_scale
    )
    row_top = jnp.maximum(cell_scores.max(-1), tok_scores.max(-1))
    cell_exp = jnp.exp(cell_scores - row_top[..., None])
    tok_exp = jnp.exp(tok_scores - row_top[..., None])
    row_total = cell_exp.sum(-1) + tok_exp.sum(-1)
    mixed = jnp.einsum(
        "rhqk,rkhd->rqhd", cell_exp.astype(jnp.bfloat16), v4, preferred_element_type=jnp.float32
    )
    mixed = mixed + jnp.einsum(
        "rhqk,khd->rqhd", tok_exp.astype(jnp.bfloat16), sv, preferred_element_type=jnp.float32
    )
    attended = mixed / row_total.transpose(0, 2, 1)[..., None]
    attended = attended.reshape(row_count * cols_dev, model_width).astype(jnp.bfloat16)

    all_in = jnp.concatenate([flat_cells, tokens], axis=0)
    all_att = jnp.concatenate([attended, summary_att], axis=0)
    all_out = finish(all_in, all_att, w_out, gain_attn, w_up, w_down, gain_ffn)
    cells_out = all_out[: row_count * cols_dev].reshape(row_count, cols_dev, model_width)
    summary_out = all_out[row_count * cols_dev :]
    return (cells_out, summary_out)


def solution(mesh):
    in_specs = (
        P("band", "col", None),
        P("band", "col", None),
        P("col"),
        P("band", "col"),
        P(),
        P(),
        P(),
        P(),
        P(),
        P(),
    )
    out_specs = (P("band", "col", None), P("col", None))
    body = functools.partial(local, n_band=mesh.shape["band"], n_col=mesh.shape["col"])
    return jax.shard_map(body, mesh=mesh, in_specs=in_specs, out_specs=out_specs, check_vma=False)
```

```python
import functools

import jax
import jax.numpy as jnp
from jax import lax
from jax.experimental import pallas as pl
from jax.sharding import PartitionSpec as P

HEADS = 12
HEAD_DIM = 64


def spread_2(value, axis, source):
    kept = jnp.where(lax.axis_index(axis) == source, value, 0).astype(value.dtype)
    return lax.psum(kept, axis)


def layer_norm(values, gain_vec):
    center = values - jnp.mean(values, -1, keepdims=True)
    spread = jnp.mean(center * center, -1, keepdims=True)
    return center * lax.rsqrt(spread + 1e-05) * gain_vec


def finish(tokens_in, attended, w_out, gain_attn, w_up, w_down, gain_ffn):
    mixed_out = jnp.dot(attended, w_out, preferred_element_type=jnp.float32)
    hidden = layer_norm(tokens_in.astype(jnp.float32) + mixed_out, gain_attn).astype(jnp.bfloat16)
    inner_act = jax.nn.gelu(jnp.dot(hidden, w_up, preferred_element_type=jnp.float32)).astype(
        jnp.bfloat16
    )
    outer_out = jnp.dot(inner_act, w_down, preferred_element_type=jnp.float32)
    return layer_norm(hidden.astype(jnp.float32) + outer_out, gain_ffn).astype(jnp.bfloat16)


def project(values, weight):
    return jnp.dot(values, weight, preferred_element_type=jnp.float32).astype(jnp.bfloat16)


def head_matrix():
    lanes = jnp.arange(HEADS * HEAD_DIM, dtype=jnp.int32) // HEAD_DIM
    return (lanes[None, :] == jnp.arange(HEADS, dtype=jnp.int32)[:, None]).astype(jnp.float32)


def head_sum(values):
    dims = values.shape[:-1]
    flat = values.reshape(-1, values.shape[-1])
    out = jnp.dot(flat, head_matrix().T, precision=lax.Precision.HIGHEST,
                  preferred_element_type=jnp.float32)
    return out.reshape(dims + (HEADS,))


def head_spread(values):
    dims = values.shape[:-1]
    flat = values.reshape(-1, HEADS)
    out = jnp.dot(flat, head_matrix(), precision=lax.Precision.HIGHEST,
                  preferred_element_type=jnp.float32)
    return out.reshape(dims + (HEADS * HEAD_DIM,))


def partner(value, axis, step, count):
    return lax.ppermute(value, axis, [(i, i ^ step) for i in range(count)])


def broadcast_from(value, axis, count, source, held):
    here = lax.axis_index(axis)
    step = 1
    while step < count:
        got = partner(value, axis, step, count)
        if step == 1:
            got, held = lax.optimization_barrier((got, held))
        value = jnp.where(here // step == source // step, value, got)
        step *= 2
    return value, held


def merge(lo, hi):
    top = jnp.maximum(lo[1][:, HEADS:], hi[1][:, HEADS:])
    fade_lo = jnp.exp(lo[1][:, HEADS:] - top)
    fade_hi = jnp.exp(hi[1][:, HEADS:] - top)
    total = lo[1][:, :HEADS] * fade_lo + hi[1][:, :HEADS] * fade_hi
    mixed = lo[0] * head_spread(fade_lo) + hi[0] * head_spread(fade_hi)
    return mixed, jnp.concatenate([total, top], axis=-1)


def pick(flag, a, b):
    return tuple(jnp.where(flag, x, y) for x, y in zip(a, b))


def half_merge(value, axis, count):
    here = lax.axis_index(axis)
    half = value[0].shape[0] // 2
    first = (here & 1) == 0
    top_half = tuple(v[:half] for v in value)
    low_half = tuple(v[half:] for v in value)
    mine = pick(first, top_half, low_half)
    sent = pick(first, low_half, top_half)
    got = tuple(partner(v, axis, 1, count) for v in sent)
    value = merge(pick(first, mine, got), pick(first, got, mine))
    step = 2
    while step < count:
        mixed = value[0].astype(jnp.bfloat16)
        got = (
            partner(mixed, axis, step, count).astype(jnp.float32),
            partner(value[1], axis, step, count),
        )
        mine = (mixed.astype(jnp.float32), value[1])
        low_side = (here & step) == 0
        value = merge(pick(low_side, mine, got), pick(low_side, got, mine))
        step *= 2
    return value


def join_halves(value, axis, count):
    first = (lax.axis_index(axis) & 1) == 0
    got = partner(value, axis, 1, count)
    return jnp.where(first, jnp.concatenate([value, got]), jnp.concatenate([got, value]))


def fan_out(value, axis, count):
    here = lax.axis_index(axis)
    got = []
    for step in range(1, count):
        if count & (count - 1) == 0:
            pairs = [(i, i ^ step) for i in range(count)]
            source = here ^ step
        else:
            pairs = [(i, (i + step) % count) for i in range(count)]
            source = (here - step) % count
        got.append((source, lax.ppermute(value, axis, pairs)))
    return got


def row_kernel(q_ref, k_ref, v_ref, sk_ref, sv_ref, allow_ref, o_ref, *, scale):
    allow = allow_ref[0] > 0.5
    lane = lax.broadcasted_iota(jnp.int32, (1, 2 * HEAD_DIM), 1)
    low = lane < HEAD_DIM
    nt = (((1,), (1,)), ((), ()))
    for pair in range(HEADS // 2):
        cols = slice(pair * 2 * HEAD_DIM, (pair + 1) * 2 * HEAD_DIM)
        q = q_ref[0, :, cols]
        k = k_ref[0, :, cols]
        v = v_ref[0, :, cols]
        sk = sk_ref[:, cols]
        sv = sv_ref[:, cols]
        outs = []
        for side in (low, jnp.logical_not(low)):
            qh = jnp.where(side, q, jnp.zeros_like(q))
            s = lax.dot_general(qh, k, nt, preferred_element_type=jnp.float32) * scale
            s = jnp.where(allow, s, -1e30)
            ts = lax.dot_general(qh, sk, nt, preferred_element_type=jnp.float32) * scale
            top = jnp.maximum(s.max(-1, keepdims=True), ts.max(-1, keepdims=True))
            e = jnp.exp(s - top)
            te = jnp.exp(ts - top)
            tot = e.sum(-1, keepdims=True) + te.sum(-1, keepdims=True)
            acc = jnp.dot(e.astype(jnp.bfloat16), v, preferred_element_type=jnp.float32)
            acc = acc + jnp.dot(te.astype(jnp.bfloat16), sv, preferred_element_type=jnp.float32)
            outs.append(acc / tot)
        o_ref[0, :, cols] = jnp.where(low, outs[0], outs[1]).astype(o_ref.dtype)


def row_attention(q, k, v, sk, sv, allow):
    rows, nq, width = q.shape
    nk = k.shape[1]
    kern = functools.partial(row_kernel, scale=HEAD_DIM ** (-0.5))
    return pl.pallas_call(
        kern,
        grid=(rows,),
        in_specs=[
            pl.BlockSpec((1, nq, width), lambda r: (r, 0, 0)),
            pl.BlockSpec((1, nk, width), lambda r: (r, 0, 0)),
            pl.BlockSpec((1, nk, width), lambda r: (r, 0, 0)),
            pl.BlockSpec((sk.shape[0], width), lambda r: (0, 0)),
            pl.BlockSpec((sv.shape[0], width), lambda r: (0, 0)),
            pl.BlockSpec((1, nq, nk), lambda r: (r, 0, 0)),
        ],
        out_specs=pl.BlockSpec((1, nq, width), lambda r: (r, 0, 0)),
        out_shape=jax.ShapeDtypeStruct(q.shape, jnp.bfloat16),
    )(q, k, v, sk, sv, allow)


def local(cells, summary, owner, schema, w_qkv, w_out, gain_attn, w_up, w_down, gain_ffn, *, n_band, n_col):
    row_count, cols_dev, model_width = cells.shape
    own_group = lax.axis_index("col")
    own_band = lax.axis_index("band")
    score_scale = HEAD_DIM ** (-0.5)
    flat_cells = cells.reshape(row_count * cols_dev, model_width)
    w_kv = w_qkv[:, model_width:]

    tokens = broadcast_from(summary[0], "band", n_band, owner[0], cells)
    row_parts = fan_out(tokens[1], "col", n_col)
    tokens = tokens[0]

    qkv_cells = project(flat_cells, w_qkv).reshape(row_count, cols_dev, 3 * model_width)
    queries = qkv_cells[:, :, :model_width]
    own_keys = qkv_cells[:, :, model_width : 2 * model_width]
    own_vals = qkv_cells[:, :, 2 * model_width :]

    sum_queries = project(tokens, w_qkv[:, :model_width])
    summary_kv = project(tokens, w_kv)
    sum_keys = summary_kv[:, :model_width]
    sum_vals = summary_kv[:, model_width:]

    sq = sum_queries.astype(jnp.float32)
    col_scores = head_sum(sq[None] * own_keys.astype(jnp.float32)) * score_scale
    self_scores = head_sum(sq * sum_keys.astype(jnp.float32)) * score_scale
    part_top = col_scores.max(0)
    col_exp = jnp.exp(col_scores - part_top[None])
    col_weights = head_spread(col_exp.astype(jnp.bfloat16).astype(jnp.float32))
    part_mixed = (col_weights * own_vals.astype(jnp.float32)).sum(0)
    part_total = col_exp.sum(0)
    merged = half_merge(
        (part_mixed, jnp.concatenate([part_total, part_top], axis=-1)), "band", n_band
    )
    half = cols_dev // 2
    first = (own_band & 1) == 0
    half_self = jnp.where(first, self_scores[:half], self_scores[half:])
    half_vals = jnp.where(first, sum_vals[:half], sum_vals[half:]).astype(jnp.float32)
    col_top = jnp.maximum(merged[1][:, HEADS:], half_self)
    fade = jnp.exp(merged[1][:, HEADS:] - col_top)
    self_exp = jnp.exp(half_self - col_top)
    col_total = merged[1][:, :HEADS] * fade + self_exp
    col_mixed = merged[0] * head_spread(fade) + head_spread(
        self_exp.astype(jnp.bfloat16).astype(jnp.float32)
    ) * half_vals
    summary_att = (col_mixed / head_spread(col_total)).astype(jnp.bfloat16)
    summary_att = join_halves(summary_att, "band", n_band)

    sources = [own_group] + [s for s, _ in row_parts]
    other_cells = jnp.concatenate([got for _, got in row_parts], axis=1)
    width_other = other_cells.shape[1]
    other_kv = project(other_cells.reshape(row_count * width_other, model_width), w_kv)
    other_kv = other_kv.reshape(row_count, width_other, 2 * model_width)
    row_keys = jnp.concatenate([own_keys, other_kv[:, :, :model_width]], axis=1)
    row_vals = jnp.concatenate([own_vals, other_kv[:, :, model_width:]], axis=1)
    width_now = row_keys.shape[1]
    key_groups = jnp.concatenate(
        [jnp.full((cols_dev,), s, jnp.int32) for s in sources]
    )
    own_block = jnp.arange(width_now, dtype=jnp.int32) < cols_dev
    allowed = (jnp.right_shift(schema[:, :, None], key_groups[None, None, :]) & 1 == 1) | own_block[
        None, None, :
    ]
    attended = row_attention(
        queries, row_keys, row_vals, sum_keys, sum_vals, allowed.astype(jnp.float32)
    )
    attended = attended.reshape(row_count * cols_dev, model_width)

    all_in = jnp.concatenate([flat_cells, tokens], axis=0)
    all_att = jnp.concatenate([attended, summary_att], axis=0)
    all_out = finish(all_in, all_att, w_out, gain_attn, w_up, w_down, gain_ffn)
    cells_out = all_out[: row_count * cols_dev].reshape(row_count, cols_dev, model_width)
    summary_out = all_out[row_count * cols_dev :]
    return (cells_out, summary_out)


def solution(mesh):
    in_specs = (
        P("band", "col", None),
        P("band", "col", None),
        P("col"),
        P("band", "col"),
        P(),
        P(),
        P(),
        P(),
        P(),
        P(),
    )
    out_specs = (P("band", "col", None), P("col", None))
    body = functools.partial(local, n_band=mesh.shape["band"], n_col=mesh.shape["col"])
    return jax.shard_map(body, mesh=mesh, in_specs=in_specs, out_specs=out_specs, check_vma=False)
```

```python
import functools

import jax
import jax.numpy as jnp
from jax import lax
from jax.experimental import pallas as pl
from jax.sharding import PartitionSpec as P

HEADS = 12
HEAD_DIM = 64


def spread_2(value, axis, source):
    kept = jnp.where(lax.axis_index(axis) == source, value, 0).astype(value.dtype)
    return lax.psum(kept, axis)


def layer_norm(values, gain_vec):
    center = values - jnp.mean(values, -1, keepdims=True)
    spread = jnp.mean(center * center, -1, keepdims=True)
    return center * lax.rsqrt(spread + 1e-05) * gain_vec


def finish(tokens_in, attended, w_out, gain_attn, w_up, w_down, gain_ffn):
    mixed_out = jnp.dot(attended, w_out, preferred_element_type=jnp.float32)
    hidden = layer_norm(tokens_in.astype(jnp.float32) + mixed_out, gain_attn).astype(jnp.bfloat16)
    inner_act = jax.nn.gelu(jnp.dot(hidden, w_up, preferred_element_type=jnp.float32)).astype(
        jnp.bfloat16
    )
    outer_out = jnp.dot(inner_act, w_down, preferred_element_type=jnp.float32)
    return layer_norm(hidden.astype(jnp.float32) + outer_out, gain_ffn).astype(jnp.bfloat16)


def project(values, weight):
    return jnp.dot(values, weight, preferred_element_type=jnp.float32).astype(jnp.bfloat16)


def head_matrix():
    lanes = jnp.arange(HEADS * HEAD_DIM, dtype=jnp.int32) // HEAD_DIM
    return (lanes[None, :] == jnp.arange(HEADS, dtype=jnp.int32)[:, None]).astype(jnp.float32)


def head_sum(values):
    dims = values.shape[:-1]
    flat = values.reshape(-1, values.shape[-1])
    out = jnp.dot(flat, head_matrix().T, precision=lax.Precision.HIGHEST,
                  preferred_element_type=jnp.float32)
    return out.reshape(dims + (HEADS,))


def head_spread(values):
    dims = values.shape[:-1]
    flat = values.reshape(-1, HEADS)
    out = jnp.dot(flat, head_matrix(), precision=lax.Precision.HIGHEST,
                  preferred_element_type=jnp.float32)
    return out.reshape(dims + (HEADS * HEAD_DIM,))


def partner(value, axis, step, count):
    return lax.ppermute(value, axis, [(i, i ^ step) for i in range(count)])


def broadcast_from(value, axis, count, source, held):
    here = lax.axis_index(axis)
    step = 1
    while step < count:
        got = partner(value, axis, step, count)
        if step == 1:
            got, held = lax.optimization_barrier((got, held))
        value = jnp.where(here // step == source // step, value, got)
        step *= 2
    return value, held


def merge(lo, hi):
    top = jnp.maximum(lo[1][:, HEADS:], hi[1][:, HEADS:])
    fade_lo = jnp.exp(lo[1][:, HEADS:] - top)
    fade_hi = jnp.exp(hi[1][:, HEADS:] - top)
    total = lo[1][:, :HEADS] * fade_lo + hi[1][:, :HEADS] * fade_hi
    mixed = lo[0] * head_spread(fade_lo) + hi[0] * head_spread(fade_hi)
    return mixed, jnp.concatenate([total, top], axis=-1)


def pick(flag, a, b):
    return tuple(jnp.where(flag, x, y) for x, y in zip(a, b))


def half_merge(value, axis, count):
    here = lax.axis_index(axis)
    half = value[0].shape[0] // 2
    first = (here & 1) == 0
    top_half = tuple(v[:half] for v in value)
    low_half = tuple(v[half:] for v in value)
    mine = pick(first, top_half, low_half)
    sent = pick(first, low_half, top_half)
    got = tuple(partner(v, axis, 1, count) for v in sent)
    value = merge(pick(first, mine, got), pick(first, got, mine))
    step = 2
    while step < count:
        mixed = value[0].astype(jnp.bfloat16)
        got = (
            partner(mixed, axis, step, count).astype(jnp.float32),
            partner(value[1], axis, step, count),
        )
        mine = (mixed.astype(jnp.float32), value[1])
        low_side = (here & step) == 0
        value = merge(pick(low_side, mine, got), pick(low_side, got, mine))
        step *= 2
    return value


def join_halves(value, axis, count):
    first = (lax.axis_index(axis) & 1) == 0
    got = partner(value, axis, 1, count)
    return jnp.where(first, jnp.concatenate([value, got]), jnp.concatenate([got, value]))


def fan_out(value, axis, count):
    here = lax.axis_index(axis)
    got = []
    for step in range(1, count):
        if count & (count - 1) == 0:
            pairs = [(i, i ^ step) for i in range(count)]
            source = here ^ step
        else:
            pairs = [(i, (i + step) % count) for i in range(count)]
            source = (here - step) % count
        got.append((source, lax.ppermute(value, axis, pairs)))
    return got


def row_kernel(q_ref, kt_ref, v_ref, skt_ref, sv_ref, allow_ref, o_ref, *, scale):
    allow = allow_ref[0] > 0.5
    lane = lax.broadcasted_iota(jnp.int32, (1, 2 * HEAD_DIM), 1)
    low = lane < HEAD_DIM
    for pair in range(HEADS // 2):
        cols = slice(pair * 2 * HEAD_DIM, (pair + 1) * 2 * HEAD_DIM)
        q = q_ref[0, :, cols]
        kt = kt_ref[0, cols, :]
        v = v_ref[0, :, cols]
        skt = skt_ref[cols, :]
        sv = sv_ref[:, cols]
        outs = []
        for side in (low, jnp.logical_not(low)):
            qh = jnp.where(side, q, jnp.zeros_like(q))
            s = jnp.dot(qh, kt, preferred_element_type=jnp.float32) * scale
            s = jnp.where(allow, s, -1e30)
            ts = jnp.dot(qh, skt, preferred_element_type=jnp.float32) * scale
            top = jnp.maximum(s.max(-1, keepdims=True), ts.max(-1, keepdims=True))
            e = jnp.exp(s - top)
            te = jnp.exp(ts - top)
            tot = e.sum(-1, keepdims=True) + te.sum(-1, keepdims=True)
            acc = jnp.dot(e.astype(jnp.bfloat16), v, preferred_element_type=jnp.float32)
            acc = acc + jnp.dot(te.astype(jnp.bfloat16), sv, preferred_element_type=jnp.float32)
            outs.append(acc / tot)
        o_ref[0, :, cols] = jnp.where(low, outs[0], outs[1]).astype(o_ref.dtype)


def row_attention(q, kt, v, skt, sv, allow):
    rows, nq, width = q.shape
    nk = v.shape[1]
    kern = functools.partial(row_kernel, scale=HEAD_DIM ** (-0.5))
    return pl.pallas_call(
        kern,
        grid=(rows,),
        in_specs=[
            pl.BlockSpec((1, nq, width), lambda r: (r, 0, 0)),
            pl.BlockSpec((1, width, nk), lambda r: (r, 0, 0)),
            pl.BlockSpec((1, nk, width), lambda r: (r, 0, 0)),
            pl.BlockSpec((width, skt.shape[1]), lambda r: (0, 0)),
            pl.BlockSpec((sv.shape[0], width), lambda r: (0, 0)),
            pl.BlockSpec((1, nq, nk), lambda r: (r, 0, 0)),
        ],
        out_specs=pl.BlockSpec((1, nq, width), lambda r: (r, 0, 0)),
        out_shape=jax.ShapeDtypeStruct(q.shape, jnp.bfloat16),
    )(q, kt, v, skt, sv, allow)


def local(cells, summary, owner, schema, w_qkv, w_out, gain_attn, w_up, w_down, gain_ffn, *, n_band, n_col):
    row_count, cols_dev, model_width = cells.shape
    own_group = lax.axis_index("col")
    own_band = lax.axis_index("band")
    score_scale = HEAD_DIM ** (-0.5)
    flat_cells = cells.reshape(row_count * cols_dev, model_width)
    w_kv = w_qkv[:, model_width:]

    tokens = broadcast_from(summary[0], "band", n_band, owner[0], cells)
    row_parts = fan_out(tokens[1], "col", n_col)
    tokens = tokens[0]

    qkv_cells = project(flat_cells, w_qkv).reshape(row_count, cols_dev, 3 * model_width)
    queries = qkv_cells[:, :, :model_width]
    own_keys = qkv_cells[:, :, model_width : 2 * model_width]
    own_vals = qkv_cells[:, :, 2 * model_width :]

    sum_queries = project(tokens, w_qkv[:, :model_width])
    summary_kv = project(tokens, w_kv)
    sum_keys = summary_kv[:, :model_width]
    sum_vals = summary_kv[:, model_width:]

    sq = sum_queries.astype(jnp.float32)
    col_scores = head_sum(sq[None] * own_keys.astype(jnp.float32)) * score_scale
    self_scores = head_sum(sq * sum_keys.astype(jnp.float32)) * score_scale
    part_top = col_scores.max(0)
    col_exp = jnp.exp(col_scores - part_top[None])
    col_weights = head_spread(col_exp.astype(jnp.bfloat16).astype(jnp.float32))
    part_mixed = (col_weights * own_vals.astype(jnp.float32)).sum(0)
    part_total = col_exp.sum(0)
    merged = half_merge(
        (part_mixed, jnp.concatenate([part_total, part_top], axis=-1)), "band", n_band
    )
    half = cols_dev // 2
    first = (own_band & 1) == 0
    half_self = jnp.where(first, self_scores[:half], self_scores[half:])
    half_vals = jnp.where(first, sum_vals[:half], sum_vals[half:]).astype(jnp.float32)
    col_top = jnp.maximum(merged[1][:, HEADS:], half_self)
    fade = jnp.exp(merged[1][:, HEADS:] - col_top)
    self_exp = jnp.exp(half_self - col_top)
    col_total = merged[1][:, :HEADS] * fade + self_exp
    col_mixed = merged[0] * head_spread(fade) + head_spread(
        self_exp.astype(jnp.bfloat16).astype(jnp.float32)
    ) * half_vals
    summary_att = (col_mixed / head_spread(col_total)).astype(jnp.bfloat16)
    summary_att = join_halves(summary_att, "band", n_band)

    sources = [own_group] + [s for s, _ in row_parts]
    other_cells = jnp.concatenate([got for _, got in row_parts], axis=1)
    width_other = other_cells.shape[1]
    other_kv = project(other_cells.reshape(row_count * width_other, model_width), w_kv)
    other_kv = other_kv.reshape(row_count, width_other, 2 * model_width)
    row_keys = jnp.concatenate([own_keys, other_kv[:, :, :model_width]], axis=1)
    row_vals = jnp.concatenate([own_vals, other_kv[:, :, model_width:]], axis=1)
    width_now = row_keys.shape[1]
    key_groups = jnp.concatenate(
        [jnp.full((cols_dev,), s, jnp.int32) for s in sources]
    )
    own_block = jnp.arange(width_now, dtype=jnp.int32) < cols_dev
    allowed = (jnp.right_shift(schema[:, :, None], key_groups[None, None, :]) & 1 == 1) | own_block[
        None, None, :
    ]
    attended = row_attention(
        queries, jnp.swapaxes(row_keys, 1, 2), row_vals, sum_keys.T, sum_vals,
        allowed.astype(jnp.float32),
    )
    attended = attended.reshape(row_count * cols_dev, model_width)

    all_in = jnp.concatenate([flat_cells, tokens], axis=0)
    all_att = jnp.concatenate([attended, summary_att], axis=0)
    all_out = finish(all_in, all_att, w_out, gain_attn, w_up, w_down, gain_ffn)
    cells_out = all_out[: row_count * cols_dev].reshape(row_count, cols_dev, model_width)
    summary_out = all_out[row_count * cols_dev :]
    return (cells_out, summary_out)


def solution(mesh):
    in_specs = (
        P("band", "col", None),
        P("band", "col", None),
        P("col"),
        P("band", "col"),
        P(),
        P(),
        P(),
        P(),
        P(),
        P(),
    )
    out_specs = (P("band", "col", None), P("col", None))
    body = functools.partial(local, n_band=mesh.shape["band"], n_col=mesh.shape["col"])
    return jax.shard_map(body, mesh=mesh, in_specs=in_specs, out_specs=out_specs, check_vma=False)
```

```python
import functools

import jax
import jax.numpy as jnp
from jax import lax
from jax.experimental import pallas as pl
from jax.sharding import PartitionSpec as P

HEADS = 12
HEAD_DIM = 64


def spread_2(value, axis, source):
    kept = jnp.where(lax.axis_index(axis) == source, value, 0).astype(value.dtype)
    return lax.psum(kept, axis)


def layer_norm(values, gain_vec):
    center = values - jnp.mean(values, -1, keepdims=True)
    spread = jnp.mean(center * center, -1, keepdims=True)
    return center * lax.rsqrt(spread + 1e-05) * gain_vec


def finish(tokens_in, attended, w_out, gain_attn, w_up, w_down, gain_ffn):
    mixed_out = jnp.dot(attended, w_out, preferred_element_type=jnp.float32)
    hidden = layer_norm(tokens_in.astype(jnp.float32) + mixed_out, gain_attn).astype(jnp.bfloat16)
    inner_act = jax.nn.gelu(jnp.dot(hidden, w_up, preferred_element_type=jnp.float32)).astype(
        jnp.bfloat16
    )
    outer_out = jnp.dot(inner_act, w_down, preferred_element_type=jnp.float32)
    return layer_norm(hidden.astype(jnp.float32) + outer_out, gain_ffn).astype(jnp.bfloat16)


def project(values, weight):
    return jnp.dot(values, weight, preferred_element_type=jnp.float32).astype(jnp.bfloat16)


def head_matrix():
    lanes = jnp.arange(HEADS * HEAD_DIM, dtype=jnp.int32) // HEAD_DIM
    return (lanes[None, :] == jnp.arange(HEADS, dtype=jnp.int32)[:, None]).astype(jnp.float32)


def head_sum(values):
    dims = values.shape[:-1]
    flat = values.reshape(-1, values.shape[-1])
    out = jnp.dot(flat, head_matrix().T, precision=lax.Precision.HIGHEST,
                  preferred_element_type=jnp.float32)
    return out.reshape(dims + (HEADS,))


def head_spread(values):
    dims = values.shape[:-1]
    flat = values.reshape(-1, HEADS)
    out = jnp.dot(flat, head_matrix(), precision=lax.Precision.HIGHEST,
                  preferred_element_type=jnp.float32)
    return out.reshape(dims + (HEADS * HEAD_DIM,))


def partner(value, axis, step, count):
    return lax.ppermute(value, axis, [(i, i ^ step) for i in range(count)])


def broadcast_from(value, axis, count, source, held):
    here = lax.axis_index(axis)
    step = 1
    while step < count:
        got = partner(value, axis, step, count)
        if step == 1:
            got, held = lax.optimization_barrier((got, held))
        value = jnp.where(here // step == source // step, value, got)
        step *= 2
    return value, held


def merge(lo, hi):
    top = jnp.maximum(lo[1][:, HEADS:], hi[1][:, HEADS:])
    fade_lo = jnp.exp(lo[1][:, HEADS:] - top)
    fade_hi = jnp.exp(hi[1][:, HEADS:] - top)
    total = lo[1][:, :HEADS] * fade_lo + hi[1][:, :HEADS] * fade_hi
    mixed = lo[0] * head_spread(fade_lo) + hi[0] * head_spread(fade_hi)
    return mixed, jnp.concatenate([total, top], axis=-1)


def pick(flag, a, b):
    return tuple(jnp.where(flag, x, y) for x, y in zip(a, b))


def half_merge(value, axis, count):
    here = lax.axis_index(axis)
    half = value[0].shape[0] // 2
    first = (here & 1) == 0
    top_half = tuple(v[:half] for v in value)
    low_half = tuple(v[half:] for v in value)
    mine = pick(first, top_half, low_half)
    sent = pick(first, low_half, top_half)
    got = tuple(partner(v, axis, 1, count) for v in sent)
    value = merge(pick(first, mine, got), pick(first, got, mine))
    step = 2
    while step < count:
        mixed = value[0].astype(jnp.bfloat16)
        got = (
            partner(mixed, axis, step, count).astype(jnp.float32),
            partner(value[1], axis, step, count),
        )
        mine = (mixed.astype(jnp.float32), value[1])
        low_side = (here & step) == 0
        value = merge(pick(low_side, mine, got), pick(low_side, got, mine))
        step *= 2
    return value


def join_halves(value, axis, count):
    first = (lax.axis_index(axis) & 1) == 0
    got = partner(value, axis, 1, count)
    return jnp.where(first, jnp.concatenate([value, got]), jnp.concatenate([got, value]))


def fan_out(value, axis, count):
    here = lax.axis_index(axis)
    got = []
    for step in range(1, count):
        if count & (count - 1) == 0:
            pairs = [(i, i ^ step) for i in range(count)]
            source = here ^ step
        else:
            pairs = [(i, (i + step) % count) for i in range(count)]
            source = (here - step) % count
        got.append((source, lax.ppermute(value, axis, pairs)))
    return got


def row_kernel(q_ref, k_ref, v_ref, sk_ref, sv_ref, allow_ref, o_ref, *, scale):
    rows = q_ref.shape[1]
    allow = allow_ref[0] > 0.5
    allow = jnp.concatenate([allow, allow], axis=0)
    lane = lax.broadcasted_iota(jnp.int32, (1, 2 * HEAD_DIM), 1)
    low = lane < HEAD_DIM
    nt = (((1,), (1,)), ((), ()))
    for pair in range(HEADS // 2):
        cols = slice(pair * 2 * HEAD_DIM, (pair + 1) * 2 * HEAD_DIM)
        q = q_ref[0, :, cols] * scale
        zero = jnp.zeros_like(q)
        qh = jnp.concatenate([jnp.where(low, q, zero), jnp.where(low, zero, q)], axis=0)
        k = k_ref[0, :, cols]
        v = v_ref[0, :, cols]
        sk = sk_ref[:, cols]
        sv = sv_ref[:, cols]
        s = lax.dot_general(qh, k, nt, preferred_element_type=jnp.float32)
        s = jnp.where(allow, s, -1e30)
        ts = lax.dot_general(qh, sk, nt, preferred_element_type=jnp.float32)
        top = jnp.maximum(s.max(-1, keepdims=True), ts.max(-1, keepdims=True))
        e = jnp.exp(s - top)
        te = jnp.exp(ts - top)
        tot = e.sum(-1, keepdims=True) + te.sum(-1, keepdims=True)
        acc = jnp.dot(e.astype(jnp.bfloat16), v, preferred_element_type=jnp.float32)
        acc = acc + jnp.dot(te.astype(jnp.bfloat16), sv, preferred_element_type=jnp.float32)
        out = jnp.where(low, acc[:rows] / tot[:rows], acc[rows:] / tot[rows:])
        o_ref[0, :, cols] = out.astype(o_ref.dtype)


def row_attention(q, k, v, sk, sv, allow):
    rows, nq, width = q.shape
    nk = k.shape[1]
    kern = functools.partial(row_kernel, scale=HEAD_DIM ** (-0.5))
    return pl.pallas_call(
        kern,
        grid=(rows,),
        in_specs=[
            pl.BlockSpec((1, nq, width), lambda r: (r, 0, 0)),
            pl.BlockSpec((1, nk, width), lambda r: (r, 0, 0)),
            pl.BlockSpec((1, nk, width), lambda r: (r, 0, 0)),
            pl.BlockSpec((sk.shape[0], width), lambda r: (0, 0)),
            pl.BlockSpec((sv.shape[0], width), lambda r: (0, 0)),
            pl.BlockSpec((1, nq, nk), lambda r: (r, 0, 0)),
        ],
        out_specs=pl.BlockSpec((1, nq, width), lambda r: (r, 0, 0)),
        out_shape=jax.ShapeDtypeStruct(q.shape, jnp.bfloat16),
    )(q, k, v, sk, sv, allow)


def local(cells, summary, owner, schema, w_qkv, w_out, gain_attn, w_up, w_down, gain_ffn, *, n_band, n_col):
    row_count, cols_dev, model_width = cells.shape
    own_group = lax.axis_index("col")
    own_band = lax.axis_index("band")
    score_scale = HEAD_DIM ** (-0.5)
    flat_cells = cells.reshape(row_count * cols_dev, model_width)
    w_kv = w_qkv[:, model_width:]

    tokens = broadcast_from(summary[0], "band", n_band, owner[0], cells)
    row_parts = fan_out(tokens[1], "col", n_col)
    tokens = tokens[0]

    qkv_cells = project(flat_cells, w_qkv).reshape(row_count, cols_dev, 3 * model_width)
    queries = qkv_cells[:, :, :model_width]
    own_keys = qkv_cells[:, :, model_width : 2 * model_width]
    own_vals = qkv_cells[:, :, 2 * model_width :]

    sum_queries = project(tokens, w_qkv[:, :model_width])
    summary_kv = project(tokens, w_kv)
    sum_keys = summary_kv[:, :model_width]
    sum_vals = summary_kv[:, model_width:]

    sq = sum_queries.astype(jnp.float32)
    col_scores = head_sum(sq[None] * own_keys.astype(jnp.float32)) * score_scale
    self_scores = head_sum(sq * sum_keys.astype(jnp.float32)) * score_scale
    part_top = col_scores.max(0)
    col_exp = jnp.exp(col_scores - part_top[None])
    col_weights = head_spread(col_exp.astype(jnp.bfloat16).astype(jnp.float32))
    part_mixed = (col_weights * own_vals.astype(jnp.float32)).sum(0)
    part_total = col_exp.sum(0)
    merged = half_merge(
        (part_mixed, jnp.concatenate([part_total, part_top], axis=-1)), "band", n_band
    )
    half = cols_dev // 2
    first = (own_band & 1) == 0
    half_self = jnp.where(first, self_scores[:half], self_scores[half:])
    half_vals = jnp.where(first, sum_vals[:half], sum_vals[half:]).astype(jnp.float32)
    col_top = jnp.maximum(merged[1][:, HEADS:], half_self)
    fade = jnp.exp(merged[1][:, HEADS:] - col_top)
    self_exp = jnp.exp(half_self - col_top)
    col_total = merged[1][:, :HEADS] * fade + self_exp
    col_mixed = merged[0] * head_spread(fade) + head_spread(
        self_exp.astype(jnp.bfloat16).astype(jnp.float32)
    ) * half_vals
    summary_att = (col_mixed / head_spread(col_total)).astype(jnp.bfloat16)
    summary_att = join_halves(summary_att, "band", n_band)

    sources = [own_group] + [s for s, _ in row_parts]
    other_cells = jnp.concatenate([got for _, got in row_parts], axis=1)
    width_other = other_cells.shape[1]
    other_kv = project(other_cells.reshape(row_count * width_other, model_width), w_kv)
    other_kv = other_kv.reshape(row_count, width_other, 2 * model_width)
    row_keys = jnp.concatenate([own_keys, other_kv[:, :, :model_width]], axis=1)
    row_vals = jnp.concatenate([own_vals, other_kv[:, :, model_width:]], axis=1)
    width_now = row_keys.shape[1]
    key_groups = jnp.concatenate(
        [jnp.full((cols_dev,), s, jnp.int32) for s in sources]
    )
    own_block = jnp.arange(width_now, dtype=jnp.int32) < cols_dev
    allowed = (jnp.right_shift(schema[:, :, None], key_groups[None, None, :]) & 1 == 1) | own_block[
        None, None, :
    ]
    attended = row_attention(
        queries, row_keys, row_vals, sum_keys, sum_vals, allowed.astype(jnp.float32)
    )
    attended = attended.reshape(row_count * cols_dev, model_width)

    all_in = jnp.concatenate([flat_cells, tokens], axis=0)
    all_att = jnp.concatenate([attended, summary_att], axis=0)
    all_out = finish(all_in, all_att, w_out, gain_attn, w_up, w_down, gain_ffn)
    cells_out = all_out[: row_count * cols_dev].reshape(row_count, cols_dev, model_width)
    summary_out = all_out[row_count * cols_dev :]
    return (cells_out, summary_out)


def solution(mesh):
    in_specs = (
        P("band", "col", None),
        P("band", "col", None),
        P("col"),
        P("band", "col"),
        P(),
        P(),
        P(),
        P(),
        P(),
        P(),
    )
    out_specs = (P("band", "col", None), P("col", None))
    body = functools.partial(local, n_band=mesh.shape["band"], n_col=mesh.shape["col"])
    return jax.shard_map(body, mesh=mesh, in_specs=in_specs, out_specs=out_specs, check_vma=False)
```

```python
import functools

import jax
import jax.numpy as jnp
from jax import lax
from jax.experimental import pallas as pl
from jax.sharding import PartitionSpec as P

HEADS = 12
HEAD_DIM = 64


def spread_2(value, axis, source):
    kept = jnp.where(lax.axis_index(axis) == source, value, 0).astype(value.dtype)
    return lax.psum(kept, axis)


def layer_norm(values, gain_vec):
    center = values - jnp.mean(values, -1, keepdims=True)
    spread = jnp.mean(center * center, -1, keepdims=True)
    return center * lax.rsqrt(spread + 1e-05) * gain_vec


def finish(tokens_in, attended, w_out, gain_attn, w_up, w_down, gain_ffn):
    mixed_out = jnp.dot(attended, w_out, preferred_element_type=jnp.float32)
    hidden = layer_norm(tokens_in.astype(jnp.float32) + mixed_out, gain_attn).astype(jnp.bfloat16)
    inner_act = jax.nn.gelu(jnp.dot(hidden, w_up, preferred_element_type=jnp.float32)).astype(
        jnp.bfloat16
    )
    outer_out = jnp.dot(inner_act, w_down, preferred_element_type=jnp.float32)
    return layer_norm(hidden.astype(jnp.float32) + outer_out, gain_ffn).astype(jnp.bfloat16)


def project(values, weight):
    return jnp.dot(values, weight, preferred_element_type=jnp.float32).astype(jnp.bfloat16)


def head_matrix():
    lanes = jnp.arange(HEADS * HEAD_DIM, dtype=jnp.int32) // HEAD_DIM
    return (lanes[None, :] == jnp.arange(HEADS, dtype=jnp.int32)[:, None]).astype(jnp.float32)


def head_sum(values):
    dims = values.shape[:-1]
    flat = values.reshape(-1, values.shape[-1])
    out = jnp.dot(flat, head_matrix().T, precision=lax.Precision.HIGHEST,
                  preferred_element_type=jnp.float32)
    return out.reshape(dims + (HEADS,))


def head_spread(values):
    dims = values.shape[:-1]
    flat = values.reshape(-1, HEADS)
    out = jnp.dot(flat, head_matrix(), precision=lax.Precision.HIGHEST,
                  preferred_element_type=jnp.float32)
    return out.reshape(dims + (HEADS * HEAD_DIM,))


def partner(value, axis, step, count):
    return lax.ppermute(value, axis, [(i, i ^ step) for i in range(count)])


def broadcast_from(value, axis, count, source, held):
    here = lax.axis_index(axis)
    step = 1
    while step < count:
        got = partner(value, axis, step, count)
        if step == 1:
            got, held = lax.optimization_barrier((got, held))
        value = jnp.where(here // step == source // step, value, got)
        step *= 2
    return value, held


def merge(lo, hi):
    top = jnp.maximum(lo[1][:, HEADS:], hi[1][:, HEADS:])
    fade_lo = jnp.exp(lo[1][:, HEADS:] - top)
    fade_hi = jnp.exp(hi[1][:, HEADS:] - top)
    total = lo[1][:, :HEADS] * fade_lo + hi[1][:, :HEADS] * fade_hi
    mixed = lo[0] * head_spread(fade_lo) + hi[0] * head_spread(fade_hi)
    return mixed, jnp.concatenate([total, top], axis=-1)


def pick(flag, a, b):
    return tuple(jnp.where(flag, x, y) for x, y in zip(a, b))


def half_merge(value, axis, count):
    here = lax.axis_index(axis)
    half = value[0].shape[0] // 2
    first = (here & 1) == 0
    top_half = tuple(v[:half] for v in value)
    low_half = tuple(v[half:] for v in value)
    mine = pick(first, top_half, low_half)
    sent = pick(first, low_half, top_half)
    got = tuple(partner(v, axis, 1, count) for v in sent)
    value = merge(pick(first, mine, got), pick(first, got, mine))
    step = 2
    while step < count:
        mixed = value[0].astype(jnp.bfloat16)
        got = (
            partner(mixed, axis, step, count).astype(jnp.float32),
            partner(value[1], axis, step, count),
        )
        mine = (mixed.astype(jnp.float32), value[1])
        low_side = (here & step) == 0
        value = merge(pick(low_side, mine, got), pick(low_side, got, mine))
        step *= 2
    return value


def join_halves(value, axis, count):
    first = (lax.axis_index(axis) & 1) == 0
    got = partner(value, axis, 1, count)
    return jnp.where(first, jnp.concatenate([value, got]), jnp.concatenate([got, value]))


def fan_out(value, axis, count):
    here = lax.axis_index(axis)
    got = []
    for step in range(1, count):
        if count & (count - 1) == 0:
            pairs = [(i, i ^ step) for i in range(count)]
            source = here ^ step
        else:
            pairs = [(i, (i + step) % count) for i in range(count)]
            source = (here - step) % count
        got.append((source, lax.ppermute(value, axis, pairs)))
    return got


def row_kernel(q_ref, k_ref, v_ref, sk_ref, sv_ref, allow_ref, o_ref, *, scale):
    rows = q_ref.shape[1]
    allow = allow_ref[0] > 0.5
    allow = jnp.concatenate([allow, allow], axis=0)
    lane = lax.broadcasted_iota(jnp.int32, (1, 2 * HEAD_DIM), 1)
    low = lane < HEAD_DIM
    nt = (((1,), (1,)), ((), ()))
    for pair in range(HEADS // 2):
        cols = slice(pair * 2 * HEAD_DIM, (pair + 1) * 2 * HEAD_DIM)
        q = q_ref[0, :, cols] * scale
        zero = jnp.zeros_like(q)
        qh = jnp.concatenate([jnp.where(low, q, zero), jnp.where(low, zero, q)], axis=0)
        k = k_ref[0, :, cols]
        v = v_ref[0, :, cols]
        sk = sk_ref[:, cols]
        sv = sv_ref[:, cols]
        s = lax.dot_general(qh, k, nt, preferred_element_type=jnp.float32)
        s = jnp.where(allow, s, -1e30)
        ts = lax.dot_general(qh, sk, nt, preferred_element_type=jnp.float32)
        top = jnp.maximum(s.max(-1, keepdims=True), ts.max(-1, keepdims=True))
        e = jnp.exp(s - top)
        te = jnp.exp(ts - top)
        tot = e.sum(-1, keepdims=True) + te.sum(-1, keepdims=True)
        acc = jnp.dot(e.astype(jnp.bfloat16), v, preferred_element_type=jnp.float32)
        acc = acc + jnp.dot(te.astype(jnp.bfloat16), sv, preferred_element_type=jnp.float32)
        out = jnp.where(low, acc[:rows] / tot[:rows], acc[rows:] / tot[rows:])
        o_ref[0, :, cols] = out.astype(o_ref.dtype)


def row_attention(qkv, kv, summary_kv, allow):
    rows, nq, triple = qkv.shape
    width = triple // 3
    nk = kv.shape[1]
    ns = summary_kv.shape[0]
    kern = functools.partial(row_kernel, scale=HEAD_DIM ** (-0.5))
    return pl.pallas_call(
        kern,
        grid=(rows,),
        in_specs=[
            pl.BlockSpec((1, nq, width), lambda r: (r, 0, 0)),
            pl.BlockSpec((1, nk, width), lambda r: (r, 0, 0)),
            pl.BlockSpec((1, nk, width), lambda r: (r, 0, 1)),
            pl.BlockSpec((ns, width), lambda r: (0, 0)),
            pl.BlockSpec((ns, width), lambda r: (0, 1)),
            pl.BlockSpec((1, nq, nk), lambda r: (r, 0, 0)),
        ],
        out_specs=pl.BlockSpec((1, nq, width), lambda r: (r, 0, 0)),
        out_shape=jax.ShapeDtypeStruct((rows, nq, width), jnp.bfloat16),
    )(qkv, kv, kv, summary_kv, summary_kv, allow)


def local(cells, summary, owner, schema, w_qkv, w_out, gain_attn, w_up, w_down, gain_ffn, *, n_band, n_col):
    row_count, cols_dev, model_width = cells.shape
    own_group = lax.axis_index("col")
    own_band = lax.axis_index("band")
    score_scale = HEAD_DIM ** (-0.5)
    flat_cells = cells.reshape(row_count * cols_dev, model_width)
    w_kv = w_qkv[:, model_width:]

    tokens = broadcast_from(summary[0], "band", n_band, owner[0], cells)
    row_parts = fan_out(tokens[1], "col", n_col)
    tokens = tokens[0]

    qkv_cells = project(flat_cells, w_qkv).reshape(row_count, cols_dev, 3 * model_width)
    queries = qkv_cells[:, :, :model_width]
    own_keys = qkv_cells[:, :, model_width : 2 * model_width]
    own_vals = qkv_cells[:, :, 2 * model_width :]

    sum_queries = project(tokens, w_qkv[:, :model_width])
    summary_kv = project(tokens, w_kv)
    sum_keys = summary_kv[:, :model_width]
    sum_vals = summary_kv[:, model_width:]

    sq = sum_queries.astype(jnp.float32)
    col_scores = head_sum(sq[None] * own_keys.astype(jnp.float32)) * score_scale
    self_scores = head_sum(sq * sum_keys.astype(jnp.float32)) * score_scale
    part_top = col_scores.max(0)
    col_exp = jnp.exp(col_scores - part_top[None])
    col_weights = head_spread(col_exp.astype(jnp.bfloat16).astype(jnp.float32))
    part_mixed = (col_weights * own_vals.astype(jnp.float32)).sum(0)
    part_total = col_exp.sum(0)
    merged = half_merge(
        (part_mixed, jnp.concatenate([part_total, part_top], axis=-1)), "band", n_band
    )
    half = cols_dev // 2
    first = (own_band & 1) == 0
    half_self = jnp.where(first, self_scores[:half], self_scores[half:])
    half_vals = jnp.where(first, sum_vals[:half], sum_vals[half:]).astype(jnp.float32)
    col_top = jnp.maximum(merged[1][:, HEADS:], half_self)
    fade = jnp.exp(merged[1][:, HEADS:] - col_top)
    self_exp = jnp.exp(half_self - col_top)
    col_total = merged[1][:, :HEADS] * fade + self_exp
    col_mixed = merged[0] * head_spread(fade) + head_spread(
        self_exp.astype(jnp.bfloat16).astype(jnp.float32)
    ) * half_vals
    summary_att = (col_mixed / head_spread(col_total)).astype(jnp.bfloat16)
    summary_att = join_halves(summary_att, "band", n_band)

    sources = [own_group] + [s for s, _ in row_parts]
    row_cells = jnp.concatenate([cells] + [got for _, got in row_parts], axis=1)
    width_now = row_cells.shape[1]
    row_kv = project(row_cells.reshape(row_count * width_now, model_width), w_kv)
    row_kv = row_kv.reshape(row_count, width_now, 2 * model_width)
    key_groups = jnp.concatenate(
        [jnp.full((cols_dev,), s, jnp.int32) for s in sources]
    )
    own_block = jnp.arange(width_now, dtype=jnp.int32) < cols_dev
    allowed = (jnp.right_shift(schema[:, :, None], key_groups[None, None, :]) & 1 == 1) | own_block[
        None, None, :
    ]
    attended = row_attention(qkv_cells, row_kv, summary_kv, allowed.astype(jnp.float32))
    attended = attended.reshape(row_count * cols_dev, model_width)

    all_in = jnp.concatenate([flat_cells, tokens], axis=0)
    all_att = jnp.concatenate([attended, summary_att], axis=0)
    all_out = finish(all_in, all_att, w_out, gain_attn, w_up, w_down, gain_ffn)
    cells_out = all_out[: row_count * cols_dev].reshape(row_count, cols_dev, model_width)
    summary_out = all_out[row_count * cols_dev :]
    return (cells_out, summary_out)


def solution(mesh):
    in_specs = (
        P("band", "col", None),
        P("band", "col", None),
        P("col"),
        P("band", "col"),
        P(),
        P(),
        P(),
        P(),
        P(),
        P(),
    )
    out_specs = (P("band", "col", None), P("col", None))
    body = functools.partial(local, n_band=mesh.shape["band"], n_col=mesh.shape["col"])
    return jax.shard_map(body, mesh=mesh, in_specs=in_specs, out_specs=out_specs, check_vma=False)
```

```python
import functools

import jax
import jax.numpy as jnp
from jax import lax
from jax.experimental import pallas as pl
from jax.sharding import PartitionSpec as P

HEADS = 12
HEAD_DIM = 64


def spread_2(value, axis, source):
    kept = jnp.where(lax.axis_index(axis) == source, value, 0).astype(value.dtype)
    return lax.psum(kept, axis)


def layer_norm(values, gain_vec):
    center = values - jnp.mean(values, -1, keepdims=True)
    spread = jnp.mean(center * center, -1, keepdims=True)
    return center * lax.rsqrt(spread + 1e-05) * gain_vec


def finish(tokens_in, attended, w_out, gain_attn, w_up, w_down, gain_ffn):
    mixed_out = jnp.dot(attended, w_out, preferred_element_type=jnp.float32)
    hidden = layer_norm(tokens_in.astype(jnp.float32) + mixed_out, gain_attn).astype(jnp.bfloat16)
    inner_act = jax.nn.gelu(jnp.dot(hidden, w_up, preferred_element_type=jnp.float32)).astype(
        jnp.bfloat16
    )
    outer_out = jnp.dot(inner_act, w_down, preferred_element_type=jnp.float32)
    return layer_norm(hidden.astype(jnp.float32) + outer_out, gain_ffn).astype(jnp.bfloat16)


def project(values, weight):
    return jnp.dot(values, weight, preferred_element_type=jnp.float32).astype(jnp.bfloat16)


def head_matrix():
    lanes = jnp.arange(HEADS * HEAD_DIM, dtype=jnp.int32) // HEAD_DIM
    return (lanes[None, :] == jnp.arange(HEADS, dtype=jnp.int32)[:, None]).astype(jnp.float32)


def head_sum(values):
    dims = values.shape[:-1]
    flat = values.reshape(-1, values.shape[-1])
    out = jnp.dot(flat, head_matrix().T, precision=lax.Precision.HIGHEST,
                  preferred_element_type=jnp.float32)
    return out.reshape(dims + (HEADS,))


def head_spread(values):
    dims = values.shape[:-1]
    flat = values.reshape(-1, HEADS)
    out = jnp.dot(flat, head_matrix(), precision=lax.Precision.HIGHEST,
                  preferred_element_type=jnp.float32)
    return out.reshape(dims + (HEADS * HEAD_DIM,))


def partner(value, axis, step, count):
    return lax.ppermute(value, axis, [(i, i ^ step) for i in range(count)])


def broadcast_from(value, axis, count, source, held):
    here = lax.axis_index(axis)
    step = 1
    while step < count:
        got = partner(value, axis, step, count)
        if step == 1:
            got, held = lax.optimization_barrier((got, held))
        value = jnp.where(here // step == source // step, value, got)
        step *= 2
    return value, held


def merge(lo, hi):
    top = jnp.maximum(lo[1][:, HEADS:], hi[1][:, HEADS:])
    fade_lo = jnp.exp(lo[1][:, HEADS:] - top)
    fade_hi = jnp.exp(hi[1][:, HEADS:] - top)
    total = lo[1][:, :HEADS] * fade_lo + hi[1][:, :HEADS] * fade_hi
    mixed = lo[0] * head_spread(fade_lo) + hi[0] * head_spread(fade_hi)
    return mixed, jnp.concatenate([total, top], axis=-1)


def pick(flag, a, b):
    return tuple(jnp.where(flag, x, y) for x, y in zip(a, b))


def pack_partial(value):
    stats = value[1]
    high = stats.astype(jnp.bfloat16)
    rest = stats - high.astype(jnp.float32)
    middle = rest.astype(jnp.bfloat16)
    low = (rest - middle.astype(jnp.float32)).astype(jnp.bfloat16)
    return jnp.concatenate([value[0].astype(jnp.bfloat16), high, middle, low], axis=-1)


def unpack_partial(packed, width):
    part = packed.astype(jnp.float32)
    n = (packed.shape[1] - width) // 3
    stats = (part[:, width : width + n] + part[:, width + n : width + 2 * n]) + part[:, width + 2 * n :]
    return part[:, :width], stats


def half_merge(value, axis, count):
    here = lax.axis_index(axis)
    half = value[0].shape[0] // 2
    first = (here & 1) == 0
    top_half = tuple(v[:half] for v in value)
    low_half = tuple(v[half:] for v in value)
    mine = pick(first, top_half, low_half)
    sent = pick(first, low_half, top_half)
    got = tuple(partner(v, axis, 1, count) for v in sent)
    value = merge(pick(first, mine, got), pick(first, got, mine))
    step = 2
    while step < count:
        packed = pack_partial(value)
        got = unpack_partial(partner(packed, axis, step, count), value[0].shape[1])
        mine = unpack_partial(packed, value[0].shape[1])
        low_side = (here & step) == 0
        value = merge(pick(low_side, mine, got), pick(low_side, got, mine))
        step *= 2
    return value


def join_halves(value, axis, count):
    first = (lax.axis_index(axis) & 1) == 0
    got = partner(value, axis, 1, count)
    return jnp.where(first, jnp.concatenate([value, got]), jnp.concatenate([got, value]))


def fan_out(value, axis, count):
    here = lax.axis_index(axis)
    got = []
    for step in range(1, count):
        if count & (count - 1) == 0:
            pairs = [(i, i ^ step) for i in range(count)]
            source = here ^ step
        else:
            pairs = [(i, (i + step) % count) for i in range(count)]
            source = (here - step) % count
        got.append((source, lax.ppermute(value, axis, pairs)))
    return got


def row_kernel(q_ref, k_ref, v_ref, sk_ref, sv_ref, allow_ref, o_ref, *, scale):
    rows = q_ref.shape[1]
    allow = allow_ref[0] > 0.5
    allow = jnp.concatenate([allow, allow], axis=0)
    lane = lax.broadcasted_iota(jnp.int32, (1, 2 * HEAD_DIM), 1)
    low = lane < HEAD_DIM
    nt = (((1,), (1,)), ((), ()))
    for pair in range(HEADS // 2):
        cols = slice(pair * 2 * HEAD_DIM, (pair + 1) * 2 * HEAD_DIM)
        q = q_ref[0, :, cols] * scale
        zero = jnp.zeros_like(q)
        qh = jnp.concatenate([jnp.where(low, q, zero), jnp.where(low, zero, q)], axis=0)
        k = k_ref[0, :, cols]
        v = v_ref[0, :, cols]
        sk = sk_ref[:, cols]
        sv = sv_ref[:, cols]
        s = lax.dot_general(qh, k, nt, preferred_element_type=jnp.float32)
        s = jnp.where(allow, s, -1e30)
        ts = lax.dot_general(qh, sk, nt, preferred_element_type=jnp.float32)
        top = jnp.maximum(s.max(-1, keepdims=True), ts.max(-1, keepdims=True))
        e = jnp.exp(s - top)
        te = jnp.exp(ts - top)
        tot = e.sum(-1, keepdims=True) + te.sum(-1, keepdims=True)
        acc = jnp.dot(e.astype(jnp.bfloat16), v, preferred_element_type=jnp.float32)
        acc = acc + jnp.dot(te.astype(jnp.bfloat16), sv, preferred_element_type=jnp.float32)
        out = jnp.where(low, acc[:rows] / tot[:rows], acc[rows:] / tot[rows:])
        o_ref[0, :, cols] = out.astype(o_ref.dtype)


def row_attention(qkv, kv, summary_kv, allow):
    rows, nq, triple = qkv.shape
    width = triple // 3
    nk = kv.shape[1]
    ns = summary_kv.shape[0]
    kern = functools.partial(row_kernel, scale=HEAD_DIM ** (-0.5))
    return pl.pallas_call(
        kern,
        grid=(rows,),
        in_specs=[
            pl.BlockSpec((1, nq, width), lambda r: (r, 0, 0)),
            pl.BlockSpec((1, nk, width), lambda r: (r, 0, 0)),
            pl.BlockSpec((1, nk, width), lambda r: (r, 0, 1)),
            pl.BlockSpec((ns, width), lambda r: (0, 0)),
            pl.BlockSpec((ns, width), lambda r: (0, 1)),
            pl.BlockSpec((1, nq, nk), lambda r: (r, 0, 0)),
        ],
        out_specs=pl.BlockSpec((1, nq, width), lambda r: (r, 0, 0)),
        out_shape=jax.ShapeDtypeStruct((rows, nq, width), jnp.bfloat16),
    )(qkv, kv, kv, summary_kv, summary_kv, allow)


def local(cells, summary, owner, schema, w_qkv, w_out, gain_attn, w_up, w_down, gain_ffn, *, n_band, n_col):
    row_count, cols_dev, model_width = cells.shape
    own_group = lax.axis_index("col")
    own_band = lax.axis_index("band")
    score_scale = HEAD_DIM ** (-0.5)
    flat_cells = cells.reshape(row_count * cols_dev, model_width)
    w_kv = w_qkv[:, model_width:]

    tokens = broadcast_from(summary[0], "band", n_band, owner[0], cells)
    row_parts = fan_out(tokens[1], "col", n_col)
    tokens = tokens[0]

    qkv_cells = project(flat_cells, w_qkv).reshape(row_count, cols_dev, 3 * model_width)
    queries = qkv_cells[:, :, :model_width]
    own_keys = qkv_cells[:, :, model_width : 2 * model_width]
    own_vals = qkv_cells[:, :, 2 * model_width :]

    sum_queries = project(tokens, w_qkv[:, :model_width])
    summary_kv = project(tokens, w_kv)
    sum_keys = summary_kv[:, :model_width]
    sum_vals = summary_kv[:, model_width:]

    sq = sum_queries.astype(jnp.float32)
    col_scores = head_sum(sq[None] * own_keys.astype(jnp.float32)) * score_scale
    self_scores = head_sum(sq * sum_keys.astype(jnp.float32)) * score_scale
    part_top = col_scores.max(0)
    col_exp = jnp.exp(col_scores - part_top[None])
    col_weights = head_spread(col_exp.astype(jnp.bfloat16).astype(jnp.float32))
    part_mixed = (col_weights * own_vals.astype(jnp.float32)).sum(0)
    part_total = col_exp.sum(0)
    merged = half_merge(
        (part_mixed, jnp.concatenate([part_total, part_top], axis=-1)), "band", n_band
    )
    half = cols_dev // 2
    first = (own_band & 1) == 0
    half_self = jnp.where(first, self_scores[:half], self_scores[half:])
    half_vals = jnp.where(first, sum_vals[:half], sum_vals[half:]).astype(jnp.float32)
    col_top = jnp.maximum(merged[1][:, HEADS:], half_self)
    fade = jnp.exp(merged[1][:, HEADS:] - col_top)
    self_exp = jnp.exp(half_self - col_top)
    col_total = merged[1][:, :HEADS] * fade + self_exp
    col_mixed = merged[0] * head_spread(fade) + head_spread(
        self_exp.astype(jnp.bfloat16).astype(jnp.float32)
    ) * half_vals
    summary_att = (col_mixed / head_spread(col_total)).astype(jnp.bfloat16)
    summary_att = join_halves(summary_att, "band", n_band)

    sources = [own_group] + [s for s, _ in row_parts]
    row_cells = jnp.concatenate([cells] + [got for _, got in row_parts], axis=1)
    width_now = row_cells.shape[1]
    row_kv = project(row_cells.reshape(row_count * width_now, model_width), w_kv)
    row_kv = row_kv.reshape(row_count, width_now, 2 * model_width)
    key_groups = jnp.concatenate(
        [jnp.full((cols_dev,), s, jnp.int32) for s in sources]
    )
    own_block = jnp.arange(width_now, dtype=jnp.int32) < cols_dev
    allowed = (jnp.right_shift(schema[:, :, None], key_groups[None, None, :]) & 1 == 1) | own_block[
        None, None, :
    ]
    attended = row_attention(qkv_cells, row_kv, summary_kv, allowed.astype(jnp.float32))
    attended = attended.reshape(row_count * cols_dev, model_width)

    all_in = jnp.concatenate([flat_cells, tokens], axis=0)
    all_att = jnp.concatenate([attended, summary_att], axis=0)
    all_out = finish(all_in, all_att, w_out, gain_attn, w_up, w_down, gain_ffn)
    cells_out = all_out[: row_count * cols_dev].reshape(row_count, cols_dev, model_width)
    summary_out = all_out[row_count * cols_dev :]
    return (cells_out, summary_out)


def solution(mesh):
    in_specs = (
        P("band", "col", None),
        P("band", "col", None),
        P("col"),
        P("band", "col"),
        P(),
        P(),
        P(),
        P(),
        P(),
        P(),
    )
    out_specs = (P("band", "col", None), P("col", None))
    body = functools.partial(local, n_band=mesh.shape["band"], n_col=mesh.shape["col"])
    return jax.shard_map(body, mesh=mesh, in_specs=in_specs, out_specs=out_specs, check_vma=False)
```

```python
import functools

import jax
import jax.numpy as jnp
from jax import lax
from jax.experimental import pallas as pl
from jax.sharding import PartitionSpec as P

HEADS = 12
HEAD_DIM = 64


def spread_2(value, axis, source):
    kept = jnp.where(lax.axis_index(axis) == source, value, 0).astype(value.dtype)
    return lax.psum(kept, axis)


def layer_norm(values, gain_vec):
    center = values - jnp.mean(values, -1, keepdims=True)
    spread = jnp.mean(center * center, -1, keepdims=True)
    return center * lax.rsqrt(spread + 1e-05) * gain_vec


def finish(tokens_in, attended, w_out, gain_attn, w_up, w_down, gain_ffn):
    mixed_out = jnp.dot(attended, w_out, preferred_element_type=jnp.float32)
    hidden = layer_norm(tokens_in.astype(jnp.float32) + mixed_out, gain_attn).astype(jnp.bfloat16)
    inner_act = jax.nn.gelu(jnp.dot(hidden, w_up, preferred_element_type=jnp.float32)).astype(
        jnp.bfloat16
    )
    outer_out = jnp.dot(inner_act, w_down, preferred_element_type=jnp.float32)
    return layer_norm(hidden.astype(jnp.float32) + outer_out, gain_ffn).astype(jnp.bfloat16)


def project(values, weight):
    return jnp.dot(values, weight, preferred_element_type=jnp.float32).astype(jnp.bfloat16)


def head_matrix():
    lanes = jnp.arange(HEADS * HEAD_DIM, dtype=jnp.int32) // HEAD_DIM
    return (lanes[None, :] == jnp.arange(HEADS, dtype=jnp.int32)[:, None]).astype(jnp.float32)


def head_sum(values):
    dims = values.shape[:-1]
    flat = values.reshape(-1, values.shape[-1])
    out = jnp.dot(flat, head_matrix().T, precision=lax.Precision.HIGHEST,
                  preferred_element_type=jnp.float32)
    return out.reshape(dims + (HEADS,))


def head_spread(values):
    dims = values.shape[:-1]
    flat = values.reshape(-1, HEADS)
    out = jnp.dot(flat, head_matrix(), precision=lax.Precision.HIGHEST,
                  preferred_element_type=jnp.float32)
    return out.reshape(dims + (HEADS * HEAD_DIM,))


def partner(value, axis, step, count):
    return lax.ppermute(value, axis, [(i, i ^ step) for i in range(count)])


def broadcast_from(value, axis, count, source, held):
    here = lax.axis_index(axis)
    step = 1
    while step < count:
        got = partner(value, axis, step, count)
        if step == 1:
            got, held = lax.optimization_barrier((got, held))
        value = jnp.where(here // step == source // step, value, got)
        step *= 2
    return value, held


def merge(lo, hi):
    top = jnp.maximum(lo[1][:, HEADS:], hi[1][:, HEADS:])
    fade_lo = jnp.exp(lo[1][:, HEADS:] - top)
    fade_hi = jnp.exp(hi[1][:, HEADS:] - top)
    total = lo[1][:, :HEADS] * fade_lo + hi[1][:, :HEADS] * fade_hi
    mixed = lo[0] * head_spread(fade_lo) + hi[0] * head_spread(fade_hi)
    return mixed, jnp.concatenate([total, top], axis=-1)


def pick(flag, a, b):
    return tuple(jnp.where(flag, x, y) for x, y in zip(a, b))


def pack_partial(value):
    stats = value[1]
    high = lax.optimization_barrier(stats.astype(jnp.bfloat16))
    rest = stats - high.astype(jnp.float32)
    middle = lax.optimization_barrier(rest.astype(jnp.bfloat16))
    low = (rest - middle.astype(jnp.float32)).astype(jnp.bfloat16)
    packed = jnp.concatenate([value[0].astype(jnp.bfloat16), high, middle, low], axis=-1)
    return lax.optimization_barrier(packed)


def unpack_partial(packed, width):
    part = packed.astype(jnp.float32)
    n = (packed.shape[1] - width) // 3
    stats = (part[:, width : width + n] + part[:, width + n : width + 2 * n]) + part[:, width + 2 * n :]
    return part[:, :width], stats


def half_merge(value, axis, count):
    here = lax.axis_index(axis)
    half = value[0].shape[0] // 2
    first = (here & 1) == 0
    top_half = tuple(v[:half] for v in value)
    low_half = tuple(v[half:] for v in value)
    mine = pick(first, top_half, low_half)
    sent = pick(first, low_half, top_half)
    got = tuple(partner(v, axis, 1, count) for v in sent)
    value = merge(pick(first, mine, got), pick(first, got, mine))
    step = 2
    while step < count:
        packed = pack_partial(value)
        got = unpack_partial(partner(packed, axis, step, count), value[0].shape[1])
        mine = unpack_partial(packed, value[0].shape[1])
        low_side = (here & step) == 0
        value = merge(pick(low_side, mine, got), pick(low_side, got, mine))
        step *= 2
    return value


def join_halves(value, axis, count):
    first = (lax.axis_index(axis) & 1) == 0
    got = partner(value, axis, 1, count)
    return jnp.where(first, jnp.concatenate([value, got]), jnp.concatenate([got, value]))


def fan_out(value, axis, count):
    here = lax.axis_index(axis)
    got = []
    for step in range(1, count):
        if count & (count - 1) == 0:
            pairs = [(i, i ^ step) for i in range(count)]
            source = here ^ step
        else:
            pairs = [(i, (i + step) % count) for i in range(count)]
            source = (here - step) % count
        got.append((source, lax.ppermute(value, axis, pairs)))
    return got


def row_kernel(q_ref, k_ref, v_ref, sk_ref, sv_ref, allow_ref, o_ref, *, scale):
    rows = q_ref.shape[1]
    allow = allow_ref[0] > 0.5
    allow = jnp.concatenate([allow, allow], axis=0)
    lane = lax.broadcasted_iota(jnp.int32, (1, 2 * HEAD_DIM), 1)
    low = lane < HEAD_DIM
    nt = (((1,), (1,)), ((), ()))
    for pair in range(HEADS // 2):
        cols = slice(pair * 2 * HEAD_DIM, (pair + 1) * 2 * HEAD_DIM)
        q = q_ref[0, :, cols] * scale
        zero = jnp.zeros_like(q)
        qh = jnp.concatenate([jnp.where(low, q, zero), jnp.where(low, zero, q)], axis=0)
        k = k_ref[0, :, cols]
        v = v_ref[0, :, cols]
        sk = sk_ref[:, cols]
        sv = sv_ref[:, cols]
        s = lax.dot_general(qh, k, nt, preferred_element_type=jnp.float32)
        s = jnp.where(allow, s, -1e30)
        ts = lax.dot_general(qh, sk, nt, preferred_element_type=jnp.float32)
        top = jnp.maximum(s.max(-1, keepdims=True), ts.max(-1, keepdims=True))
        e = jnp.exp(s - top)
        te = jnp.exp(ts - top)
        tot = e.sum(-1, keepdims=True) + te.sum(-1, keepdims=True)
        acc = jnp.dot(e.astype(jnp.bfloat16), v, preferred_element_type=jnp.float32)
        acc = acc + jnp.dot(te.astype(jnp.bfloat16), sv, preferred_element_type=jnp.float32)
        out = jnp.where(low, acc[:rows] / tot[:rows], acc[rows:] / tot[rows:])
        o_ref[0, :, cols] = out.astype(o_ref.dtype)


def row_attention(qkv, kv, summary_kv, allow):
    rows, nq, triple = qkv.shape
    width = triple // 3
    nk = kv.shape[1]
    ns = summary_kv.shape[0]
    kern = functools.partial(row_kernel, scale=HEAD_DIM ** (-0.5))
    return pl.pallas_call(
        kern,
        grid=(rows,),
        in_specs=[
            pl.BlockSpec((1, nq, width), lambda r: (r, 0, 0)),
            pl.BlockSpec((1, nk, width), lambda r: (r, 0, 0)),
            pl.BlockSpec((1, nk, width), lambda r: (r, 0, 1)),
            pl.BlockSpec((ns, width), lambda r: (0, 0)),
            pl.BlockSpec((ns, width), lambda r: (0, 1)),
            pl.BlockSpec((1, nq, nk), lambda r: (r, 0, 0)),
        ],
        out_specs=pl.BlockSpec((1, nq, width), lambda r: (r, 0, 0)),
        out_shape=jax.ShapeDtypeStruct((rows, nq, width), jnp.bfloat16),
    )(qkv, kv, kv, summary_kv, summary_kv, allow)


def local(cells, summary, owner, schema, w_qkv, w_out, gain_attn, w_up, w_down, gain_ffn, *, n_band, n_col):
    row_count, cols_dev, model_width = cells.shape
    own_group = lax.axis_index("col")
    own_band = lax.axis_index("band")
    score_scale = HEAD_DIM ** (-0.5)
    flat_cells = cells.reshape(row_count * cols_dev, model_width)
    w_kv = w_qkv[:, model_width:]

    tokens = broadcast_from(summary[0], "band", n_band, owner[0], cells)
    row_parts = fan_out(tokens[1], "col", n_col)
    tokens = tokens[0]

    qkv_cells = project(flat_cells, w_qkv).reshape(row_count, cols_dev, 3 * model_width)
    queries = qkv_cells[:, :, :model_width]
    own_keys = qkv_cells[:, :, model_width : 2 * model_width]
    own_vals = qkv_cells[:, :, 2 * model_width :]

    sum_queries = project(tokens, w_qkv[:, :model_width])
    summary_kv = project(tokens, w_kv)
    sum_keys = summary_kv[:, :model_width]
    sum_vals = summary_kv[:, model_width:]

    sq = sum_queries.astype(jnp.float32)
    col_scores = head_sum(sq[None] * own_keys.astype(jnp.float32)) * score_scale
    self_scores = head_sum(sq * sum_keys.astype(jnp.float32)) * score_scale
    part_top = col_scores.max(0)
    col_exp = jnp.exp(col_scores - part_top[None])
    col_weights = head_spread(lax.optimization_barrier(col_exp.astype(jnp.bfloat16)).astype(jnp.float32))
    part_mixed = (col_weights * own_vals.astype(jnp.float32)).sum(0)
    part_total = col_exp.sum(0)
    merged = half_merge(
        (part_mixed, jnp.concatenate([part_total, part_top], axis=-1)), "band", n_band
    )
    half = cols_dev // 2
    first = (own_band & 1) == 0
    half_self = jnp.where(first, self_scores[:half], self_scores[half:])
    half_vals = jnp.where(first, sum_vals[:half], sum_vals[half:]).astype(jnp.float32)
    col_top = jnp.maximum(merged[1][:, HEADS:], half_self)
    fade = jnp.exp(merged[1][:, HEADS:] - col_top)
    self_exp = jnp.exp(half_self - col_top)
    col_total = merged[1][:, :HEADS] * fade + self_exp
    col_mixed = merged[0] * head_spread(fade) + head_spread(
        lax.optimization_barrier(self_exp.astype(jnp.bfloat16)).astype(jnp.float32)
    ) * half_vals
    summary_att = (col_mixed / head_spread(col_total)).astype(jnp.bfloat16)
    summary_att = join_halves(summary_att, "band", n_band)

    sources = [own_group] + [s for s, _ in row_parts]
    row_cells = jnp.concatenate([cells] + [got for _, got in row_parts], axis=1)
    width_now = row_cells.shape[1]
    row_kv = project(row_cells.reshape(row_count * width_now, model_width), w_kv)
    row_kv = row_kv.reshape(row_count, width_now, 2 * model_width)
    key_groups = jnp.concatenate(
        [jnp.full((cols_dev,), s, jnp.int32) for s in sources]
    )
    own_block = jnp.arange(width_now, dtype=jnp.int32) < cols_dev
    allowed = (jnp.right_shift(schema[:, :, None], key_groups[None, None, :]) & 1 == 1) | own_block[
        None, None, :
    ]
    attended = row_attention(qkv_cells, row_kv, summary_kv, allowed.astype(jnp.float32))
    attended = attended.reshape(row_count * cols_dev, model_width)

    all_in = jnp.concatenate([flat_cells, tokens], axis=0)
    all_att = jnp.concatenate([attended, summary_att], axis=0)
    all_out = finish(all_in, all_att, w_out, gain_attn, w_up, w_down, gain_ffn)
    cells_out = all_out[: row_count * cols_dev].reshape(row_count, cols_dev, model_width)
    summary_out = all_out[row_count * cols_dev :]
    return (cells_out, summary_out)


def solution(mesh):
    in_specs = (
        P("band", "col", None),
        P("band", "col", None),
        P("col"),
        P("band", "col"),
        P(),
        P(),
        P(),
        P(),
        P(),
        P(),
    )
    out_specs = (P("band", "col", None), P("col", None))
    body = functools.partial(local, n_band=mesh.shape["band"], n_col=mesh.shape["col"])
    return jax.shard_map(body, mesh=mesh, in_specs=in_specs, out_specs=out_specs, check_vma=False)
```

```python
import functools

import jax
import jax.numpy as jnp
from jax import lax
from jax.experimental import pallas as pl
from jax.sharding import PartitionSpec as P

HEADS = 12
HEAD_DIM = 64


def spread_2(value, axis, source):
    kept = jnp.where(lax.axis_index(axis) == source, value, 0).astype(value.dtype)
    return lax.psum(kept, axis)


def layer_norm(values, gain_vec):
    center = values - jnp.mean(values, -1, keepdims=True)
    spread = jnp.mean(center * center, -1, keepdims=True)
    return center * lax.rsqrt(spread + 1e-05) * gain_vec


def finish(tokens_in, attended, w_out, gain_attn, w_up, w_down, gain_ffn):
    mixed_out = jnp.dot(attended, w_out, preferred_element_type=jnp.float32)
    hidden = layer_norm(tokens_in.astype(jnp.float32) + mixed_out, gain_attn).astype(jnp.bfloat16)
    inner_act = jax.nn.gelu(jnp.dot(hidden, w_up, preferred_element_type=jnp.float32)).astype(
        jnp.bfloat16
    )
    outer_out = jnp.dot(inner_act, w_down, preferred_element_type=jnp.float32)
    return hidden.astype(jnp.float32) + outer_out


def project(values, weight):
    return jnp.dot(values, weight, preferred_element_type=jnp.float32).astype(jnp.bfloat16)


def head_matrix():
    lanes = jnp.arange(HEADS * HEAD_DIM, dtype=jnp.int32) // HEAD_DIM
    return (lanes[None, :] == jnp.arange(HEADS, dtype=jnp.int32)[:, None]).astype(jnp.float32)


def head_sum(values):
    dims = values.shape[:-1]
    flat = values.reshape(-1, values.shape[-1])
    out = jnp.dot(flat, head_matrix().T, precision=lax.Precision.HIGHEST,
                  preferred_element_type=jnp.float32)
    return out.reshape(dims + (HEADS,))


def head_spread(values):
    dims = values.shape[:-1]
    flat = values.reshape(-1, HEADS)
    out = jnp.dot(flat, head_matrix(), precision=lax.Precision.HIGHEST,
                  preferred_element_type=jnp.float32)
    return out.reshape(dims + (HEADS * HEAD_DIM,))


def partner(value, axis, step, count):
    return lax.ppermute(value, axis, [(i, i ^ step) for i in range(count)])


def broadcast_from(value, axis, count, source, held):
    here = lax.axis_index(axis)
    step = 1
    while step < count:
        got = partner(value, axis, step, count)
        if step == 1:
            got, held = lax.optimization_barrier((got, held))
        value = jnp.where(here // step == source // step, value, got)
        step *= 2
    return value, held


def merge(lo, hi):
    top = jnp.maximum(lo[1][:, HEADS:], hi[1][:, HEADS:])
    fade_lo = jnp.exp(lo[1][:, HEADS:] - top)
    fade_hi = jnp.exp(hi[1][:, HEADS:] - top)
    total = lo[1][:, :HEADS] * fade_lo + hi[1][:, :HEADS] * fade_hi
    mixed = lo[0] * head_spread(fade_lo) + hi[0] * head_spread(fade_hi)
    return mixed, jnp.concatenate([total, top], axis=-1)


def pick(flag, a, b):
    return tuple(jnp.where(flag, x, y) for x, y in zip(a, b))


def pack_partial(value):
    stats = value[1]
    high = lax.optimization_barrier(stats.astype(jnp.bfloat16))
    rest = stats - high.astype(jnp.float32)
    middle = lax.optimization_barrier(rest.astype(jnp.bfloat16))
    low = (rest - middle.astype(jnp.float32)).astype(jnp.bfloat16)
    packed = jnp.concatenate([value[0].astype(jnp.bfloat16), high, middle, low], axis=-1)
    return lax.optimization_barrier(packed)


def unpack_partial(packed, width):
    part = packed.astype(jnp.float32)
    n = (packed.shape[1] - width) // 3
    stats = (part[:, width : width + n] + part[:, width + n : width + 2 * n]) + part[:, width + 2 * n :]
    return part[:, :width], stats


def half_merge(value, axis, count):
    here = lax.axis_index(axis)
    half = value[0].shape[0] // 2
    first = (here & 1) == 0
    top_half = tuple(v[:half] for v in value)
    low_half = tuple(v[half:] for v in value)
    mine = pick(first, top_half, low_half)
    sent = pick(first, low_half, top_half)
    got = tuple(partner(v, axis, 1, count) for v in sent)
    value = merge(pick(first, mine, got), pick(first, got, mine))
    step = 2
    while step < count:
        packed = pack_partial(value)
        got = unpack_partial(partner(packed, axis, step, count), value[0].shape[1])
        mine = unpack_partial(packed, value[0].shape[1])
        low_side = (here & step) == 0
        value = merge(pick(low_side, mine, got), pick(low_side, got, mine))
        step *= 2
    return value


def join_halves(value, axis, count):
    first = (lax.axis_index(axis) & 1) == 0
    got = partner(value, axis, 1, count)
    return jnp.where(first, jnp.concatenate([value, got]), jnp.concatenate([got, value]))


def fan_out(value, axis, count):
    here = lax.axis_index(axis)
    got = []
    for step in range(1, count):
        if count & (count - 1) == 0:
            pairs = [(i, i ^ step) for i in range(count)]
            source = here ^ step
        else:
            pairs = [(i, (i + step) % count) for i in range(count)]
            source = (here - step) % count
        got.append((source, lax.ppermute(value, axis, pairs)))
    return got


def row_kernel(q_ref, k_ref, v_ref, sk_ref, sv_ref, allow_ref, o_ref, *, scale):
    rows = q_ref.shape[1]
    allow = allow_ref[0] > 0.5
    allow = jnp.concatenate([allow, allow], axis=0)
    lane = lax.broadcasted_iota(jnp.int32, (1, 2 * HEAD_DIM), 1)
    low = lane < HEAD_DIM
    nt = (((1,), (1,)), ((), ()))
    for pair in range(HEADS // 2):
        cols = slice(pair * 2 * HEAD_DIM, (pair + 1) * 2 * HEAD_DIM)
        q = q_ref[0, :, cols] * scale
        zero = jnp.zeros_like(q)
        qh = jnp.concatenate([jnp.where(low, q, zero), jnp.where(low, zero, q)], axis=0)
        k = k_ref[0, :, cols]
        v = v_ref[0, :, cols]
        sk = sk_ref[:, cols]
        sv = sv_ref[:, cols]
        s = lax.dot_general(qh, k, nt, preferred_element_type=jnp.float32)
        s = jnp.where(allow, s, -1e30)
        ts = lax.dot_general(qh, sk, nt, preferred_element_type=jnp.float32)
        top = jnp.maximum(s.max(-1, keepdims=True), ts.max(-1, keepdims=True))
        e = jnp.exp(s - top)
        te = jnp.exp(ts - top)
        tot = e.sum(-1, keepdims=True) + te.sum(-1, keepdims=True)
        acc = jnp.dot(e.astype(jnp.bfloat16), v, preferred_element_type=jnp.float32)
        acc = acc + jnp.dot(te.astype(jnp.bfloat16), sv, preferred_element_type=jnp.float32)
        out = jnp.where(low, acc[:rows] / tot[:rows], acc[rows:] / tot[rows:])
        o_ref[0, :, cols] = out.astype(o_ref.dtype)


def row_attention(qkv, kv, summary_kv, allow):
    rows, nq, triple = qkv.shape
    width = triple // 3
    nk = kv.shape[1]
    ns = summary_kv.shape[0]
    kern = functools.partial(row_kernel, scale=HEAD_DIM ** (-0.5))
    return pl.pallas_call(
        kern,
        grid=(rows,),
        in_specs=[
            pl.BlockSpec((1, nq, width), lambda r: (r, 0, 0)),
            pl.BlockSpec((1, nk, width), lambda r: (r, 0, 0)),
            pl.BlockSpec((1, nk, width), lambda r: (r, 0, 1)),
            pl.BlockSpec((ns, width), lambda r: (0, 0)),
            pl.BlockSpec((ns, width), lambda r: (0, 1)),
            pl.BlockSpec((1, nq, nk), lambda r: (r, 0, 0)),
        ],
        out_specs=pl.BlockSpec((1, nq, width), lambda r: (r, 0, 0)),
        out_shape=jax.ShapeDtypeStruct((rows, nq, width), jnp.bfloat16),
    )(qkv, kv, kv, summary_kv, summary_kv, allow)


def local(cells, summary, owner, schema, w_qkv, w_out, gain_attn, w_up, w_down, gain_ffn, *, n_band, n_col):
    row_count, cols_dev, model_width = cells.shape
    own_group = lax.axis_index("col")
    own_band = lax.axis_index("band")
    score_scale = HEAD_DIM ** (-0.5)
    flat_cells = cells.reshape(row_count * cols_dev, model_width)
    w_kv = w_qkv[:, model_width:]

    tokens = broadcast_from(summary[0], "band", n_band, owner[0], cells)
    row_parts = fan_out(tokens[1], "col", n_col)
    tokens = tokens[0]

    qkv_cells = project(flat_cells, w_qkv).reshape(row_count, cols_dev, 3 * model_width)
    queries = qkv_cells[:, :, :model_width]
    own_keys = qkv_cells[:, :, model_width : 2 * model_width]
    own_vals = qkv_cells[:, :, 2 * model_width :]

    sum_queries = project(tokens, w_qkv[:, :model_width])
    summary_kv = project(tokens, w_kv)
    sum_keys = summary_kv[:, :model_width]
    sum_vals = summary_kv[:, model_width:]

    sq = sum_queries.astype(jnp.float32)
    col_scores = head_sum(sq[None] * own_keys.astype(jnp.float32)) * score_scale
    self_scores = head_sum(sq * sum_keys.astype(jnp.float32)) * score_scale
    part_top = col_scores.max(0)
    col_exp = jnp.exp(col_scores - part_top[None])
    col_weights = head_spread(lax.optimization_barrier(col_exp.astype(jnp.bfloat16)).astype(jnp.float32))
    part_mixed = (col_weights * own_vals.astype(jnp.float32)).sum(0)
    part_total = col_exp.sum(0)
    merged = half_merge(
        (part_mixed, jnp.concatenate([part_total, part_top], axis=-1)), "band", n_band
    )
    half = cols_dev // 2
    first = (own_band & 1) == 0
    half_self = jnp.where(first, self_scores[:half], self_scores[half:])
    half_vals = jnp.where(first, sum_vals[:half], sum_vals[half:]).astype(jnp.float32)
    col_top = jnp.maximum(merged[1][:, HEADS:], half_self)
    fade = jnp.exp(merged[1][:, HEADS:] - col_top)
    self_exp = jnp.exp(half_self - col_top)
    col_total = merged[1][:, :HEADS] * fade + self_exp
    col_mixed = merged[0] * head_spread(fade) + head_spread(
        lax.optimization_barrier(self_exp.astype(jnp.bfloat16)).astype(jnp.float32)
    ) * half_vals
    summary_att = (col_mixed / head_spread(col_total)).astype(jnp.bfloat16)
    summary_att = join_halves(summary_att, "band", n_band)

    sources = [own_group] + [s for s, _ in row_parts]
    row_cells = jnp.concatenate([cells] + [got for _, got in row_parts], axis=1)
    width_now = row_cells.shape[1]
    row_kv = project(row_cells.reshape(row_count * width_now, model_width), w_kv)
    row_kv = row_kv.reshape(row_count, width_now, 2 * model_width)
    key_groups = jnp.concatenate(
        [jnp.full((cols_dev,), s, jnp.int32) for s in sources]
    )
    own_block = jnp.arange(width_now, dtype=jnp.int32) < cols_dev
    allowed = (jnp.right_shift(schema[:, :, None], key_groups[None, None, :]) & 1 == 1) | own_block[
        None, None, :
    ]
    attended = row_attention(qkv_cells, row_kv, summary_kv, allowed.astype(jnp.float32))
    attended = attended.reshape(row_count * cols_dev, model_width)

    all_in = jnp.concatenate([flat_cells, tokens], axis=0)
    all_att = jnp.concatenate([attended, summary_att], axis=0)
    all_out = finish(all_in, all_att, w_out, gain_attn, w_up, w_down, gain_ffn)
    cells_out = layer_norm(all_out[: row_count * cols_dev], gain_ffn).astype(jnp.bfloat16)
    cells_out = cells_out.reshape(row_count, cols_dev, model_width)
    summary_out = layer_norm(all_out[row_count * cols_dev :], gain_ffn).astype(jnp.bfloat16)
    return (cells_out, summary_out)


def solution(mesh):
    in_specs = (
        P("band", "col", None),
        P("band", "col", None),
        P("col"),
        P("band", "col"),
        P(),
        P(),
        P(),
        P(),
        P(),
        P(),
    )
    out_specs = (P("band", "col", None), P("col", None))
    body = functools.partial(local, n_band=mesh.shape["band"], n_col=mesh.shape["col"])
    return jax.shard_map(body, mesh=mesh, in_specs=in_specs, out_specs=out_specs, check_vma=False)
```

```python
import functools

import jax
import jax.numpy as jnp
from jax import lax
from jax.experimental import pallas as pl
from jax.sharding import PartitionSpec as P

HEADS = 12
HEAD_DIM = 64


def spread_2(value, axis, source):
    kept = jnp.where(lax.axis_index(axis) == source, value, 0).astype(value.dtype)
    return lax.psum(kept, axis)


def layer_norm(values, gain_vec):
    center = values - jnp.mean(values, -1, keepdims=True)
    spread = jnp.mean(center * center, -1, keepdims=True)
    return center * lax.rsqrt(spread + 1e-05) * gain_vec


def finish(tokens_in, attended, w_out, gain_attn, w_up, w_down, gain_ffn):
    mixed_out = jnp.dot(attended, w_out, preferred_element_type=jnp.float32)
    hidden = layer_norm(tokens_in.astype(jnp.float32) + mixed_out, gain_attn).astype(jnp.bfloat16)
    inner_act = jax.nn.gelu(jnp.dot(hidden, w_up, preferred_element_type=jnp.float32)).astype(
        jnp.bfloat16
    )
    outer_out = jnp.dot(inner_act, w_down, preferred_element_type=jnp.float32)
    return layer_norm(hidden.astype(jnp.float32) + outer_out, gain_ffn).astype(jnp.bfloat16)


def project(values, weight):
    return jnp.dot(values, weight, preferred_element_type=jnp.float32).astype(jnp.bfloat16)


def head_matrix():
    lanes = jnp.arange(HEADS * HEAD_DIM, dtype=jnp.int32) // HEAD_DIM
    return (lanes[None, :] == jnp.arange(HEADS, dtype=jnp.int32)[:, None]).astype(jnp.float32)


def head_sum(values):
    dims = values.shape[:-1]
    flat = values.reshape(-1, values.shape[-1])
    out = jnp.dot(flat, head_matrix().T, precision=lax.Precision.HIGHEST,
                  preferred_element_type=jnp.float32)
    return out.reshape(dims + (HEADS,))


def head_spread(values):
    dims = values.shape[:-1]
    flat = values.reshape(-1, HEADS)
    out = jnp.dot(flat, head_matrix(), precision=lax.Precision.HIGHEST,
                  preferred_element_type=jnp.float32)
    return out.reshape(dims + (HEADS * HEAD_DIM,))


def partner(value, axis, step, count):
    return lax.ppermute(value, axis, [(i, i ^ step) for i in range(count)])


def broadcast_from(value, axis, count, source, held):
    here = lax.axis_index(axis)
    step = 1
    while step < count:
        got = partner(value, axis, step, count)
        if step == 1:
            got, held = lax.optimization_barrier((got, held))
        value = jnp.where(here // step == source // step, value, got)
        step *= 2
    return value, held


def merge(lo, hi):
    top = jnp.maximum(lo[1][:, HEADS:], hi[1][:, HEADS:])
    fade_lo = jnp.exp(lo[1][:, HEADS:] - top)
    fade_hi = jnp.exp(hi[1][:, HEADS:] - top)
    total = lo[1][:, :HEADS] * fade_lo + hi[1][:, :HEADS] * fade_hi
    mixed = lo[0] * head_spread(fade_lo) + hi[0] * head_spread(fade_hi)
    return mixed, jnp.concatenate([total, top], axis=-1)


def pick(flag, a, b):
    return tuple(jnp.where(flag, x, y) for x, y in zip(a, b))


def pack_partial(value):
    stats = value[1]
    high = lax.optimization_barrier(stats.astype(jnp.bfloat16))
    rest = stats - high.astype(jnp.float32)
    middle = lax.optimization_barrier(rest.astype(jnp.bfloat16))
    low = (rest - middle.astype(jnp.float32)).astype(jnp.bfloat16)
    packed = jnp.concatenate([value[0].astype(jnp.bfloat16), high, middle, low], axis=-1)
    return lax.optimization_barrier(packed)


def unpack_partial(packed, width):
    part = packed.astype(jnp.float32)
    n = (packed.shape[1] - width) // 3
    stats = (part[:, width : width + n] + part[:, width + n : width + 2 * n]) + part[:, width + 2 * n :]
    return part[:, :width], stats


def half_merge(value, axis, count, rider):
    here = lax.axis_index(axis)
    half = value[0].shape[0] // 2
    first = (here & 1) == 0
    top_half = tuple(v[:half] for v in value)
    low_half = tuple(v[half:] for v in value)
    mine = pick(first, top_half, low_half)
    sent = pick(first, low_half, top_half)
    got = tuple(partner(v, axis, 1, count) for v in sent)
    value = merge(pick(first, mine, got), pick(first, got, mine))
    step = 2
    while step < count:
        packed = pack_partial(value)
        got = partner(packed, axis, step, count)
        if step * 2 >= count:
            got, rider = lax.optimization_barrier((got, rider))
        got = unpack_partial(got, value[0].shape[1])
        mine = unpack_partial(packed, value[0].shape[1])
        low_side = (here & step) == 0
        value = merge(pick(low_side, mine, got), pick(low_side, got, mine))
        step *= 2
    return value, rider


def join_halves(value, axis, count):
    first = (lax.axis_index(axis) & 1) == 0
    got = partner(value, axis, 1, count)
    return jnp.where(first, jnp.concatenate([value, got]), jnp.concatenate([got, value]))


def fan_out(value, axis, count):
    here = lax.axis_index(axis)
    got = []
    for step in range(1, count):
        if count & (count - 1) == 0:
            pairs = [(i, i ^ step) for i in range(count)]
            source = here ^ step
        else:
            pairs = [(i, (i + step) % count) for i in range(count)]
            source = (here - step) % count
        got.append((source, lax.ppermute(value, axis, pairs)))
    return got


def row_kernel(q_ref, k_ref, v_ref, sk_ref, sv_ref, allow_ref, o_ref, *, scale):
    rows = q_ref.shape[1]
    allow = allow_ref[0] > 0.5
    allow = jnp.concatenate([allow, allow], axis=0)
    lane = lax.broadcasted_iota(jnp.int32, (1, 2 * HEAD_DIM), 1)
    low = lane < HEAD_DIM
    nt = (((1,), (1,)), ((), ()))
    for pair in range(HEADS // 2):
        cols = slice(pair * 2 * HEAD_DIM, (pair + 1) * 2 * HEAD_DIM)
        q = q_ref[0, :, cols] * scale
        zero = jnp.zeros_like(q)
        qh = jnp.concatenate([jnp.where(low, q, zero), jnp.where(low, zero, q)], axis=0)
        k = k_ref[0, :, cols]
        v = v_ref[0, :, cols]
        sk = sk_ref[:, cols]
        sv = sv_ref[:, cols]
        s = lax.dot_general(qh, k, nt, preferred_element_type=jnp.float32)
        s = jnp.where(allow, s, -1e30)
        ts = lax.dot_general(qh, sk, nt, preferred_element_type=jnp.float32)
        top = jnp.maximum(s.max(-1, keepdims=True), ts.max(-1, keepdims=True))
        e = jnp.exp(s - top)
        te = jnp.exp(ts - top)
        tot = e.sum(-1, keepdims=True) + te.sum(-1, keepdims=True)
        acc = jnp.dot(e.astype(jnp.bfloat16), v, preferred_element_type=jnp.float32)
        acc = acc + jnp.dot(te.astype(jnp.bfloat16), sv, preferred_element_type=jnp.float32)
        out = jnp.where(low, acc[:rows] / tot[:rows], acc[rows:] / tot[rows:])
        o_ref[0, :, cols] = out.astype(o_ref.dtype)


def row_attention(qkv, kv, summary_kv, allow):
    rows, nq, triple = qkv.shape
    width = triple // 3
    nk = kv.shape[1]
    ns = summary_kv.shape[0]
    kern = functools.partial(row_kernel, scale=HEAD_DIM ** (-0.5))
    return pl.pallas_call(
        kern,
        grid=(rows,),
        in_specs=[
            pl.BlockSpec((1, nq, width), lambda r: (r, 0, 0)),
            pl.BlockSpec((1, nk, width), lambda r: (r, 0, 0)),
            pl.BlockSpec((1, nk, width), lambda r: (r, 0, 1)),
            pl.BlockSpec((ns, width), lambda r: (0, 0)),
            pl.BlockSpec((ns, width), lambda r: (0, 1)),
            pl.BlockSpec((1, nq, nk), lambda r: (r, 0, 0)),
        ],
        out_specs=pl.BlockSpec((1, nq, width), lambda r: (r, 0, 0)),
        out_shape=jax.ShapeDtypeStruct((rows, nq, width), jnp.bfloat16),
    )(qkv, kv, kv, summary_kv, summary_kv, allow)


def local(cells, summary, owner, schema, w_qkv, w_out, gain_attn, w_up, w_down, gain_ffn, *, n_band, n_col):
    row_count, cols_dev, model_width = cells.shape
    own_group = lax.axis_index("col")
    own_band = lax.axis_index("band")
    score_scale = HEAD_DIM ** (-0.5)
    flat_cells = cells.reshape(row_count * cols_dev, model_width)
    w_kv = w_qkv[:, model_width:]

    tokens = broadcast_from(summary[0], "band", n_band, owner[0], cells)
    row_parts = fan_out(tokens[1], "col", n_col)
    tokens = tokens[0]

    qkv_cells = project(flat_cells, w_qkv).reshape(row_count, cols_dev, 3 * model_width)
    queries = qkv_cells[:, :, :model_width]
    own_keys = qkv_cells[:, :, model_width : 2 * model_width]
    own_vals = qkv_cells[:, :, 2 * model_width :]

    sum_queries = project(tokens, w_qkv[:, :model_width])
    summary_kv = project(tokens, w_kv)
    sum_keys = summary_kv[:, :model_width]
    sum_vals = summary_kv[:, model_width:]

    sq = sum_queries.astype(jnp.float32)
    col_scores = head_sum(sq[None] * own_keys.astype(jnp.float32)) * score_scale
    self_scores = head_sum(sq * sum_keys.astype(jnp.float32)) * score_scale
    part_top = col_scores.max(0)
    col_exp = jnp.exp(col_scores - part_top[None])
    col_weights = head_spread(lax.optimization_barrier(col_exp.astype(jnp.bfloat16)).astype(jnp.float32))
    part_mixed = (col_weights * own_vals.astype(jnp.float32)).sum(0)
    part_total = col_exp.sum(0)
    row_cells = jnp.concatenate([cells] + [got for _, got in row_parts], axis=1)
    width_now = row_cells.shape[1]
    row_kv = project(row_cells.reshape(row_count * width_now, model_width), w_kv)
    row_kv = row_kv.reshape(row_count, width_now, 2 * model_width)
    merged, row_kv = half_merge(
        (part_mixed, jnp.concatenate([part_total, part_top], axis=-1)), "band", n_band, row_kv
    )
    half = cols_dev // 2
    first = (own_band & 1) == 0
    half_self = jnp.where(first, self_scores[:half], self_scores[half:])
    half_vals = jnp.where(first, sum_vals[:half], sum_vals[half:]).astype(jnp.float32)
    col_top = jnp.maximum(merged[1][:, HEADS:], half_self)
    fade = jnp.exp(merged[1][:, HEADS:] - col_top)
    self_exp = jnp.exp(half_self - col_top)
    col_total = merged[1][:, :HEADS] * fade + self_exp
    col_mixed = merged[0] * head_spread(fade) + head_spread(
        lax.optimization_barrier(self_exp.astype(jnp.bfloat16)).astype(jnp.float32)
    ) * half_vals
    summary_att = (col_mixed / head_spread(col_total)).astype(jnp.bfloat16)
    summary_att = join_halves(summary_att, "band", n_band)

    sources = [own_group] + [s for s, _ in row_parts]
    key_groups = jnp.concatenate(
        [jnp.full((cols_dev,), s, jnp.int32) for s in sources]
    )
    own_block = jnp.arange(width_now, dtype=jnp.int32) < cols_dev
    allowed = (jnp.right_shift(schema[:, :, None], key_groups[None, None, :]) & 1 == 1) | own_block[
        None, None, :
    ]
    attended = row_attention(qkv_cells, row_kv, summary_kv, allowed.astype(jnp.float32))
    attended = attended.reshape(row_count * cols_dev, model_width)

    all_in = jnp.concatenate([flat_cells, tokens], axis=0)
    all_att = jnp.concatenate([attended, summary_att], axis=0)
    all_out = finish(all_in, all_att, w_out, gain_attn, w_up, w_down, gain_ffn)
    cells_out = all_out[: row_count * cols_dev].reshape(row_count, cols_dev, model_width)
    summary_out = all_out[row_count * cols_dev :]
    return (cells_out, summary_out)


def solution(mesh):
    in_specs = (
        P("band", "col", None),
        P("band", "col", None),
        P("col"),
        P("band", "col"),
        P(),
        P(),
        P(),
        P(),
        P(),
        P(),
    )
    out_specs = (P("band", "col", None), P("col", None))
    body = functools.partial(local, n_band=mesh.shape["band"], n_col=mesh.shape["col"])
    return jax.shard_map(body, mesh=mesh, in_specs=in_specs, out_specs=out_specs, check_vma=False)
```

```python
import functools

import jax
import jax.numpy as jnp
from jax import lax
from jax.experimental import pallas as pl
from jax.sharding import PartitionSpec as P

HEADS = 12
HEAD_DIM = 64


def spread_2(value, axis, source):
    kept = jnp.where(lax.axis_index(axis) == source, value, 0).astype(value.dtype)
    return lax.psum(kept, axis)


def layer_norm(values, gain_vec):
    center = values - jnp.mean(values, -1, keepdims=True)
    spread = jnp.mean(center * center, -1, keepdims=True)
    return center * lax.rsqrt(spread + 1e-05) * gain_vec


def finish(tokens_in, attended, w_out, gain_attn, w_up, w_down, gain_ffn):
    mixed_out = jnp.dot(attended, w_out, preferred_element_type=jnp.float32)
    hidden = layer_norm(tokens_in.astype(jnp.float32) + mixed_out, gain_attn).astype(jnp.bfloat16)
    inner_act = jax.nn.gelu(jnp.dot(hidden, w_up, preferred_element_type=jnp.float32)).astype(
        jnp.bfloat16
    )
    outer_out = jnp.dot(inner_act, w_down, preferred_element_type=jnp.float32)
    return layer_norm(hidden.astype(jnp.float32) + outer_out, gain_ffn).astype(jnp.bfloat16)


def project(values, weight):
    return jnp.dot(values, weight, preferred_element_type=jnp.float32).astype(jnp.bfloat16)


def head_matrix():
    lanes = jnp.arange(HEADS * HEAD_DIM, dtype=jnp.int32) // HEAD_DIM
    return (lanes[None, :] == jnp.arange(HEADS, dtype=jnp.int32)[:, None]).astype(jnp.float32)


def head_sum(values):
    dims = values.shape[:-1]
    flat = values.reshape(-1, values.shape[-1])
    out = jnp.dot(flat, head_matrix().T, precision=lax.Precision.HIGHEST,
                  preferred_element_type=jnp.float32)
    return out.reshape(dims + (HEADS,))


def head_spread(values):
    dims = values.shape[:-1]
    flat = values.reshape(-1, HEADS)
    out = jnp.dot(flat, head_matrix(), precision=lax.Precision.HIGHEST,
                  preferred_element_type=jnp.float32)
    return out.reshape(dims + (HEADS * HEAD_DIM,))


def partner(value, axis, step, count):
    return lax.ppermute(value, axis, [(i, i ^ step) for i in range(count)])


def broadcast_from(value, axis, count, source, held):
    here = lax.axis_index(axis)
    step = 1
    while step < count:
        got = partner(value, axis, step, count)
        if step == 1:
            got, held = lax.optimization_barrier((got, held))
        value = jnp.where(here // step == source // step, value, got)
        step *= 2
    return value, held


def merge(lo, hi):
    top = jnp.maximum(lo[1][:, HEADS:], hi[1][:, HEADS:])
    fade_lo = jnp.exp(lo[1][:, HEADS:] - top)
    fade_hi = jnp.exp(hi[1][:, HEADS:] - top)
    total = lo[1][:, :HEADS] * fade_lo + hi[1][:, :HEADS] * fade_hi
    mixed = lo[0] * head_spread(fade_lo) + hi[0] * head_spread(fade_hi)
    return mixed, jnp.concatenate([total, top], axis=-1)


def pick(flag, a, b):
    return tuple(jnp.where(flag, x, y) for x, y in zip(a, b))


def pack_partial(value):
    stats = value[1]
    high = lax.optimization_barrier(stats.astype(jnp.bfloat16))
    rest = stats - high.astype(jnp.float32)
    middle = lax.optimization_barrier(rest.astype(jnp.bfloat16))
    low = (rest - middle.astype(jnp.float32)).astype(jnp.bfloat16)
    packed = jnp.concatenate([value[0].astype(jnp.bfloat16), high, middle, low], axis=-1)
    return lax.optimization_barrier(packed)


def unpack_partial(packed, width):
    part = packed.astype(jnp.float32)
    n = (packed.shape[1] - width) // 3
    stats = (part[:, width : width + n] + part[:, width + n : width + 2 * n]) + part[:, width + 2 * n :]
    return part[:, :width], stats


def half_merge(value, axis, count, rider):
    here = lax.axis_index(axis)
    half = value[0].shape[0] // 2
    first = (here & 1) == 0
    top_half = tuple(v[:half] for v in value)
    low_half = tuple(v[half:] for v in value)
    mine = pick(first, top_half, low_half)
    sent = pick(first, low_half, top_half)
    got = tuple(partner(v, axis, 1, count) for v in sent)
    value = merge(pick(first, mine, got), pick(first, got, mine))
    step = 2
    while step < count:
        packed = pack_partial(value)
        got = partner(packed, axis, step, count)
        if step * 2 >= count:
            got, rider = lax.optimization_barrier((got, rider))
        got = unpack_partial(got, value[0].shape[1])
        mine = unpack_partial(packed, value[0].shape[1])
        low_side = (here & step) == 0
        value = merge(pick(low_side, mine, got), pick(low_side, got, mine))
        step *= 2
    return value, rider


def join_halves(value, axis, count):
    first = (lax.axis_index(axis) & 1) == 0
    got = partner(value, axis, 1, count)
    return jnp.where(first, jnp.concatenate([value, got]), jnp.concatenate([got, value]))


def fan_out(value, axis, count):
    here = lax.axis_index(axis)
    got = []
    for step in range(1, count):
        if count & (count - 1) == 0:
            pairs = [(i, i ^ step) for i in range(count)]
            source = here ^ step
        else:
            pairs = [(i, (i + step) % count) for i in range(count)]
            source = (here - step) % count
        got.append((source, lax.ppermute(value, axis, pairs)))
    return got


def row_kernel(q_ref, k_ref, v_ref, sk_ref, sv_ref, allow_ref, o_ref, *, scale):
    rows = q_ref.shape[1]
    allow = allow_ref[0] > 0.5
    allow = jnp.concatenate([allow, allow], axis=0)
    lane = lax.broadcasted_iota(jnp.int32, (1, 2 * HEAD_DIM), 1)
    low = lane < HEAD_DIM
    nt = (((1,), (1,)), ((), ()))
    for pair in range(HEADS // 2):
        cols = slice(pair * 2 * HEAD_DIM, (pair + 1) * 2 * HEAD_DIM)
        q = q_ref[0, :, cols] * scale
        zero = jnp.zeros_like(q)
        qh = jnp.concatenate([jnp.where(low, q, zero), jnp.where(low, zero, q)], axis=0)
        k = k_ref[0, :, cols]
        v = v_ref[0, :, cols]
        sk = sk_ref[:, cols]
        sv = sv_ref[:, cols]
        s = lax.dot_general(qh, k, nt, preferred_element_type=jnp.float32)
        s = jnp.where(allow, s, -1e30)
        ts = lax.dot_general(qh, sk, nt, preferred_element_type=jnp.float32)
        top = jnp.maximum(s.max(-1, keepdims=True), ts.max(-1, keepdims=True))
        e = jnp.exp(s - top)
        te = jnp.exp(ts - top)
        tot = e.sum(-1, keepdims=True) + te.sum(-1, keepdims=True)
        acc = jnp.dot(e.astype(jnp.bfloat16), v, preferred_element_type=jnp.float32)
        acc = acc + jnp.dot(te.astype(jnp.bfloat16), sv, preferred_element_type=jnp.float32)
        out = jnp.where(low, acc[:rows] / tot[:rows], acc[rows:] / tot[rows:])
        o_ref[0, :, cols] = out.astype(o_ref.dtype)


def row_attention(qkv, kv, summary_kv, allow):
    rows, nq, triple = qkv.shape
    width = triple // 3
    nk = kv.shape[1]
    ns = summary_kv.shape[0]
    kern = functools.partial(row_kernel, scale=HEAD_DIM ** (-0.5))
    return pl.pallas_call(
        kern,
        grid=(rows,),
        in_specs=[
            pl.BlockSpec((1, nq, width), lambda r: (r, 0, 0)),
            pl.BlockSpec((1, nk, width), lambda r: (r, 0, 0)),
            pl.BlockSpec((1, nk, width), lambda r: (r, 0, 1)),
            pl.BlockSpec((ns, width), lambda r: (0, 0)),
            pl.BlockSpec((ns, width), lambda r: (0, 1)),
            pl.BlockSpec((1, nq, nk), lambda r: (r, 0, 0)),
        ],
        out_specs=pl.BlockSpec((1, nq, width), lambda r: (r, 0, 0)),
        out_shape=jax.ShapeDtypeStruct((rows, nq, width), jnp.bfloat16),
    )(qkv, kv, kv, summary_kv, summary_kv, allow)


def local(cells, summary, owner, schema, w_qkv, w_out, gain_attn, w_up, w_down, gain_ffn, *, n_band, n_col):
    row_count, cols_dev, model_width = cells.shape
    own_group = lax.axis_index("col")
    own_band = lax.axis_index("band")
    score_scale = HEAD_DIM ** (-0.5)
    flat_cells = cells.reshape(row_count * cols_dev, model_width)
    w_kv = w_qkv[:, model_width:]

    key_sources = [own_group] + [own_group ^ step for step in range(1, n_col)]
    key_groups = jnp.concatenate(
        [jnp.full((cols_dev,), s, jnp.int32) for s in key_sources]
    )
    own_block = jnp.arange(n_col * cols_dev, dtype=jnp.int32) < cols_dev
    allowed = (jnp.right_shift(schema[:, :, None], key_groups[None, None, :]) & 1 == 1) | own_block[
        None, None, :
    ]
    allowed = allowed.astype(jnp.float32)
    tokens = broadcast_from(summary[0], "band", n_band, owner[0], (cells, allowed))
    held_cells, allowed = tokens[1]
    row_parts = fan_out(held_cells, "col", n_col)
    tokens = tokens[0]

    qkv_cells = project(flat_cells, w_qkv).reshape(row_count, cols_dev, 3 * model_width)
    queries = qkv_cells[:, :, :model_width]
    own_keys = qkv_cells[:, :, model_width : 2 * model_width]
    own_vals = qkv_cells[:, :, 2 * model_width :]

    sum_queries = project(tokens, w_qkv[:, :model_width])
    summary_kv = project(tokens, w_kv)
    sum_keys = summary_kv[:, :model_width]
    sum_vals = summary_kv[:, model_width:]

    sq = sum_queries.astype(jnp.float32)
    col_scores = head_sum(sq[None] * own_keys.astype(jnp.float32)) * score_scale
    self_scores = head_sum(sq * sum_keys.astype(jnp.float32)) * score_scale
    part_top = col_scores.max(0)
    col_exp = jnp.exp(col_scores - part_top[None])
    col_weights = head_spread(lax.optimization_barrier(col_exp.astype(jnp.bfloat16)).astype(jnp.float32))
    part_mixed = (col_weights * own_vals.astype(jnp.float32)).sum(0)
    part_total = col_exp.sum(0)
    row_cells = jnp.concatenate([cells] + [got for _, got in row_parts], axis=1)
    width_now = row_cells.shape[1]
    row_kv = project(row_cells.reshape(row_count * width_now, model_width), w_kv)
    row_kv = row_kv.reshape(row_count, width_now, 2 * model_width)
    merged, row_kv = half_merge(
        (part_mixed, jnp.concatenate([part_total, part_top], axis=-1)), "band", n_band, row_kv
    )
    half = cols_dev // 2
    first = (own_band & 1) == 0
    half_self = jnp.where(first, self_scores[:half], self_scores[half:])
    half_vals = jnp.where(first, sum_vals[:half], sum_vals[half:]).astype(jnp.float32)
    col_top = jnp.maximum(merged[1][:, HEADS:], half_self)
    fade = jnp.exp(merged[1][:, HEADS:] - col_top)
    self_exp = jnp.exp(half_self - col_top)
    col_total = merged[1][:, :HEADS] * fade + self_exp
    col_mixed = merged[0] * head_spread(fade) + head_spread(
        lax.optimization_barrier(self_exp.astype(jnp.bfloat16)).astype(jnp.float32)
    ) * half_vals
    summary_att = (col_mixed / head_spread(col_total)).astype(jnp.bfloat16)
    summary_att = join_halves(summary_att, "band", n_band)

    sources = [own_group] + [s for s, _ in row_parts]
    attended = row_attention(qkv_cells, row_kv, summary_kv, allowed)
    attended = attended.reshape(row_count * cols_dev, model_width)

    all_in = jnp.concatenate([flat_cells, tokens], axis=0)
    all_att = jnp.concatenate([attended, summary_att], axis=0)
    all_out = finish(all_in, all_att, w_out, gain_attn, w_up, w_down, gain_ffn)
    cells_out = all_out[: row_count * cols_dev].reshape(row_count, cols_dev, model_width)
    summary_out = all_out[row_count * cols_dev :]
    return (cells_out, summary_out)


def solution(mesh):
    in_specs = (
        P("band", "col", None),
        P("band", "col", None),
        P("col"),
        P("band", "col"),
        P(),
        P(),
        P(),
        P(),
        P(),
        P(),
    )
    out_specs = (P("band", "col", None), P("col", None))
    body = functools.partial(local, n_band=mesh.shape["band"], n_col=mesh.shape["col"])
    return jax.shard_map(body, mesh=mesh, in_specs=in_specs, out_specs=out_specs, check_vma=False)
```

```python
import functools

import jax
import jax.numpy as jnp
from jax import lax
from jax.experimental import pallas as pl
from jax.sharding import PartitionSpec as P

HEADS = 12
HEAD_DIM = 64


def spread_2(value, axis, source):
    kept = jnp.where(lax.axis_index(axis) == source, value, 0).astype(value.dtype)
    return lax.psum(kept, axis)


def layer_norm(values, gain_vec):
    center = values - jnp.mean(values, -1, keepdims=True)
    spread = jnp.mean(center * center, -1, keepdims=True)
    return center * lax.rsqrt(spread + 1e-05) * gain_vec


def finish(tokens_in, attended, w_out, gain_attn, w_up, w_down, gain_ffn):
    mixed_out = jnp.dot(attended, w_out, preferred_element_type=jnp.float32)
    hidden = layer_norm(tokens_in.astype(jnp.float32) + mixed_out, gain_attn).astype(jnp.bfloat16)
    inner_act = jax.nn.gelu(jnp.dot(hidden, w_up, preferred_element_type=jnp.float32)).astype(
        jnp.bfloat16
    )
    outer_out = jnp.dot(inner_act, w_down, preferred_element_type=jnp.float32)
    return layer_norm(hidden.astype(jnp.float32) + outer_out, gain_ffn).astype(jnp.bfloat16)


def project(values, weight):
    return jnp.dot(values, weight, preferred_element_type=jnp.float32).astype(jnp.bfloat16)


def head_matrix():
    lanes = jnp.arange(HEADS * HEAD_DIM, dtype=jnp.int32) // HEAD_DIM
    return (lanes[None, :] == jnp.arange(HEADS, dtype=jnp.int32)[:, None]).astype(jnp.float32)


def head_sum(values):
    dims = values.shape[:-1]
    flat = values.reshape(-1, values.shape[-1])
    out = jnp.dot(flat, head_matrix().T, precision=lax.Precision.HIGHEST,
                  preferred_element_type=jnp.float32)
    return out.reshape(dims + (HEADS,))


def head_spread(values):
    dims = values.shape[:-1]
    flat = values.reshape(-1, HEADS)
    out = jnp.dot(flat, head_matrix(), precision=lax.Precision.HIGHEST,
                  preferred_element_type=jnp.float32)
    return out.reshape(dims + (HEADS * HEAD_DIM,))


def partner(value, axis, step, count):
    return lax.ppermute(value, axis, [(i, i ^ step) for i in range(count)])


def broadcast_from(value, axis, count, source, held):
    here = lax.axis_index(axis)
    step = 1
    while step < count:
        got = partner(value, axis, step, count)
        if step == 1:
            got, held = lax.optimization_barrier((got, held))
        value = jnp.where(here // step == source // step, value, got)
        step *= 2
    return value, held


def merge(lo, hi):
    top = jnp.maximum(lo[1][:, HEADS:], hi[1][:, HEADS:])
    fade_lo = jnp.exp(lo[1][:, HEADS:] - top)
    fade_hi = jnp.exp(hi[1][:, HEADS:] - top)
    total = lo[1][:, :HEADS] * fade_lo + hi[1][:, :HEADS] * fade_hi
    mixed = lo[0] * head_spread(fade_lo) + hi[0] * head_spread(fade_hi)
    return mixed, jnp.concatenate([total, top], axis=-1)


def pick(flag, a, b):
    return tuple(jnp.where(flag, x, y) for x, y in zip(a, b))


def pack_partial(value):
    stats = value[1]
    high = lax.optimization_barrier(stats.astype(jnp.bfloat16))
    rest = stats - high.astype(jnp.float32)
    middle = lax.optimization_barrier(rest.astype(jnp.bfloat16))
    low = (rest - middle.astype(jnp.float32)).astype(jnp.bfloat16)
    packed = jnp.concatenate([value[0].astype(jnp.bfloat16), high, middle, low], axis=-1)
    return lax.optimization_barrier(packed)


def unpack_partial(packed, width):
    part = packed.astype(jnp.float32)
    n = (packed.shape[1] - width) // 3
    stats = (part[:, width : width + n] + part[:, width + n : width + 2 * n]) + part[:, width + 2 * n :]
    return part[:, :width], stats


def half_merge(value, axis, count, rider):
    here = lax.axis_index(axis)
    half = value[0].shape[0] // 2
    first = (here & 1) == 0
    top_half = tuple(v[:half] for v in value)
    low_half = tuple(v[half:] for v in value)
    mine = pick(first, top_half, low_half)
    sent = pick(first, low_half, top_half)
    got = tuple(partner(v, axis, 1, count) for v in sent)
    value = merge(pick(first, mine, got), pick(first, got, mine))
    step = 2
    while step < count:
        packed = pack_partial(value)
        got = partner(packed, axis, step, count)
        if step * 2 >= count:
            got, rider = lax.optimization_barrier((got, rider))
        got = unpack_partial(got, value[0].shape[1])
        mine = unpack_partial(packed, value[0].shape[1])
        low_side = (here & step) == 0
        value = merge(pick(low_side, mine, got), pick(low_side, got, mine))
        step *= 2
    return value, rider


def join_halves(value, axis, count):
    first = (lax.axis_index(axis) & 1) == 0
    got = partner(value, axis, 1, count)
    return jnp.where(first, jnp.concatenate([value, got]), jnp.concatenate([got, value]))


def fan_out(value, axis, count):
    here = lax.axis_index(axis)
    got = []
    for step in range(1, count):
        if count & (count - 1) == 0:
            pairs = [(i, i ^ step) for i in range(count)]
            source = here ^ step
        else:
            pairs = [(i, (i + step) % count) for i in range(count)]
            source = (here - step) % count
        got.append((source, lax.ppermute(value, axis, pairs)))
    return got


def row_kernel(q_ref, k_ref, v_ref, sk_ref, sv_ref, allow_ref, o_ref, *, scale):
    rows = q_ref.shape[1]
    allow = allow_ref[0] > 0.5
    allow = jnp.concatenate([allow, allow], axis=0)
    lane = lax.broadcasted_iota(jnp.int32, (1, 2 * HEAD_DIM), 1)
    low = lane < HEAD_DIM
    nt = (((1,), (1,)), ((), ()))
    for pair in range(HEADS // 2):
        cols = slice(pair * 2 * HEAD_DIM, (pair + 1) * 2 * HEAD_DIM)
        q = q_ref[0, :, cols] * scale
        zero = jnp.zeros_like(q)
        qh = jnp.concatenate([jnp.where(low, q, zero), jnp.where(low, zero, q)], axis=0)
        k = k_ref[0, :, cols]
        v = v_ref[0, :, cols]
        sk = sk_ref[:, cols]
        sv = sv_ref[:, cols]
        s = lax.dot_general(qh, k, nt, preferred_element_type=jnp.float32)
        s = jnp.where(allow, s, -1e30)
        ts = lax.dot_general(qh, sk, nt, preferred_element_type=jnp.float32)
        top = jnp.maximum(s.max(-1, keepdims=True), ts.max(-1, keepdims=True))
        e = jnp.exp(s - top)
        te = jnp.exp(ts - top)
        tot = e.sum(-1, keepdims=True) + te.sum(-1, keepdims=True)
        acc = jnp.dot(e.astype(jnp.bfloat16), v, preferred_element_type=jnp.float32)
        acc = acc + jnp.dot(te.astype(jnp.bfloat16), sv, preferred_element_type=jnp.float32)
        out = jnp.where(low, acc[:rows] / tot[:rows], acc[rows:] / tot[rows:])
        o_ref[0, :, cols] = out.astype(o_ref.dtype)


def row_attention(qkv, kv, summary_kv, allow):
    rows, nq, triple = qkv.shape
    width = triple // 3
    nk = kv.shape[1]
    ns = summary_kv.shape[0]
    kern = functools.partial(row_kernel, scale=HEAD_DIM ** (-0.5))
    return pl.pallas_call(
        kern,
        grid=(rows,),
        in_specs=[
            pl.BlockSpec((1, nq, width), lambda r: (r, 0, 0)),
            pl.BlockSpec((1, nk, width), lambda r: (r, 0, 0)),
            pl.BlockSpec((1, nk, width), lambda r: (r, 0, 1)),
            pl.BlockSpec((ns, width), lambda r: (0, 0)),
            pl.BlockSpec((ns, width), lambda r: (0, 1)),
            pl.BlockSpec((1, nq, nk), lambda r: (r, 0, 0)),
        ],
        out_specs=pl.BlockSpec((1, nq, width), lambda r: (r, 0, 0)),
        out_shape=jax.ShapeDtypeStruct((rows, nq, width), jnp.bfloat16),
    )(qkv, kv, kv, summary_kv, summary_kv, allow)


def local(cells, summary, owner, schema, w_qkv, w_out, gain_attn, w_up, w_down, gain_ffn, *, n_band, n_col):
    row_count, cols_dev, model_width = cells.shape
    own_group = lax.axis_index("col")
    own_band = lax.axis_index("band")
    score_scale = HEAD_DIM ** (-0.5)
    flat_cells = cells.reshape(row_count * cols_dev, model_width)
    w_kv = w_qkv[:, model_width:]

    key_sources = [own_group] + [own_group ^ step for step in range(1, n_col)]
    key_groups = jnp.concatenate(
        [jnp.full((cols_dev,), s, jnp.int32) for s in key_sources]
    )
    own_block = jnp.arange(n_col * cols_dev, dtype=jnp.int32) < cols_dev
    allowed = (jnp.right_shift(schema[:, :, None], key_groups[None, None, :]) & 1 == 1) | own_block[
        None, None, :
    ]
    allowed = allowed.astype(jnp.float32)
    row_parts = fan_out(cells, "col", n_col)
    tokens = broadcast_from(summary[0], "band", n_band, owner[0], allowed)
    allowed = tokens[1]
    tokens = tokens[0]

    qkv_cells = project(flat_cells, w_qkv).reshape(row_count, cols_dev, 3 * model_width)
    queries = qkv_cells[:, :, :model_width]
    own_keys = qkv_cells[:, :, model_width : 2 * model_width]
    own_vals = qkv_cells[:, :, 2 * model_width :]

    sum_queries = project(tokens, w_qkv[:, :model_width])
    summary_kv = project(tokens, w_kv)
    sum_keys = summary_kv[:, :model_width]
    sum_vals = summary_kv[:, model_width:]

    sq = sum_queries.astype(jnp.float32)
    col_scores = head_sum(sq[None] * own_keys.astype(jnp.float32)) * score_scale
    self_scores = head_sum(sq * sum_keys.astype(jnp.float32)) * score_scale
    part_top = col_scores.max(0)
    col_exp = jnp.exp(col_scores - part_top[None])
    col_weights = head_spread(lax.optimization_barrier(col_exp.astype(jnp.bfloat16)).astype(jnp.float32))
    part_mixed = (col_weights * own_vals.astype(jnp.float32)).sum(0)
    part_total = col_exp.sum(0)
    row_cells = jnp.concatenate([cells] + [got for _, got in row_parts], axis=1)
    width_now = row_cells.shape[1]
    row_kv = project(row_cells.reshape(row_count * width_now, model_width), w_kv)
    row_kv = row_kv.reshape(row_count, width_now, 2 * model_width)
    merged, row_kv = half_merge(
        (part_mixed, jnp.concatenate([part_total, part_top], axis=-1)), "band", n_band, row_kv
    )
    half = cols_dev // 2
    first = (own_band & 1) == 0
    half_self = jnp.where(first, self_scores[:half], self_scores[half:])
    half_vals = jnp.where(first, sum_vals[:half], sum_vals[half:]).astype(jnp.float32)
    col_top = jnp.maximum(merged[1][:, HEADS:], half_self)
    fade = jnp.exp(merged[1][:, HEADS:] - col_top)
    self_exp = jnp.exp(half_self - col_top)
    col_total = merged[1][:, :HEADS] * fade + self_exp
    col_mixed = merged[0] * head_spread(fade) + head_spread(
        lax.optimization_barrier(self_exp.astype(jnp.bfloat16)).astype(jnp.float32)
    ) * half_vals
    summary_att = (col_mixed / head_spread(col_total)).astype(jnp.bfloat16)
    summary_att = join_halves(summary_att, "band", n_band)

    sources = [own_group] + [s for s, _ in row_parts]
    attended = row_attention(qkv_cells, row_kv, summary_kv, allowed)
    attended = attended.reshape(row_count * cols_dev, model_width)

    all_in = jnp.concatenate([flat_cells, tokens], axis=0)
    all_att = jnp.concatenate([attended, summary_att], axis=0)
    all_out = finish(all_in, all_att, w_out, gain_attn, w_up, w_down, gain_ffn)
    cells_out = all_out[: row_count * cols_dev].reshape(row_count, cols_dev, model_width)
    summary_out = all_out[row_count * cols_dev :]
    return (cells_out, summary_out)


def solution(mesh):
    in_specs = (
        P("band", "col", None),
        P("band", "col", None),
        P("col"),
        P("band", "col"),
        P(),
        P(),
        P(),
        P(),
        P(),
        P(),
    )
    out_specs = (P("band", "col", None), P("col", None))
    body = functools.partial(local, n_band=mesh.shape["band"], n_col=mesh.shape["col"])
    return jax.shard_map(body, mesh=mesh, in_specs=in_specs, out_specs=out_specs, check_vma=False)
```

```python
import functools

import jax
import jax.numpy as jnp
from jax import lax
from jax.experimental import pallas as pl
from jax.sharding import PartitionSpec as P

HEADS = 12
HEAD_DIM = 64


def spread_2(value, axis, source):
    kept = jnp.where(lax.axis_index(axis) == source, value, 0).astype(value.dtype)
    return lax.psum(kept, axis)


def layer_norm(values, gain_vec):
    center = values - jnp.mean(values, -1, keepdims=True)
    spread = jnp.mean(center * center, -1, keepdims=True)
    return center * lax.rsqrt(spread + 1e-05) * gain_vec


def finish(tokens_in, attended, w_out, gain_attn, w_up, w_down, gain_ffn):
    mixed_out = jnp.dot(attended, w_out, preferred_element_type=jnp.float32)
    hidden = layer_norm(tokens_in.astype(jnp.float32) + mixed_out, gain_attn).astype(jnp.bfloat16)
    inner_act = jax.nn.gelu(jnp.dot(hidden, w_up, preferred_element_type=jnp.float32)).astype(
        jnp.bfloat16
    )
    outer_out = jnp.dot(inner_act, w_down, preferred_element_type=jnp.float32)
    return layer_norm(hidden.astype(jnp.float32) + outer_out, gain_ffn).astype(jnp.bfloat16)


def project(values, weight):
    return jnp.dot(values, weight, preferred_element_type=jnp.float32).astype(jnp.bfloat16)


def head_matrix():
    lanes = jnp.arange(HEADS * HEAD_DIM, dtype=jnp.int32) // HEAD_DIM
    return (lanes[None, :] == jnp.arange(HEADS, dtype=jnp.int32)[:, None]).astype(jnp.float32)


def head_sum(values):
    dims = values.shape[:-1]
    flat = values.reshape(-1, values.shape[-1])
    out = jnp.dot(flat, head_matrix().T, precision=lax.Precision.HIGHEST,
                  preferred_element_type=jnp.float32)
    return out.reshape(dims + (HEADS,))


def head_spread(values):
    dims = values.shape[:-1]
    flat = values.reshape(-1, HEADS)
    out = jnp.dot(flat, head_matrix(), precision=lax.Precision.HIGHEST,
                  preferred_element_type=jnp.float32)
    return out.reshape(dims + (HEADS * HEAD_DIM,))


def partner(value, axis, step, count):
    return lax.ppermute(value, axis, [(i, i ^ step) for i in range(count)])


def broadcast_from(value, axis, count, source, held):
    here = lax.axis_index(axis)
    step = 1
    while step < count:
        got = partner(value, axis, step, count)
        if step == 1:
            got, held = lax.optimization_barrier((got, held))
        value = jnp.where(here // step == source // step, value, got)
        step *= 2
    return value, held


def merge(lo, hi):
    top = jnp.maximum(lo[1][:, HEADS:], hi[1][:, HEADS:])
    fade_lo = jnp.exp(lo[1][:, HEADS:] - top)
    fade_hi = jnp.exp(hi[1][:, HEADS:] - top)
    total = lo[1][:, :HEADS] * fade_lo + hi[1][:, :HEADS] * fade_hi
    mixed = lo[0] * head_spread(fade_lo) + hi[0] * head_spread(fade_hi)
    return mixed, jnp.concatenate([total, top], axis=-1)


def pick(flag, a, b):
    return tuple(jnp.where(flag, x, y) for x, y in zip(a, b))


def pack_partial(value):
    stats = value[1]
    high = lax.optimization_barrier(stats.astype(jnp.bfloat16))
    rest = stats - high.astype(jnp.float32)
    middle = lax.optimization_barrier(rest.astype(jnp.bfloat16))
    low = (rest - middle.astype(jnp.float32)).astype(jnp.bfloat16)
    packed = jnp.concatenate([value[0].astype(jnp.bfloat16), high, middle, low], axis=-1)
    return lax.optimization_barrier(packed)


def unpack_partial(packed, width):
    part = packed.astype(jnp.float32)
    n = (packed.shape[1] - width) // 3
    stats = (part[:, width : width + n] + part[:, width + n : width + 2 * n]) + part[:, width + 2 * n :]
    return part[:, :width], stats


def half_merge(value, axis, count, rider):
    here = lax.axis_index(axis)
    half = value[0].shape[0] // 2
    first = (here & 1) == 0
    top_half = tuple(v[:half] for v in value)
    low_half = tuple(v[half:] for v in value)
    mine = pick(first, top_half, low_half)
    sent = pick(first, low_half, top_half)
    got = tuple(partner(v, axis, 1, count) for v in sent)
    value = merge(pick(first, mine, got), pick(first, got, mine))
    step = 2
    while step < count:
        packed = pack_partial(value)
        got = partner(packed, axis, step, count)
        if step * 2 >= count:
            got, rider = lax.optimization_barrier((got, rider))
        got = unpack_partial(got, value[0].shape[1])
        mine = unpack_partial(packed, value[0].shape[1])
        low_side = (here & step) == 0
        value = merge(pick(low_side, mine, got), pick(low_side, got, mine))
        step *= 2
    return value, rider


def join_halves(value, axis, count):
    first = (lax.axis_index(axis) & 1) == 0
    got = partner(value, axis, 1, count)
    return jnp.where(first, jnp.concatenate([value, got]), jnp.concatenate([got, value]))


def fan_out(value, axis, count):
    here = lax.axis_index(axis)
    got = []
    for step in range(1, count):
        if count & (count - 1) == 0:
            pairs = [(i, i ^ step) for i in range(count)]
            source = here ^ step
        else:
            pairs = [(i, (i + step) % count) for i in range(count)]
            source = (here - step) % count
        got.append((source, lax.ppermute(value, axis, pairs)))
    return got


def row_kernel(q_ref, k_ref, v_ref, sk_ref, sv_ref, allow_ref, o_ref, *, scale):
    rows = q_ref.shape[1]
    lane = lax.broadcasted_iota(jnp.int32, (1, 2 * HEAD_DIM), 1)
    low = lane < HEAD_DIM
    nt = (((1,), (1,)), ((), ()))
    for row, pair in [(row, pair) for row in range(q_ref.shape[0]) for pair in range(HEADS // 2)]:
        allow = allow_ref[row] > 0.5
        allow = jnp.concatenate([allow, allow], axis=0)
        cols = slice(pair * 2 * HEAD_DIM, (pair + 1) * 2 * HEAD_DIM)
        q = q_ref[row, :, cols] * scale
        zero = jnp.zeros_like(q)
        qh = jnp.concatenate([jnp.where(low, q, zero), jnp.where(low, zero, q)], axis=0)
        k = k_ref[row, :, cols]
        v = v_ref[row, :, cols]
        sk = sk_ref[:, cols]
        sv = sv_ref[:, cols]
        s = lax.dot_general(qh, k, nt, preferred_element_type=jnp.float32)
        s = jnp.where(allow, s, -1e30)
        ts = lax.dot_general(qh, sk, nt, preferred_element_type=jnp.float32)
        top = jnp.maximum(s.max(-1, keepdims=True), ts.max(-1, keepdims=True))
        e = jnp.exp(s - top)
        te = jnp.exp(ts - top)
        tot = e.sum(-1, keepdims=True) + te.sum(-1, keepdims=True)
        acc = jnp.dot(e.astype(jnp.bfloat16), v, preferred_element_type=jnp.float32)
        acc = acc + jnp.dot(te.astype(jnp.bfloat16), sv, preferred_element_type=jnp.float32)
        out = jnp.where(low, acc[:rows] / tot[:rows], acc[rows:] / tot[rows:])
        o_ref[row, :, cols] = out.astype(o_ref.dtype)


def row_attention(qkv, kv, summary_kv, allow):
    rows, nq, triple = qkv.shape
    width = triple // 3
    nk = kv.shape[1]
    ns = summary_kv.shape[0]
    kern = functools.partial(row_kernel, scale=HEAD_DIM ** (-0.5))
    return pl.pallas_call(
        kern,
        grid=(rows // 2,),
        in_specs=[
            pl.BlockSpec((2, nq, width), lambda r: (r, 0, 0)),
            pl.BlockSpec((2, nk, width), lambda r: (r, 0, 0)),
            pl.BlockSpec((2, nk, width), lambda r: (r, 0, 1)),
            pl.BlockSpec((ns, width), lambda r: (0, 0)),
            pl.BlockSpec((ns, width), lambda r: (0, 1)),
            pl.BlockSpec((2, nq, nk), lambda r: (r, 0, 0)),
        ],
        out_specs=pl.BlockSpec((2, nq, width), lambda r: (r, 0, 0)),
        out_shape=jax.ShapeDtypeStruct((rows, nq, width), jnp.bfloat16),
    )(qkv, kv, kv, summary_kv, summary_kv, allow)


def local(cells, summary, owner, schema, w_qkv, w_out, gain_attn, w_up, w_down, gain_ffn, *, n_band, n_col):
    row_count, cols_dev, model_width = cells.shape
    own_group = lax.axis_index("col")
    own_band = lax.axis_index("band")
    score_scale = HEAD_DIM ** (-0.5)
    flat_cells = cells.reshape(row_count * cols_dev, model_width)
    w_kv = w_qkv[:, model_width:]

    key_sources = [own_group] + [own_group ^ step for step in range(1, n_col)]
    key_groups = jnp.concatenate(
        [jnp.full((cols_dev,), s, jnp.int32) for s in key_sources]
    )
    own_block = jnp.arange(n_col * cols_dev, dtype=jnp.int32) < cols_dev
    allowed = (jnp.right_shift(schema[:, :, None], key_groups[None, None, :]) & 1 == 1) | own_block[
        None, None, :
    ]
    allowed = allowed.astype(jnp.float32)
    tokens = broadcast_from(summary[0], "band", n_band, owner[0], (cells, allowed))
    held_cells, allowed = tokens[1]
    row_parts = fan_out(held_cells, "col", n_col)
    tokens = tokens[0]

    qkv_cells = project(flat_cells, w_qkv).reshape(row_count, cols_dev, 3 * model_width)
    queries = qkv_cells[:, :, :model_width]
    own_keys = qkv_cells[:, :, model_width : 2 * model_width]
    own_vals = qkv_cells[:, :, 2 * model_width :]

    sum_queries = project(tokens, w_qkv[:, :model_width])
    summary_kv = project(tokens, w_kv)
    sum_keys = summary_kv[:, :model_width]
    sum_vals = summary_kv[:, model_width:]

    sq = sum_queries.astype(jnp.float32)
    col_scores = head_sum(sq[None] * own_keys.astype(jnp.float32)) * score_scale
    self_scores = head_sum(sq * sum_keys.astype(jnp.float32)) * score_scale
    part_top = col_scores.max(0)
    col_exp = jnp.exp(col_scores - part_top[None])
    col_weights = head_spread(lax.optimization_barrier(col_exp.astype(jnp.bfloat16)).astype(jnp.float32))
    part_mixed = (col_weights * own_vals.astype(jnp.float32)).sum(0)
    part_total = col_exp.sum(0)
    row_cells = jnp.concatenate([cells] + [got for _, got in row_parts], axis=1)
    width_now = row_cells.shape[1]
    row_kv = project(row_cells.reshape(row_count * width_now, model_width), w_kv)
    row_kv = row_kv.reshape(row_count, width_now, 2 * model_width)
    merged, row_kv = half_merge(
        (part_mixed, jnp.concatenate([part_total, part_top], axis=-1)), "band", n_band, row_kv
    )
    half = cols_dev // 2
    first = (own_band & 1) == 0
    half_self = jnp.where(first, self_scores[:half], self_scores[half:])
    half_vals = jnp.where(first, sum_vals[:half], sum_vals[half:]).astype(jnp.float32)
    col_top = jnp.maximum(merged[1][:, HEADS:], half_self)
    fade = jnp.exp(merged[1][:, HEADS:] - col_top)
    self_exp = jnp.exp(half_self - col_top)
    col_total = merged[1][:, :HEADS] * fade + self_exp
    col_mixed = merged[0] * head_spread(fade) + head_spread(
        lax.optimization_barrier(self_exp.astype(jnp.bfloat16)).astype(jnp.float32)
    ) * half_vals
    summary_att = (col_mixed / head_spread(col_total)).astype(jnp.bfloat16)
    summary_att = join_halves(summary_att, "band", n_band)

    sources = [own_group] + [s for s, _ in row_parts]
    attended = row_attention(qkv_cells, row_kv, summary_kv, allowed)
    attended = attended.reshape(row_count * cols_dev, model_width)

    all_in = jnp.concatenate([flat_cells, tokens], axis=0)
    all_att = jnp.concatenate([attended, summary_att], axis=0)
    all_out = finish(all_in, all_att, w_out, gain_attn, w_up, w_down, gain_ffn)
    cells_out = all_out[: row_count * cols_dev].reshape(row_count, cols_dev, model_width)
    summary_out = all_out[row_count * cols_dev :]
    return (cells_out, summary_out)


def solution(mesh):
    in_specs = (
        P("band", "col", None),
        P("band", "col", None),
        P("col"),
        P("band", "col"),
        P(),
        P(),
        P(),
        P(),
        P(),
        P(),
    )
    out_specs = (P("band", "col", None), P("col", None))
    body = functools.partial(local, n_band=mesh.shape["band"], n_col=mesh.shape["col"])
    return jax.shard_map(body, mesh=mesh, in_specs=in_specs, out_specs=out_specs, check_vma=False)
```

```python
import functools

import jax
import jax.numpy as jnp
from jax import lax
from jax.experimental import pallas as pl
from jax.sharding import PartitionSpec as P

HEADS = 12
HEAD_DIM = 64


def spread_2(value, axis, source):
    kept = jnp.where(lax.axis_index(axis) == source, value, 0).astype(value.dtype)
    return lax.psum(kept, axis)


def layer_norm(values, gain_vec):
    center = values - jnp.mean(values, -1, keepdims=True)
    spread = jnp.mean(center * center, -1, keepdims=True)
    return center * lax.rsqrt(spread + 1e-05) * gain_vec


def finish(tokens_in, attended, w_out, gain_attn, w_up, w_down, gain_ffn):
    mixed_out = jnp.dot(attended, w_out, preferred_element_type=jnp.float32)
    hidden = layer_norm(tokens_in.astype(jnp.float32) + mixed_out, gain_attn).astype(jnp.bfloat16)
    inner_act = jax.nn.gelu(jnp.dot(hidden, w_up, preferred_element_type=jnp.float32)).astype(
        jnp.bfloat16
    )
    outer_out = jnp.dot(inner_act, w_down, preferred_element_type=jnp.float32)
    return layer_norm(hidden.astype(jnp.float32) + outer_out, gain_ffn).astype(jnp.bfloat16)


def project(values, weight):
    return jnp.dot(values, weight, preferred_element_type=jnp.float32).astype(jnp.bfloat16)


def head_matrix():
    lanes = jnp.arange(HEADS * HEAD_DIM, dtype=jnp.int32) // HEAD_DIM
    return (lanes[None, :] == jnp.arange(HEADS, dtype=jnp.int32)[:, None]).astype(jnp.float32)


def head_sum(values):
    dims = values.shape[:-1]
    flat = values.reshape(-1, values.shape[-1])
    out = jnp.dot(flat, head_matrix().T, precision=lax.Precision.HIGHEST,
                  preferred_element_type=jnp.float32)
    return out.reshape(dims + (HEADS,))


def head_spread(values):
    dims = values.shape[:-1]
    flat = values.reshape(-1, HEADS)
    out = jnp.dot(flat, head_matrix(), precision=lax.Precision.HIGHEST,
                  preferred_element_type=jnp.float32)
    return out.reshape(dims + (HEADS * HEAD_DIM,))


def partner(value, axis, step, count):
    return lax.ppermute(value, axis, [(i, i ^ step) for i in range(count)])


def broadcast_from(value, axis, count, source, held):
    here = lax.axis_index(axis)
    step = 1
    while step < count:
        got = partner(value, axis, step, count)
        if step == 1:
            got, held = lax.optimization_barrier((got, held))
        value = jnp.where(here // step == source // step, value, got)
        step *= 2
    return value, held


def merge(lo, hi):
    top = jnp.maximum(lo[1][:, HEADS:], hi[1][:, HEADS:])
    fade_lo = jnp.exp(lo[1][:, HEADS:] - top)
    fade_hi = jnp.exp(hi[1][:, HEADS:] - top)
    total = lo[1][:, :HEADS] * fade_lo + hi[1][:, :HEADS] * fade_hi
    mixed = lo[0] * head_spread(fade_lo) + hi[0] * head_spread(fade_hi)
    return mixed, jnp.concatenate([total, top], axis=-1)


def pick(flag, a, b):
    return tuple(jnp.where(flag, x, y) for x, y in zip(a, b))


def pack_partial(value):
    stats = value[1]
    high = lax.optimization_barrier(stats.astype(jnp.bfloat16))
    rest = stats - high.astype(jnp.float32)
    middle = lax.optimization_barrier(rest.astype(jnp.bfloat16))
    low = (rest - middle.astype(jnp.float32)).astype(jnp.bfloat16)
    packed = jnp.concatenate([value[0].astype(jnp.bfloat16), high, middle, low], axis=-1)
    return lax.optimization_barrier(packed)


def unpack_partial(packed, width):
    part = packed.astype(jnp.float32)
    n = (packed.shape[1] - width) // 3
    stats = (part[:, width : width + n] + part[:, width + n : width + 2 * n]) + part[:, width + 2 * n :]
    return part[:, :width], stats


def half_merge(value, axis, count, rider):
    here = lax.axis_index(axis)
    half = value[0].shape[0] // 2
    first = (here & 1) == 0
    top_half = tuple(v[:half] for v in value)
    low_half = tuple(v[half:] for v in value)
    mine = pick(first, top_half, low_half)
    sent = pick(first, low_half, top_half)
    got = tuple(partner(v, axis, 1, count) for v in sent)
    value = merge(pick(first, mine, got), pick(first, got, mine))
    step = 2
    while step < count:
        packed = pack_partial(value)
        got = partner(packed, axis, step, count)
        if step * 2 >= count:
            got, rider = lax.optimization_barrier((got, rider))
        got = unpack_partial(got, value[0].shape[1])
        mine = unpack_partial(packed, value[0].shape[1])
        low_side = (here & step) == 0
        value = merge(pick(low_side, mine, got), pick(low_side, got, mine))
        step *= 2
    return value, rider


def join_halves(value, axis, count):
    first = (lax.axis_index(axis) & 1) == 0
    got = partner(value, axis, 1, count)
    return jnp.where(first, jnp.concatenate([value, got]), jnp.concatenate([got, value]))


def fan_out(value, axis, count):
    here = lax.axis_index(axis)
    got = []
    for step in range(1, count):
        if count & (count - 1) == 0:
            pairs = [(i, i ^ step) for i in range(count)]
            source = here ^ step
        else:
            pairs = [(i, (i + step) % count) for i in range(count)]
            source = (here - step) % count
        got.append((source, lax.ppermute(value, axis, pairs)))
    return got


def row_kernel(q_ref, k_ref, v_ref, sk_ref, sv_ref, allow_ref, o_ref, *, scale):
    rows = q_ref.shape[1]
    allow = allow_ref[0] > 0.5
    allow = jnp.concatenate([allow, allow], axis=0)
    lane = lax.broadcasted_iota(jnp.int32, (1, 2 * HEAD_DIM), 1)
    low = lane < HEAD_DIM
    nt = (((1,), (1,)), ((), ()))
    for pair in range(HEADS // 2):
        cols = slice(pair * 2 * HEAD_DIM, (pair + 1) * 2 * HEAD_DIM)
        q = q_ref[0, :, cols] * scale
        zero = jnp.zeros_like(q)
        qh = jnp.concatenate([jnp.where(low, q, zero), jnp.where(low, zero, q)], axis=0)
        k = k_ref[0, :, cols]
        v = v_ref[0, :, cols]
        sk = sk_ref[:, cols]
        sv = sv_ref[:, cols]
        s = lax.dot_general(qh, k, nt, preferred_element_type=jnp.float32)
        s = jnp.where(allow, s, -1e30)
        ts = lax.dot_general(qh, sk, nt, preferred_element_type=jnp.float32)
        top = jnp.maximum(s.max(-1, keepdims=True), ts.max(-1, keepdims=True))
        e = jnp.exp(s - top)
        te = jnp.exp(ts - top)
        tot = e.sum(-1, keepdims=True) + te.sum(-1, keepdims=True)
        acc = jnp.dot(e.astype(jnp.bfloat16), v, preferred_element_type=jnp.float32)
        acc = acc + jnp.dot(te.astype(jnp.bfloat16), sv, preferred_element_type=jnp.float32)
        out = jnp.where(low, acc[:rows] / tot[:rows], acc[rows:] / tot[rows:])
        o_ref[0, :, cols] = out.astype(o_ref.dtype)


def row_attention(qkv, kv, summary_kv, allow):
    rows, nq, triple = qkv.shape
    width = triple // 3
    nk = kv.shape[1]
    ns = summary_kv.shape[0]
    kern = functools.partial(row_kernel, scale=HEAD_DIM ** (-0.5))
    return pl.pallas_call(
        kern,
        grid=(rows,),
        in_specs=[
            pl.BlockSpec((1, nq, width), lambda r: (r, 0, 0)),
            pl.BlockSpec((1, nk, width), lambda r: (r, 0, 0)),
            pl.BlockSpec((1, nk, width), lambda r: (r, 0, 1)),
            pl.BlockSpec((ns, width), lambda r: (0, 0)),
            pl.BlockSpec((ns, width), lambda r: (0, 1)),
            pl.BlockSpec((1, nq, nk), lambda r: (r, 0, 0)),
        ],
        out_specs=pl.BlockSpec((1, nq, width), lambda r: (r, 0, 0)),
        out_shape=jax.ShapeDtypeStruct((rows, nq, width), jnp.bfloat16),
    )(qkv, kv, kv, summary_kv, summary_kv, allow)


def local(cells, summary, owner, schema, w_qkv, w_out, gain_attn, w_up, w_down, gain_ffn, *, n_band, n_col):
    row_count, cols_dev, model_width = cells.shape
    own_group = lax.axis_index("col")
    own_band = lax.axis_index("band")
    score_scale = HEAD_DIM ** (-0.5)
    flat_cells = cells.reshape(row_count * cols_dev, model_width)
    w_kv = w_qkv[:, model_width:]

    key_sources = [own_group] + [own_group ^ step for step in range(1, n_col)]
    key_groups = jnp.concatenate(
        [jnp.full((cols_dev,), s, jnp.int32) for s in key_sources]
    )
    own_block = jnp.arange(n_col * cols_dev, dtype=jnp.int32) < cols_dev
    allowed = (jnp.right_shift(schema[:, :, None], key_groups[None, None, :]) & 1 == 1) | own_block[
        None, None, :
    ]
    allowed = allowed.astype(jnp.float32)
    tokens = broadcast_from(summary[0], "band", n_band, owner[0], (cells, allowed))
    held_cells, allowed = tokens[1]
    row_parts = fan_out(held_cells, "col", n_col)
    tokens = tokens[0]

    qkv_cells = project(flat_cells, w_qkv).reshape(row_count, cols_dev, 3 * model_width)
    queries = qkv_cells[:, :, :model_width]
    own_keys = qkv_cells[:, :, model_width : 2 * model_width]
    own_vals = qkv_cells[:, :, 2 * model_width :]

    sum_queries = project(tokens, w_qkv[:, :model_width])
    summary_kv = project(tokens, w_kv)
    sum_keys = summary_kv[:, :model_width]
    sum_vals = summary_kv[:, model_width:]

    sq = sum_queries.astype(jnp.float32)
    col_scores = head_sum(sq[None] * own_keys.astype(jnp.float32)) * score_scale
    self_scores = head_sum(sq * sum_keys.astype(jnp.float32)) * score_scale
    part_top = col_scores.max(0)
    col_exp = jnp.exp(col_scores - part_top[None])
    col_weights = head_spread(lax.optimization_barrier(col_exp.astype(jnp.bfloat16)).astype(jnp.float32))
    part_mixed = (col_weights * own_vals.astype(jnp.float32)).sum(0)
    part_total = col_exp.sum(0)
    row_cells = jnp.concatenate([cells] + [got for _, got in row_parts], axis=1)
    width_now = row_cells.shape[1]
    row_kv = project(row_cells.reshape(row_count * width_now, model_width), w_kv)
    row_kv = row_kv.reshape(row_count, width_now, 2 * model_width)
    merged, row_kv = half_merge(
        (part_mixed, jnp.concatenate([part_total, part_top], axis=-1)), "band", n_band, row_kv
    )
    half = cols_dev // 2
    first = (own_band & 1) == 0
    half_self = jnp.where(first, self_scores[:half], self_scores[half:])
    half_vals = jnp.where(first, sum_vals[:half], sum_vals[half:]).astype(jnp.float32)
    col_top = jnp.maximum(merged[1][:, HEADS:], half_self)
    fade = jnp.exp(merged[1][:, HEADS:] - col_top)
    self_exp = jnp.exp(half_self - col_top)
    col_total = merged[1][:, :HEADS] * fade + self_exp
    col_mixed = merged[0] * head_spread(fade) + head_spread(
        lax.optimization_barrier(self_exp.astype(jnp.bfloat16)).astype(jnp.float32)
    ) * half_vals
    summary_att = (col_mixed / head_spread(col_total)).astype(jnp.bfloat16)

    sources = [own_group] + [s for s, _ in row_parts]
    attended = row_attention(qkv_cells, row_kv, summary_kv, allowed)
    attended = attended.reshape(row_count * cols_dev, model_width)

    half_tokens = jnp.where(first, tokens[:half], tokens[half:])
    all_in = jnp.concatenate([flat_cells, half_tokens], axis=0)
    all_att = jnp.concatenate([attended, summary_att], axis=0)
    all_out = finish(all_in, all_att, w_out, gain_attn, w_up, w_down, gain_ffn)
    cells_out = all_out[: row_count * cols_dev].reshape(row_count, cols_dev, model_width)
    summary_out = join_halves(all_out[row_count * cols_dev :], "band", n_band)
    return (cells_out, summary_out)


def solution(mesh):
    in_specs = (
        P("band", "col", None),
        P("band", "col", None),
        P("col"),
        P("band", "col"),
        P(),
        P(),
        P(),
        P(),
        P(),
        P(),
    )
    out_specs = (P("band", "col", None), P("col", None))
    body = functools.partial(local, n_band=mesh.shape["band"], n_col=mesh.shape["col"])
    return jax.shard_map(body, mesh=mesh, in_specs=in_specs, out_specs=out_specs, check_vma=False)
```

```python
import functools

import jax
import jax.numpy as jnp
from jax import lax
from jax.experimental import pallas as pl
from jax.sharding import PartitionSpec as P

HEADS = 12
HEAD_DIM = 64


def spread_2(value, axis, source):
    kept = jnp.where(lax.axis_index(axis) == source, value, 0).astype(value.dtype)
    return lax.psum(kept, axis)


def layer_norm(values, gain_vec):
    center = values - jnp.mean(values, -1, keepdims=True)
    spread = jnp.mean(center * center, -1, keepdims=True)
    return center * lax.rsqrt(spread + 1e-05) * gain_vec


def finish(tokens_in, attended, w_out, gain_attn, w_up, w_down, gain_ffn):
    mixed_out = jnp.dot(attended, w_out, preferred_element_type=jnp.float32)
    hidden = layer_norm(tokens_in.astype(jnp.float32) + mixed_out, gain_attn).astype(jnp.bfloat16)
    inner_act = jax.nn.gelu(jnp.dot(hidden, w_up, preferred_element_type=jnp.float32)).astype(
        jnp.bfloat16
    )
    outer_out = jnp.dot(inner_act, w_down, preferred_element_type=jnp.float32)
    return layer_norm(hidden.astype(jnp.float32) + outer_out, gain_ffn).astype(jnp.bfloat16)


def project(values, weight):
    return jnp.dot(values, weight, preferred_element_type=jnp.float32).astype(jnp.bfloat16)


def head_matrix():
    lanes = jnp.arange(HEADS * HEAD_DIM, dtype=jnp.int32) // HEAD_DIM
    return (lanes[None, :] == jnp.arange(HEADS, dtype=jnp.int32)[:, None]).astype(jnp.float32)


def head_sum(values):
    dims = values.shape[:-1]
    flat = values.reshape(-1, values.shape[-1])
    out = jnp.dot(flat, head_matrix().T, precision=lax.Precision.HIGHEST,
                  preferred_element_type=jnp.float32)
    return out.reshape(dims + (HEADS,))


def head_spread(values):
    dims = values.shape[:-1]
    flat = values.reshape(-1, HEADS)
    out = jnp.dot(flat, head_matrix(), precision=lax.Precision.HIGHEST,
                  preferred_element_type=jnp.float32)
    return out.reshape(dims + (HEADS * HEAD_DIM,))


def partner(value, axis, step, count):
    return lax.ppermute(value, axis, [(i, i ^ step) for i in range(count)])


def broadcast_from(value, axis, count, source, held):
    here = lax.axis_index(axis)
    step = 1
    while step < count:
        got = partner(value, axis, step, count)
        if step == 1:
            got, held = lax.optimization_barrier((got, held))
        value = jnp.where(here // step == source // step, value, got)
        step *= 2
    return value, held


def merge(lo, hi):
    top = jnp.maximum(lo[1][:, HEADS:], hi[1][:, HEADS:])
    fade_lo = jnp.exp(lo[1][:, HEADS:] - top)
    fade_hi = jnp.exp(hi[1][:, HEADS:] - top)
    total = lo[1][:, :HEADS] * fade_lo + hi[1][:, :HEADS] * fade_hi
    mixed = lo[0] * head_spread(fade_lo) + hi[0] * head_spread(fade_hi)
    return mixed, jnp.concatenate([total, top], axis=-1)


def pick(flag, a, b):
    return tuple(jnp.where(flag, x, y) for x, y in zip(a, b))


def pack_partial(value):
    stats = value[1]
    high = lax.optimization_barrier(stats.astype(jnp.bfloat16))
    rest = stats - high.astype(jnp.float32)
    middle = lax.optimization_barrier(rest.astype(jnp.bfloat16))
    low = (rest - middle.astype(jnp.float32)).astype(jnp.bfloat16)
    packed = jnp.concatenate([value[0].astype(jnp.bfloat16), high, middle, low], axis=-1)
    return lax.optimization_barrier(packed)


def unpack_partial(packed, width):
    part = packed.astype(jnp.float32)
    n = (packed.shape[1] - width) // 3
    stats = (part[:, width : width + n] + part[:, width + n : width + 2 * n]) + part[:, width + 2 * n :]
    return part[:, :width], stats


def half_merge(value, axis, count, rider):
    here = lax.axis_index(axis)
    half = value[0].shape[0] // 2
    first = (here & 1) == 0
    top_half = tuple(v[:half] for v in value)
    low_half = tuple(v[half:] for v in value)
    mine = pick(first, top_half, low_half)
    sent = pick(first, low_half, top_half)
    got = tuple(partner(v, axis, 1, count) for v in sent)
    value = merge(pick(first, mine, got), pick(first, got, mine))
    step = 2
    while step < count:
        packed = pack_partial(value)
        got = partner(packed, axis, step, count)
        if step * 2 >= count:
            got, rider = lax.optimization_barrier((got, rider))
        got = unpack_partial(got, value[0].shape[1])
        mine = unpack_partial(packed, value[0].shape[1])
        low_side = (here & step) == 0
        value = merge(pick(low_side, mine, got), pick(low_side, got, mine))
        step *= 2
    return value, rider


def join_halves(value, axis, count):
    first = (lax.axis_index(axis) & 1) == 0
    got = partner(value, axis, 1, count)
    return jnp.where(first, jnp.concatenate([value, got]), jnp.concatenate([got, value]))


def fan_out(value, axis, count):
    here = lax.axis_index(axis)
    got = []
    for step in range(1, count):
        if count & (count - 1) == 0:
            pairs = [(i, i ^ step) for i in range(count)]
            source = here ^ step
        else:
            pairs = [(i, (i + step) % count) for i in range(count)]
            source = (here - step) % count
        got.append((source, lax.ppermute(value, axis, pairs)))
    return got


def row_kernel(q_ref, k_ref, v_ref, sk_ref, sv_ref, allow_ref, o_ref, *, scale):
    rows = q_ref.shape[1]
    allow = allow_ref[0] > 0.5
    allow = jnp.concatenate([allow, allow], axis=0)
    lane = lax.broadcasted_iota(jnp.int32, (1, 2 * HEAD_DIM), 1)
    low = lane < HEAD_DIM
    nt = (((1,), (1,)), ((), ()))
    for pair in range(HEADS // 2):
        cols = slice(pair * 2 * HEAD_DIM, (pair + 1) * 2 * HEAD_DIM)
        q = q_ref[0, :, cols] * scale
        zero = jnp.zeros_like(q)
        qh = jnp.concatenate([jnp.where(low, q, zero), jnp.where(low, zero, q)], axis=0)
        k = k_ref[0, :, cols]
        v = v_ref[0, :, cols]
        sk = sk_ref[:, cols]
        sv = sv_ref[:, cols]
        s = lax.dot_general(qh, k, nt, preferred_element_type=jnp.float32)
        s = jnp.where(allow, s, -1e30)
        ts = lax.dot_general(qh, sk, nt, preferred_element_type=jnp.float32)
        top = jnp.maximum(s.max(-1, keepdims=True), ts.max(-1, keepdims=True))
        e = jnp.exp(s - top)
        te = jnp.exp(ts - top)
        tot = e.sum(-1, keepdims=True) + te.sum(-1, keepdims=True)
        acc = jnp.dot(e.astype(jnp.bfloat16), v, preferred_element_type=jnp.float32)
        acc = acc + jnp.dot(te.astype(jnp.bfloat16), sv, preferred_element_type=jnp.float32)
        out = jnp.where(low, acc[:rows] / tot[:rows], acc[rows:] / tot[rows:])
        o_ref[0, :, cols] = out.astype(o_ref.dtype)


def row_attention(qkv, kv, summary_kv, allow):
    rows, nq, triple = qkv.shape
    width = triple // 3
    nk = kv.shape[1]
    ns = summary_kv.shape[0]
    kern = functools.partial(row_kernel, scale=HEAD_DIM ** (-0.5))
    return pl.pallas_call(
        kern,
        grid=(rows,),
        in_specs=[
            pl.BlockSpec((1, nq, width), lambda r: (r, 0, 0)),
            pl.BlockSpec((1, nk, width), lambda r: (r, 0, 0)),
            pl.BlockSpec((1, nk, width), lambda r: (r, 0, 1)),
            pl.BlockSpec((ns, width), lambda r: (0, 0)),
            pl.BlockSpec((ns, width), lambda r: (0, 1)),
            pl.BlockSpec((1, nq, nk), lambda r: (r, 0, 0)),
        ],
        out_specs=pl.BlockSpec((1, nq, width), lambda r: (r, 0, 0)),
        out_shape=jax.ShapeDtypeStruct((rows, nq, width), jnp.bfloat16),
    )(qkv, kv, kv, summary_kv, summary_kv, allow)


def local(cells, summary, owner, schema, w_qkv, w_out, gain_attn, w_up, w_down, gain_ffn, *, n_band, n_col):
    row_count, cols_dev, model_width = cells.shape
    own_group = lax.axis_index("col")
    own_band = lax.axis_index("band")
    score_scale = HEAD_DIM ** (-0.5)
    flat_cells = cells.reshape(row_count * cols_dev, model_width)
    w_kv = w_qkv[:, model_width:]

    key_sources = [own_group] + [own_group ^ step for step in range(1, n_col)]
    key_groups = jnp.concatenate(
        [jnp.full((cols_dev,), s, jnp.int32) for s in key_sources]
    )
    own_block = jnp.arange(n_col * cols_dev, dtype=jnp.int32) < cols_dev
    allowed = (jnp.right_shift(schema[:, :, None], key_groups[None, None, :]) & 1 == 1) | own_block[
        None, None, :
    ]
    allowed = allowed.astype(jnp.bfloat16)
    tokens = broadcast_from(summary[0], "band", n_band, owner[0], (cells, allowed))
    held_cells, allowed = tokens[1]
    row_parts = fan_out(held_cells, "col", n_col)
    tokens = tokens[0]

    qkv_cells = project(flat_cells, w_qkv).reshape(row_count, cols_dev, 3 * model_width)
    queries = qkv_cells[:, :, :model_width]
    own_keys = qkv_cells[:, :, model_width : 2 * model_width]
    own_vals = qkv_cells[:, :, 2 * model_width :]

    sum_queries = project(tokens, w_qkv[:, :model_width])
    summary_kv = project(tokens, w_kv)
    sum_keys = summary_kv[:, :model_width]
    sum_vals = summary_kv[:, model_width:]

    sq = sum_queries.astype(jnp.float32)
    col_scores = head_sum(sq[None] * own_keys.astype(jnp.float32)) * score_scale
    self_scores = head_sum(sq * sum_keys.astype(jnp.float32)) * score_scale
    part_top = col_scores.max(0)
    col_exp = jnp.exp(col_scores - part_top[None])
    col_weights = head_spread(lax.optimization_barrier(col_exp.astype(jnp.bfloat16)).astype(jnp.float32))
    part_mixed = (col_weights * own_vals.astype(jnp.float32)).sum(0)
    part_total = col_exp.sum(0)
    row_cells = jnp.concatenate([cells] + [got for _, got in row_parts], axis=1)
    width_now = row_cells.shape[1]
    row_kv = project(row_cells.reshape(row_count * width_now, model_width), w_kv)
    row_kv = row_kv.reshape(row_count, width_now, 2 * model_width)
    merged, row_kv = half_merge(
        (part_mixed, jnp.concatenate([part_total, part_top], axis=-1)), "band", n_band, row_kv
    )
    half = cols_dev // 2
    first = (own_band & 1) == 0
    half_self = jnp.where(first, self_scores[:half], self_scores[half:])
    half_vals = jnp.where(first, sum_vals[:half], sum_vals[half:]).astype(jnp.float32)
    col_top = jnp.maximum(merged[1][:, HEADS:], half_self)
    fade = jnp.exp(merged[1][:, HEADS:] - col_top)
    self_exp = jnp.exp(half_self - col_top)
    col_total = merged[1][:, :HEADS] * fade + self_exp
    col_mixed = merged[0] * head_spread(fade) + head_spread(
        lax.optimization_barrier(self_exp.astype(jnp.bfloat16)).astype(jnp.float32)
    ) * half_vals
    summary_att = (col_mixed / head_spread(col_total)).astype(jnp.bfloat16)

    sources = [own_group] + [s for s, _ in row_parts]
    attended = row_attention(qkv_cells, row_kv, summary_kv, allowed)
    attended = attended.reshape(row_count * cols_dev, model_width)

    half_tokens = jnp.where(first, tokens[:half], tokens[half:])
    all_in = jnp.concatenate([flat_cells, half_tokens], axis=0)
    all_att = jnp.concatenate([attended, summary_att], axis=0)
    all_out = finish(all_in, all_att, w_out, gain_attn, w_up, w_down, gain_ffn)
    cells_out = all_out[: row_count * cols_dev].reshape(row_count, cols_dev, model_width)
    summary_out = join_halves(all_out[row_count * cols_dev :], "band", n_band)
    return (cells_out, summary_out)


def solution(mesh):
    in_specs = (
        P("band", "col", None),
        P("band", "col", None),
        P("col"),
        P("band", "col"),
        P(),
        P(),
        P(),
        P(),
        P(),
        P(),
    )
    out_specs = (P("band", "col", None), P("col", None))
    body = functools.partial(local, n_band=mesh.shape["band"], n_col=mesh.shape["col"])
    return jax.shard_map(body, mesh=mesh, in_specs=in_specs, out_specs=out_specs, check_vma=False)
```
